128 devices in a mesh: vessel: 8 (over x, core), blk: 16 (over z, y).
Axes of the slice: x: 4, y: 4, z: 4, core: 2. Of those that a mesh axis runs over, the one named last changes fastest.
Arguments:
- populations: float32 [19, 64, 512, 128], P(None, 'vessel', 'blk'), may hold values from 0.5 to 1.5
- voxel_mask: int32 [64, 512, 128], P('vessel', 'blk'), may hold values from 0 to 2
- tracer: float32 [64, 32, 256], P('blk', 'vessel'), may hold values from -6 to 6
Outputs:
- final_populations: float32 [19, 64, 512, 128], P(None, 'vessel', 'blk')
- final_tracer: float32 [64, 32, 256], P('blk', 'vessel')
The draws below stay inside these ranges and needn't reach their ends.
All inputs are finite; a program needn't handle non-finite values.
Results may differ from the reference program's by a relative error of at most 0.0001.
Values sent between devices are 32-bit elements; how exact they have to be, the bound alone decides.
No kernel may reach another device: no remote copies, remote signals or barrier semaphores. Data moves between devices by JAX's collectives and lax.ppermute only.
A program may use at most 128 MiB of HBM per device.

```python
import jax
import jax.numpy as jnp
import numpy as np
from jax import lax

NZ = 128
STEPS = 4
TRACER_STEPS = 2
NX = 64
NY = 512
MX = 32
MY = 256
MZ = 64


def plant(result, stream_key, smallest, largest):
    longest = result.shape.index(max(result.shape))
    spots = []
    for shift in (0, 1):
        where = [jax.random.randint(jax.random.fold_in(stream_key, axis), (), 0, length) for axis, length in enumerate(result.shape)]
        where[longest] = (where[longest] + shift) % result.shape[longest]
        spots.append(tuple(where))
    return result.at[spots[0]].set(smallest).at[spots[1]].set(largest)


def block_levels(key, dims, pieces, low, top_value):
    def one(dim, blocks):
        draws = jax.random.uniform(jax.random.fold_in(jax.random.fold_in(key, 6), dim), (blocks,), jnp.float32, low / len(pieces), top_value / len(pieces))
        return jnp.repeat(jnp.exp(draws), dims[dim] // blocks).reshape((-1,) + (1,) * (len(dims) - dim - 1))

    level = one(*pieces[0])
    for cut in pieces[1:]:
        level = level * one(*cut)
    return level


def gaussian(own_key, shape, spread, limit, pieces=(), dtype=jnp.bfloat16):
    result = spread * jax.random.normal(own_key, shape, jnp.float32)
    if pieces:
        result = result * block_levels(own_key, shape, pieces, -0.22, 0.18)
    return jnp.clip(result, -limit, limit).astype(dtype)


def setup_inputs(seed: int = 0) -> dict:
    keys = jax.random.split(jax.random.key(seed), 4)
    populations = jnp.clip(0.5 + 1.0 * jax.random.uniform(keys[0], (19, NX, NY, NZ), jnp.float32) ** block_levels(keys[0], (19, NX, NY, NZ), ((1, 8), (2, 16)), -0.2, 0.2), 0.5, 1.5)
    voxel_mask = plant(jax.random.randint(keys[1], (NX, NY, NZ), 0, 3), jax.random.fold_in(keys[1], 1), 0, 2).astype(jnp.int32)
    tracer = gaussian(keys[2], (MZ, MX, MY), 1.0, 6.0, ((0, 16), (1, 8)), jnp.float32)
    return dict(populations=populations, voxel_mask=voxel_mask, tracer=tracer)


VELOCITY = np.array([[0, 0, 0], [1, 0, 0], [-1, 0, 0], [0, 1, 0], [0, -1, 0], [0, 0, 1], [0, 0, -1], [1, 1, 0], [-1, -1, 0], [1, -1, 0], [-1, 1, 0], [1, 0, 1], [-1, 0, -1], [1, 0, -1], [-1, 0, 1], [0, 1, 1], [0, -1, -1], [0, 1, -1], [0, -1, 1]])
WEIGHTS = np.array([1.0 / 3.0] + [1.0 / 18.0] * 6 + [1.0 / 36.0] * 12)
OPPOSITE = [0, 2, 1, 4, 3, 6, 5, 8, 7, 10, 9, 12, 11, 14, 13, 16, 15, 18, 17]
relax_rate = 1.25
pore_damping = 0.5
advect_gain = 8.0
diffusion = 0.1


def moments(popul):
    weight_vec = jnp.asarray(WEIGHTS, jnp.float32)
    weight_vel = jnp.asarray(WEIGHTS[:, None] * VELOCITY, jnp.float32)
    density = jnp.einsum("i,ixyz->xyz", weight_vec, popul, precision=lax.Precision.HIGHEST)
    momentum = jnp.einsum("id,ixyz->dxyz", weight_vel, popul, precision=lax.Precision.HIGHEST)
    return density, momentum


def collide(popul, mask):
    density, momentum = moments(popul)
    velocity = momentum / density
    damped = jnp.where(mask == 1, pore_damping * velocity, velocity)
    projected = jnp.einsum("id,dxyz->ixyz", jnp.asarray(VELOCITY, jnp.float32), damped, precision=lax.Precision.HIGHEST)
    speed_sq = jnp.sum(damped * damped, axis=0)
    balance = density * (1.0 + 3.0 * projected + 4.5 * projected * projected - 1.5 * speed_sq)
    relaxed = popul + relax_rate * (balance - popul)
    bounced = jnp.stack([popul[j] for j in OPPOSITE])
    return jnp.where(mask == 2, bounced, relaxed)


def flow_velocity(popul, mask):
    density, momentum = moments(popul)
    return jnp.where(mask == 2, jnp.float32(0.0), momentum / density)


def coarsen(field):
    comps, first, second, third = field.shape
    shaped = field.reshape(comps, first // 2, 2, second // 2, 2, third // 2, 2)
    return jnp.mean(shaped, axis=(2, 4, 6))


def tracer_step(conc, flow):
    flux_x = flow[0] * conc
    flux_y = flow[1] * conc
    flux_z = flow[2] * conc
    div_x = (jnp.roll(flux_x, -1, 1) - jnp.roll(flux_x, 1, 1)) * 0.5
    div_y = (jnp.roll(flux_y, -1, 2) - jnp.roll(flux_y, 1, 2)) * 0.5
    div_z = (jnp.roll(flux_z, -1, 0) - jnp.roll(flux_z, 1, 0)) * 0.5
    divergence = div_x + div_y + div_z
    beside_all = (jnp.roll(conc, -1, 1) + jnp.roll(conc, 1, 1)) + (jnp.roll(conc, -1, 2) + jnp.roll(conc, 1, 2)) + (jnp.roll(conc, -1, 0) + jnp.roll(conc, 1, 0))
    laplace = beside_all - 6.0 * conc
    return conc - advect_gain * divergence + diffusion * laplace


def reference(populations, voxel_mask, tracer):
    state = populations
    for step in range(STEPS):
        post = collide(state, voxel_mask)
        state = jnp.stack([jnp.roll(post[i], (int(VELOCITY[i, 0]), int(VELOCITY[i, 1]), int(VELOCITY[i, 2])), axis=(0, 1, 2)) for i in range(19)])
    flow = flow_velocity(state, voxel_mask)
    coarse = jnp.transpose(coarsen(flow), (0, 3, 1, 2))
    conc = tracer
    for step in range(TRACER_STEPS):
        conc = tracer_step(conc, coarse)
    return state, conc
```

```python
import functools

import jax
import jax.numpy as jnp
import numpy as np
from jax import lax
from jax.experimental import pallas as pl
from jax.experimental.pallas import tpu as pltpu
from jax.sharding import PartitionSpec as P

STEPS = 4
TRACER_STEPS = 2


VELOCITY = np.array(
    [
        [0, 0, 0],
        [1, 0, 0],
        [-1, 0, 0],
        [0, 1, 0],
        [0, -1, 0],
        [0, 0, 1],
        [0, 0, -1],
        [1, 1, 0],
        [-1, -1, 0],
        [1, -1, 0],
        [-1, 1, 0],
        [1, 0, 1],
        [-1, 0, -1],
        [1, 0, -1],
        [-1, 0, 1],
        [0, 1, 1],
        [0, -1, -1],
        [0, 1, -1],
        [0, -1, 1],
    ]
)
WEIGHTS = np.array([1.0 / 3.0] + [1.0 / 18.0] * 6 + [1.0 / 36.0] * 12)
OPPOSITE = [0, 2, 1, 4, 3, 6, 5, 8, 7, 10, 9, 12, 11, 14, 13, 16, 15, 18, 17]
relax_rate = 1.25
pore_damping = 0.5
advect_gain = 8.0
diffusion = 0.1

NPOP = 19
CX = [int(v) for v in VELOCITY[:, 0]]
CY = [int(v) for v in VELOCITY[:, 1]]
CZ = [int(v) for v in VELOCITY[:, 2]]
CXP = [i for i in range(NPOP) if CX[i] == 1]
CXM = [i for i in range(NPOP) if CX[i] == -1]
CYP = [i for i in range(NPOP) if CY[i] == 1]
CYM = [i for i in range(NPOP) if CY[i] == -1]
SHIFTED = [i for i in range(NPOP) if CX[i] != 0 or CY[i] != 0]
ROWS = 8
YOFF = 8


def moments_chunk(g):
    w0 = jnp.float32(WEIGHTS[0])
    w1 = jnp.float32(WEIGHTS[1])
    w2 = jnp.float32(WEIGHTS[7])
    s1 = ((g[1] + g[2]) + (g[3] + g[4])) + (g[5] + g[6])
    s2 = (((g[7] + g[8]) + (g[9] + g[10])) + ((g[11] + g[12]) + (g[13] + g[14]))) + (
        (g[15] + g[16]) + (g[17] + g[18])
    )
    density = w0 * g[0] + w1 * s1 + w2 * s2
    mx = w1 * (g[1] - g[2]) + w2 * (((g[7] - g[8]) + (g[9] - g[10])) + ((g[11] - g[12]) + (g[13] - g[14])))
    my = w1 * (g[3] - g[4]) + w2 * (((g[7] - g[8]) + (g[10] - g[9])) + ((g[15] - g[16]) + (g[17] - g[18])))
    mz = w1 * (g[5] - g[6]) + w2 * (((g[11] - g[12]) + (g[14] - g[13])) + ((g[15] - g[16]) + (g[18] - g[17])))
    return density, (mx, my, mz)


def collide_chunk(g, mask):
    density, (mx, my, mz) = moments_chunk(g)
    ux = mx / density
    uy = my / density
    uz = mz / density
    porous = mask == 1
    ux = jnp.where(porous, pore_damping * ux, ux)
    uy = jnp.where(porous, pore_damping * uy, uy)
    uz = jnp.where(porous, pore_damping * uz, uz)
    speed_sq = ux * ux + uy * uy + uz * uz
    solid = mask == 2
    comps = (ux, uy, uz)
    out = [None] * NPOP
    for i in range(NPOP):
        proj = None
        for d in range(3):
            c = int(VELOCITY[i, d])
            if c == 0:
                continue
            term = comps[d] if c > 0 else -comps[d]
            proj = term if proj is None else proj + term
        if proj is None:
            balance = density * (1.0 - 1.5 * speed_sq)
        else:
            balance = density * (1.0 + 3.0 * proj + 4.5 * proj * proj - 1.5 * speed_sq)
        relaxed = g[i] + relax_rate * (balance - g[i])
        out[i] = jnp.where(solid, g[OPPOSITE[i]], relaxed)
    return out


def lb_kernel(mode, nx, ny, *refs):
    if mode == "first":
        src_ref, mask_ref = refs[:2]
        rest = refs[2:]
    else:
        src_ref, mask_ref, xlo, xhi, ylo, yhi, k7, k8, k9, k10 = refs[:10]
        rest = refs[10:]
    if mode == "last":
        out_ref, coarse_ref, ext, flow_s = rest
    else:
        out_ref, fxh, fxl, fyh, fyl, o7, o8, o9, o10 = rest[:9]
        ext = rest[9] if mode == "mid" else None

    if mode != "first":
        for i in SHIFTED:
            ext[i, 1 : nx + 1, YOFF : YOFF + ny, :] = src_ref[i]
        for k, i in enumerate(CXP):
            ext[i, 0, YOFF : YOFF + ny, :] = xlo[k]
        for k, i in enumerate(CXM):
            ext[i, nx + 1, YOFF : YOFF + ny, :] = xhi[k]
        for k, i in enumerate(CYP):
            for x in range(nx):
                ext[i, x + 1, YOFF - 1 : YOFF, :] = ylo[k, x : x + 1, :]
        for k, i in enumerate(CYM):
            for x in range(nx):
                ext[i, x + 1, YOFF + ny : YOFF + ny + 1, :] = yhi[k, x : x + 1, :]
        ext[7, 0, YOFF - 1 : YOFF, :] = k7[...]
        ext[8, nx + 1, YOFF + ny : YOFF + ny + 1, :] = k8[...]
        ext[9, 0, YOFF + ny : YOFF + ny + 1, :] = k9[...]
        ext[10, nx + 1, YOFF - 1 : YOFF, :] = k10[...]

    def body(x, carry):
        for y0 in range(0, ny, ROWS):
            g = []
            for i in range(NPOP):
                if mode == "first":
                    v = src_ref[i, x, pl.ds(y0, ROWS), :]
                elif i in SHIFTED:
                    v = ext[i, x + 1 - CX[i], pl.ds(YOFF + y0 - CY[i], ROWS), :]
                else:
                    v = src_ref[i, x, pl.ds(y0, ROWS), :]
                if mode != "first" and CZ[i] != 0:
                    v = pltpu.roll(v, CZ[i] % v.shape[1], 1)
                g.append(v)
            mask = mask_ref[x, pl.ds(y0, ROWS), :]
            if mode == "last":
                for i in range(NPOP):
                    out_ref[i, x, pl.ds(y0, ROWS), :] = g[i]
                density, mom = moments_chunk(g)
                solid = mask == 2
                for d in range(3):
                    flow_s[d, x, pl.ds(y0, ROWS), :] = jnp.where(solid, jnp.float32(0.0), mom[d] / density)
            else:
                post = collide_chunk(g, mask)
                for i in range(NPOP):
                    out_ref[i, x, pl.ds(y0, ROWS), :] = post[i]
        return carry

    lax.fori_loop(0, nx, body, 0)

    if mode == "last":
        nz = flow_s.shape[3]
        pz = (
            lax.broadcasted_iota(jnp.int32, (nz // 2, nz), 1) // 2 == lax.broadcasted_iota(jnp.int32, (nz // 2, nz), 0)
        ).astype(jnp.float32)
        py = (
            lax.broadcasted_iota(jnp.int32, (ny, ny // 2), 0) // 2 == lax.broadcasted_iota(jnp.int32, (ny, ny // 2), 1)
        ).astype(jnp.float32)
        for d in range(3):
            for xp in range(nx // 2):
                plane = flow_s[d, 2 * xp] + flow_s[d, 2 * xp + 1]
                zy = lax.dot_general(
                    pz,
                    plane,
                    (((1,), (1,)), ((), ())),
                    precision=lax.Precision.HIGHEST,
                    preferred_element_type=jnp.float32,
                )
                zc = jnp.dot(zy, py, precision=lax.Precision.HIGHEST, preferred_element_type=jnp.float32)
                coarse_ref[d, xp] = zc * jnp.float32(0.125)
    else:
        for k, i in enumerate(CXP):
            fxh[k] = out_ref[i, nx - 1]
        for k, i in enumerate(CXM):
            fxl[k] = out_ref[i, 0]
        for k, i in enumerate(CYP):
            for x in range(nx):
                fyh[k, x : x + 1, :] = out_ref[i, x, ny - 1 : ny, :]
        for k, i in enumerate(CYM):
            for x in range(nx):
                fyl[k, x : x + 1, :] = out_ref[i, x, 0:1, :]
        o7[...] = out_ref[7, nx - 1, ny - 1 : ny, :]
        o8[...] = out_ref[8, 0, 0:1, :]
        o9[...] = out_ref[9, nx - 1, 0:1, :]
        o10[...] = out_ref[10, 0, ny - 1 : ny, :]


def lb_call(mode, src, mask, halos=()):
    _, nx, ny, nz = src.shape
    f32 = jnp.float32
    vmem = pl.BlockSpec(memory_space=pltpu.VMEM)
    n_in = 2 + len(halos)
    scratch = []
    if mode == "last":
        out_shape = (
            jax.ShapeDtypeStruct(src.shape, f32),
            jax.ShapeDtypeStruct((3, nx // 2, nz // 2, ny // 2), f32),
        )
        scratch = [pltpu.VMEM((NPOP, nx + 2, ny + 2 * YOFF, nz), f32), pltpu.VMEM((3, nx, ny, nz), f32)]
    else:
        out_shape = (
            jax.ShapeDtypeStruct(src.shape, f32),
            jax.ShapeDtypeStruct((len(CXP), ny, nz), f32),
            jax.ShapeDtypeStruct((len(CXM), ny, nz), f32),
            jax.ShapeDtypeStruct((len(CYP), nx, nz), f32),
            jax.ShapeDtypeStruct((len(CYM), nx, nz), f32),
        ) + tuple(jax.ShapeDtypeStruct((1, nz), f32) for _ in range(4))
        if mode == "mid":
            scratch = [pltpu.VMEM((NPOP, nx + 2, ny + 2 * YOFF, nz), f32)]
    cells = nx * ny * nz
    cost = pl.CostEstimate(flops=320 * cells, transcendentals=0, bytes_accessed=2 * NPOP * 4 * cells + 4 * cells)
    return pl.pallas_call(
        functools.partial(lb_kernel, mode, nx, ny),
        out_shape=out_shape,
        in_specs=[vmem] * n_in,
        out_specs=tuple(vmem for _ in out_shape),
        scratch_shapes=scratch,
        cost_estimate=cost,
        compiler_params=pltpu.CompilerParams(vmem_limit_bytes=48 * 1024 * 1024),
    )(src, mask, *halos)


def send(x, dv, db):
    nv = lax.axis_size("vessel")
    nb = lax.axis_size("blk")
    if db == 0:
        return lax.ppermute(x, "vessel", [(i, (i + dv) % nv) for i in range(nv)])
    if dv == 0:
        return lax.ppermute(x, "blk", [(i, (i + db) % nb) for i in range(nb)])
    pairs = []
    for v in range(nv):
        for b in range(nb):
            pairs.append((v * nb + b, ((v + dv) % nv) * nb + (b + db) % nb))
    return lax.ppermute(x, ("vessel", "blk"), pairs)


def exchange(faces):
    fxh, fxl, fyh, fyl, o7, o8, o9, o10 = faces
    return (
        send(fxh, 1, 0),
        send(fxl, -1, 0),
        send(fyh, 0, 1),
        send(fyl, 0, -1),
        send(o7, 1, 1),
        send(o8, -1, -1),
        send(o9, 1, -1),
        send(o10, -1, 1),
    )


def tracer_update(c, fx, fy, fz):
    flux_x = fx * c
    flux_y = fy[1:-1, 1:-1] * c[1:-1, 1:-1]
    flux_z = fz * c
    center = c[1:-1, 1:-1]
    div_x = (flux_x[1:-1, 2:] - flux_x[1:-1, :-2]) * 0.5
    div_y = (jnp.roll(flux_y, -1, 2) - jnp.roll(flux_y, 1, 2)) * 0.5
    div_z = (flux_z[2:, 1:-1] - flux_z[:-2, 1:-1]) * 0.5
    divergence = div_x + div_y + div_z
    beside_all = (
        (c[1:-1, 2:] + c[1:-1, :-2])
        + (jnp.roll(center, -1, 2) + jnp.roll(center, 1, 2))
        + (c[2:, 1:-1] + c[:-2, 1:-1])
    )
    laplace = beside_all - 6.0 * center
    return center - advect_gain * divergence + diffusion * laplace


def local(populations, voxel_mask, tracer):
    post, *faces = lb_call("first", populations, voxel_mask)
    for step in range(1, STEPS):
        halos = exchange(faces)
        post, *faces = lb_call("mid", post, voxel_mask, halos)
    halos = exchange(faces)
    state, coarse = lb_call("last", post, voxel_mask, halos)
    moved = lax.all_to_all(coarse, "blk", split_axis=2, concat_axis=3, tiled=True)
    flow = jnp.transpose(moved, (0, 2, 1, 3))
    w = TRACER_STEPS
    q = jnp.concatenate([tracer[None], flow], axis=0)
    nzb, nxb = q.shape[1], q.shape[2]
    zlo = send(q[:, nzb - w :], 0, 1)
    zhi = send(q[:, :w], 0, -1)
    xlo = send(q[:, :, nxb - w :], 1, 0)
    xhi = send(q[:, :, :w], -1, 0)
    c_mm = send(q[:, nzb - w :, nxb - w :], 1, 1)
    c_pp = send(q[:, :w, :w], -1, -1)
    c_mp = send(q[:, nzb - w :, :w], -1, 1)
    c_pm = send(q[:, :w, nxb - w :], 1, -1)
    ext = jnp.concatenate(
        [
            jnp.concatenate([c_mm, zlo, c_mp], axis=2),
            jnp.concatenate([xlo, q, xhi], axis=2),
            jnp.concatenate([c_pm, zhi, c_pp], axis=2),
        ],
        axis=1,
    )
    conc, fx, fy, fz = ext[0], ext[1], ext[2], ext[3]
    for step in range(TRACER_STEPS):
        conc = tracer_update(conc, fx, fy, fz)
        fx, fy, fz = fx[1:-1, 1:-1], fy[1:-1, 1:-1], fz[1:-1, 1:-1]
    return (state, conc)


def solution(mesh):
    placed = (P(None, "vessel", "blk", None), P("vessel", "blk", None), P("blk", "vessel", None))
    return jax.shard_map(
        local,
        mesh=mesh,
        in_specs=placed,
        out_specs=(P(None, "vessel", "blk", None), P("blk", "vessel", None)),
        check_vma=False,
    )
```

```python
import functools

import jax
import jax.numpy as jnp
import numpy as np
from jax import lax
from jax.experimental import pallas as pl
from jax.experimental.pallas import tpu as pltpu
from jax.sharding import PartitionSpec as P

STEPS = 4
TRACER_STEPS = 2


VELOCITY = np.array(
    [
        [0, 0, 0],
        [1, 0, 0],
        [-1, 0, 0],
        [0, 1, 0],
        [0, -1, 0],
        [0, 0, 1],
        [0, 0, -1],
        [1, 1, 0],
        [-1, -1, 0],
        [1, -1, 0],
        [-1, 1, 0],
        [1, 0, 1],
        [-1, 0, -1],
        [1, 0, -1],
        [-1, 0, 1],
        [0, 1, 1],
        [0, -1, -1],
        [0, 1, -1],
        [0, -1, 1],
    ]
)
WEIGHTS = np.array([1.0 / 3.0] + [1.0 / 18.0] * 6 + [1.0 / 36.0] * 12)
OPPOSITE = [0, 2, 1, 4, 3, 6, 5, 8, 7, 10, 9, 12, 11, 14, 13, 16, 15, 18, 17]
relax_rate = 1.25
pore_damping = 0.5
advect_gain = 8.0
diffusion = 0.1

NPOP = 19
CX = [int(v) for v in VELOCITY[:, 0]]
CY = [int(v) for v in VELOCITY[:, 1]]
CZ = [int(v) for v in VELOCITY[:, 2]]
CXP = [i for i in range(NPOP) if CX[i] == 1]
CXM = [i for i in range(NPOP) if CX[i] == -1]
CYP = [i for i in range(NPOP) if CY[i] == 1]
CYM = [i for i in range(NPOP) if CY[i] == -1]
SHIFTED = [i for i in range(NPOP) if CX[i] != 0 or CY[i] != 0]
ROWS = 8
YOFF = 8


def moments_chunk(g):
    w0 = jnp.float32(WEIGHTS[0])
    w1 = jnp.float32(WEIGHTS[1])
    w2 = jnp.float32(WEIGHTS[7])
    s1 = ((g[1] + g[2]) + (g[3] + g[4])) + (g[5] + g[6])
    s2 = (((g[7] + g[8]) + (g[9] + g[10])) + ((g[11] + g[12]) + (g[13] + g[14]))) + (
        (g[15] + g[16]) + (g[17] + g[18])
    )
    density = w0 * g[0] + w1 * s1 + w2 * s2
    mx = w1 * (g[1] - g[2]) + w2 * (((g[7] - g[8]) + (g[9] - g[10])) + ((g[11] - g[12]) + (g[13] - g[14])))
    my = w1 * (g[3] - g[4]) + w2 * (((g[7] - g[8]) + (g[10] - g[9])) + ((g[15] - g[16]) + (g[17] - g[18])))
    mz = w1 * (g[5] - g[6]) + w2 * (((g[11] - g[12]) + (g[14] - g[13])) + ((g[15] - g[16]) + (g[18] - g[17])))
    return density, (mx, my, mz)


def collide_chunk(g, mask):
    density, (mx, my, mz) = moments_chunk(g)
    ux = mx / density
    uy = my / density
    uz = mz / density
    porous = mask == 1
    ux = jnp.where(porous, pore_damping * ux, ux)
    uy = jnp.where(porous, pore_damping * uy, uy)
    uz = jnp.where(porous, pore_damping * uz, uz)
    speed_sq = ux * ux + uy * uy + uz * uz
    solid = mask == 2
    comps = (ux, uy, uz)
    out = [None] * NPOP
    for i in range(NPOP):
        proj = None
        for d in range(3):
            c = int(VELOCITY[i, d])
            if c == 0:
                continue
            term = comps[d] if c > 0 else -comps[d]
            proj = term if proj is None else proj + term
        if proj is None:
            balance = density * (1.0 - 1.5 * speed_sq)
        else:
            balance = density * (1.0 + 3.0 * proj + 4.5 * proj * proj - 1.5 * speed_sq)
        relaxed = g[i] + relax_rate * (balance - g[i])
        out[i] = jnp.where(solid, g[OPPOSITE[i]], relaxed)
    return out


def lb_kernel(halo, nx, ny, *refs):
    g0, mask_ref, xlo, xhi, ylo, yhi, c_mm, c_mp, c_pm, c_pp = refs[:10]
    out_ref, coarse_ref, abuf, bbuf, flow_s = refs[10:]
    h = halo
    top = YOFF
    abuf[0:NPOP, h : h + nx, top : top + ny, :] = g0[...]
    abuf[NPOP, h : h + nx, top : top + ny, :] = mask_ref[...].astype(jnp.float32)
    abuf[:, 0:h, top : top + ny, :] = xlo[...]
    abuf[:, h + nx : 2 * h + nx, top : top + ny, :] = xhi[...]
    abuf[:, h : h + nx, top - h : top, :] = ylo[...]
    abuf[:, h : h + nx, top + ny : top + ny + h, :] = yhi[...]
    abuf[:, 0:h, top - h : top, :] = c_mm[...]
    abuf[:, h + nx : 2 * h + nx, top - h : top, :] = c_mp[...]
    abuf[:, 0:h, top + ny : top + ny + h, :] = c_pm[...]
    abuf[:, h + nx : 2 * h + nx, top + ny : top + ny + h, :] = c_pp[...]

    bufs = [bbuf, abuf]
    offs = [top] + [h - s for s in range(1, h + 1)]

    def run_step(s):
        src = abuf if s == 0 else bufs[(s - 1) % 2]
        dst = bufs[s % 2]
        if s == 0:
            rows = list(range(0, top + ny + h, ROWS))
        else:
            rows = list(range(0, ny + 2 * (h - s), ROWS))
        shift = offs[s - 1] - offs[s] if s > 0 else 0

        def body(x, carry):
            for r in rows:
                g = []
                for i in range(NPOP):
                    if s == 0:
                        v = src[i, x, pl.ds(r, ROWS), :]
                    else:
                        v = src[i, x - CX[i], pl.ds(r + shift - CY[i], ROWS), :]
                        if CZ[i] != 0:
                            v = pltpu.roll(v, CZ[i] % v.shape[1], 1)
                    g.append(v)
                mask = abuf[NPOP, x, pl.ds(r - offs[s] + top, ROWS), :]
                post = collide_chunk(g, mask)
                for i in range(NPOP):
                    dst[i, x, pl.ds(r, ROWS), :] = post[i]
            return carry

        lax.fori_loop(s, nx + 2 * h - s, body, 0)

    for s in range(h):
        run_step(s)

    src = bufs[(h - 1) % 2]
    shift = offs[h - 1] - 0

    def last_body(x, carry):
        for r in range(0, ny, ROWS):
            g = []
            for i in range(NPOP):
                v = src[i, x + h - CX[i], pl.ds(r + shift - CY[i], ROWS), :]
                if CZ[i] != 0:
                    v = pltpu.roll(v, CZ[i] % v.shape[1], 1)
                g.append(v)
                out_ref[i, x, pl.ds(r, ROWS), :] = v
            mask = abuf[NPOP, x + h, pl.ds(r + top, ROWS), :]
            density, mom = moments_chunk(g)
            solid = mask == 2
            for d in range(3):
                flow_s[d, x, pl.ds(r, ROWS), :] = jnp.where(solid, jnp.float32(0.0), mom[d] / density)
        return carry

    lax.fori_loop(0, nx, last_body, 0)

    nz = flow_s.shape[3]
    pz = (
        lax.broadcasted_iota(jnp.int32, (nz // 2, nz), 1) // 2 == lax.broadcasted_iota(jnp.int32, (nz // 2, nz), 0)
    ).astype(jnp.float32)
    py = (
        lax.broadcasted_iota(jnp.int32, (ny, ny // 2), 0) // 2 == lax.broadcasted_iota(jnp.int32, (ny, ny // 2), 1)
    ).astype(jnp.float32)
    for d in range(3):
        for xp in range(nx // 2):
            plane = flow_s[d, 2 * xp] + flow_s[d, 2 * xp + 1]
            zy = lax.dot_general(
                pz,
                plane,
                (((1,), (1,)), ((), ())),
                precision=lax.Precision.HIGHEST,
                preferred_element_type=jnp.float32,
            )
            zc = jnp.dot(zy, py, precision=lax.Precision.HIGHEST, preferred_element_type=jnp.float32)
            coarse_ref[d, xp] = zc * jnp.float32(0.125)


def lb_call(g0, mask, halos, halo):
    _, nx, ny, nz = g0.shape
    f32 = jnp.float32
    vmem = pl.BlockSpec(memory_space=pltpu.VMEM)
    rows = YOFF + ny + 2 * halo
    rows = -(-rows // ROWS) * ROWS
    out_shape = (
        jax.ShapeDtypeStruct(g0.shape, f32),
        jax.ShapeDtypeStruct((3, nx // 2, nz // 2, ny // 2), f32),
    )
    scratch = [
        pltpu.VMEM((NPOP + 1, nx + 2 * halo, rows, nz), f32),
        pltpu.VMEM((NPOP, nx + 2 * halo, rows, nz), f32),
        pltpu.VMEM((3, nx, ny, nz), f32),
    ]
    cells = (nx + halo) * (ny + 2 * halo) * nz * halo
    cost = pl.CostEstimate(flops=320 * cells, transcendentals=0, bytes_accessed=2 * NPOP * 4 * nx * ny * nz * 2)
    return pl.pallas_call(
        functools.partial(lb_kernel, halo, nx, ny),
        out_shape=out_shape,
        in_specs=[vmem] * (2 + len(halos)),
        out_specs=(vmem, vmem),
        scratch_shapes=scratch,
        cost_estimate=cost,
        compiler_params=pltpu.CompilerParams(vmem_limit_bytes=60 * 1024 * 1024),
    )(g0, mask, *halos)


def send(x, dv, db):
    nv = lax.axis_size("vessel")
    nb = lax.axis_size("blk")
    if db == 0:
        return lax.ppermute(x, "vessel", [(i, (i + dv) % nv) for i in range(nv)])
    if dv == 0:
        return lax.ppermute(x, "blk", [(i, (i + db) % nb) for i in range(nb)])
    pairs = []
    for v in range(nv):
        for b in range(nb):
            pairs.append((v * nb + b, ((v + dv) % nv) * nb + (b + db) % nb))
    return lax.ppermute(x, ("vessel", "blk"), pairs)


def lattice_halos(g0, mask, h):
    _, nx, ny, _ = g0.shape
    maskf = mask.astype(jnp.float32)[None]

    def piece(xs, ys):
        return jnp.concatenate([g0[:, xs, ys], maskf[:, xs, ys]], axis=0)

    lo_x, hi_x = slice(nx - h, nx), slice(0, h)
    lo_y, hi_y = slice(ny - h, ny), slice(0, h)
    whole_x, whole_y = slice(0, nx), slice(0, ny)
    return (
        send(piece(lo_x, whole_y), 1, 0),
        send(piece(hi_x, whole_y), -1, 0),
        send(piece(whole_x, lo_y), 0, 1),
        send(piece(whole_x, hi_y), 0, -1),
        send(piece(lo_x, lo_y), 1, 1),
        send(piece(hi_x, lo_y), -1, 1),
        send(piece(lo_x, hi_y), 1, -1),
        send(piece(hi_x, hi_y), -1, -1),
    )


def tracer_update(c, fx, fy, fz):
    flux_x = fx * c
    flux_y = fy[1:-1, 1:-1] * c[1:-1, 1:-1]
    flux_z = fz * c
    center = c[1:-1, 1:-1]
    div_x = (flux_x[1:-1, 2:] - flux_x[1:-1, :-2]) * 0.5
    div_y = (jnp.roll(flux_y, -1, 2) - jnp.roll(flux_y, 1, 2)) * 0.5
    div_z = (flux_z[2:, 1:-1] - flux_z[:-2, 1:-1]) * 0.5
    divergence = div_x + div_y + div_z
    beside_all = (
        (c[1:-1, 2:] + c[1:-1, :-2])
        + (jnp.roll(center, -1, 2) + jnp.roll(center, 1, 2))
        + (c[2:, 1:-1] + c[:-2, 1:-1])
    )
    laplace = beside_all - 6.0 * center
    return center - advect_gain * divergence + diffusion * laplace


def local(populations, voxel_mask, tracer):
    halos = lattice_halos(populations, voxel_mask, STEPS)
    state, coarse = lb_call(populations, voxel_mask, halos, STEPS)
    moved = lax.all_to_all(coarse, "blk", split_axis=2, concat_axis=3, tiled=True)
    flow = jnp.transpose(moved, (0, 2, 1, 3))
    w = TRACER_STEPS
    q = jnp.concatenate([tracer[None], flow], axis=0)
    nzb, nxb = q.shape[1], q.shape[2]
    zlo = send(q[:, nzb - w :], 0, 1)
    zhi = send(q[:, :w], 0, -1)
    xlo = send(q[:, :, nxb - w :], 1, 0)
    xhi = send(q[:, :, :w], -1, 0)
    c_mm = send(q[:, nzb - w :, nxb - w :], 1, 1)
    c_pp = send(q[:, :w, :w], -1, -1)
    c_mp = send(q[:, nzb - w :, :w], -1, 1)
    c_pm = send(q[:, :w, nxb - w :], 1, -1)
    ext = jnp.concatenate(
        [
            jnp.concatenate([c_mm, zlo, c_mp], axis=2),
            jnp.concatenate([xlo, q, xhi], axis=2),
            jnp.concatenate([c_pm, zhi, c_pp], axis=2),
        ],
        axis=1,
    )
    conc, fx, fy, fz = ext[0], ext[1], ext[2], ext[3]
    for step in range(TRACER_STEPS):
        conc = tracer_update(conc, fx, fy, fz)
        fx, fy, fz = fx[1:-1, 1:-1], fy[1:-1, 1:-1], fz[1:-1, 1:-1]
    return (state, conc)


def solution(mesh):
    placed = (P(None, "vessel", "blk", None), P("vessel", "blk", None), P("blk", "vessel", None))
    return jax.shard_map(
        local,
        mesh=mesh,
        in_specs=placed,
        out_specs=(P(None, "vessel", "blk", None), P("blk", "vessel", None)),
        check_vma=False,
    )
```

```python
import functools

import jax
import jax.numpy as jnp
import numpy as np
from jax import lax
from jax.experimental import pallas as pl
from jax.experimental.pallas import tpu as pltpu
from jax.sharding import PartitionSpec as P

STEPS = 4
TRACER_STEPS = 2


VELOCITY = np.array(
    [
        [0, 0, 0],
        [1, 0, 0],
        [-1, 0, 0],
        [0, 1, 0],
        [0, -1, 0],
        [0, 0, 1],
        [0, 0, -1],
        [1, 1, 0],
        [-1, -1, 0],
        [1, -1, 0],
        [-1, 1, 0],
        [1, 0, 1],
        [-1, 0, -1],
        [1, 0, -1],
        [-1, 0, 1],
        [0, 1, 1],
        [0, -1, -1],
        [0, 1, -1],
        [0, -1, 1],
    ]
)
WEIGHTS = np.array([1.0 / 3.0] + [1.0 / 18.0] * 6 + [1.0 / 36.0] * 12)
OPPOSITE = [0, 2, 1, 4, 3, 6, 5, 8, 7, 10, 9, 12, 11, 14, 13, 16, 15, 18, 17]
relax_rate = 1.25
pore_damping = 0.5
advect_gain = 8.0
diffusion = 0.1

NPOP = 19
CX = [int(v) for v in VELOCITY[:, 0]]
CY = [int(v) for v in VELOCITY[:, 1]]
CZ = [int(v) for v in VELOCITY[:, 2]]
CXP = [i for i in range(NPOP) if CX[i] == 1]
CXM = [i for i in range(NPOP) if CX[i] == -1]
CYP = [i for i in range(NPOP) if CY[i] == 1]
CYM = [i for i in range(NPOP) if CY[i] == -1]
SHIFTED = [i for i in range(NPOP) if CX[i] != 0 or CY[i] != 0]
ROWS = 8
YOFF = 8


def moments_chunk(g):
    w0 = jnp.float32(WEIGHTS[0])
    w1 = jnp.float32(WEIGHTS[1])
    w2 = jnp.float32(WEIGHTS[7])
    s1 = ((g[1] + g[2]) + (g[3] + g[4])) + (g[5] + g[6])
    s2 = (((g[7] + g[8]) + (g[9] + g[10])) + ((g[11] + g[12]) + (g[13] + g[14]))) + (
        (g[15] + g[16]) + (g[17] + g[18])
    )
    density = w0 * g[0] + w1 * s1 + w2 * s2
    mx = w1 * (g[1] - g[2]) + w2 * (((g[7] - g[8]) + (g[9] - g[10])) + ((g[11] - g[12]) + (g[13] - g[14])))
    my = w1 * (g[3] - g[4]) + w2 * (((g[7] - g[8]) + (g[10] - g[9])) + ((g[15] - g[16]) + (g[17] - g[18])))
    mz = w1 * (g[5] - g[6]) + w2 * (((g[11] - g[12]) + (g[14] - g[13])) + ((g[15] - g[16]) + (g[18] - g[17])))
    return density, (mx, my, mz)


def collide_chunk(g, mask):
    density, (mx, my, mz) = moments_chunk(g)
    ux = mx / density
    uy = my / density
    uz = mz / density
    porous = mask == 1
    ux = jnp.where(porous, pore_damping * ux, ux)
    uy = jnp.where(porous, pore_damping * uy, uy)
    uz = jnp.where(porous, pore_damping * uz, uz)
    speed_sq = ux * ux + uy * uy + uz * uz
    solid = mask == 2
    comps = (ux, uy, uz)
    out = [None] * NPOP
    for i in range(NPOP):
        proj = None
        for d in range(3):
            c = int(VELOCITY[i, d])
            if c == 0:
                continue
            term = comps[d] if c > 0 else -comps[d]
            proj = term if proj is None else proj + term
        if proj is None:
            balance = density * (1.0 - 1.5 * speed_sq)
        else:
            balance = density * (1.0 + 3.0 * proj + 4.5 * proj * proj - 1.5 * speed_sq)
        relaxed = g[i] + relax_rate * (balance - g[i])
        out[i] = jnp.where(solid, g[OPPOSITE[i]], relaxed)
    return out


def lb_kernel(halo, nx, ny, *refs):
    g0, mask_ref, xlo, xhi, ylo, yhi, c_mm, c_mp, c_pm, c_pp = refs[:10]
    out_ref, coarse_ref, abuf, bbuf, flow_s = refs[10:]
    h = halo
    top = YOFF
    abuf[0:NPOP, h : h + nx, top : top + ny, :] = g0[...]
    abuf[NPOP, h : h + nx, top : top + ny, :] = mask_ref[...].astype(jnp.float32)
    planes = NPOP + 1
    abuf[:, 0:h, top : top + ny, :] = xlo[0:planes]
    abuf[:, h + nx : 2 * h + nx, top : top + ny, :] = xhi[0:planes]
    abuf[:, h : h + nx, top - h : top, :] = ylo[0:planes]
    abuf[:, h : h + nx, top + ny : top + ny + h, :] = yhi[0:planes]
    abuf[:, 0:h, top - h : top, :] = c_mm[0:planes]
    abuf[:, h + nx : 2 * h + nx, top - h : top, :] = c_mp[0:planes]
    abuf[:, 0:h, top + ny : top + ny + h, :] = c_pm[0:planes]
    abuf[:, h + nx : 2 * h + nx, top + ny : top + ny + h, :] = c_pp[0:planes]

    bufs = [bbuf, abuf]
    offs = [top] + [h - s for s in range(1, h + 1)]

    def run_step(s):
        src = abuf if s == 0 else bufs[(s - 1) % 2]
        dst = bufs[s % 2]
        if s == 0:
            rows = list(range(0, top + ny + h, ROWS))
        else:
            rows = list(range(0, ny + 2 * (h - s), ROWS))
        shift = offs[s - 1] - offs[s] if s > 0 else 0

        def body(x, carry):
            for r in rows:
                g = []
                for i in range(NPOP):
                    if s == 0:
                        v = src[i, x, pl.ds(r, ROWS), :]
                    else:
                        v = src[i, x - CX[i], pl.ds(r + shift - CY[i], ROWS), :]
                        if CZ[i] != 0:
                            v = pltpu.roll(v, CZ[i] % v.shape[1], 1)
                    g.append(v)
                mask = abuf[NPOP, x, pl.ds(r - offs[s] + top, ROWS), :]
                post = collide_chunk(g, mask)
                for i in range(NPOP):
                    dst[i, x, pl.ds(r, ROWS), :] = post[i]
            return carry

        lax.fori_loop(s, nx + 2 * h - s, body, 0)

    for s in range(h):
        run_step(s)

    src = bufs[(h - 1) % 2]
    shift = offs[h - 1] - 0

    def last_body(x, carry):
        for r in range(0, ny, ROWS):
            g = []
            for i in range(NPOP):
                v = src[i, x + h - CX[i], pl.ds(r + shift - CY[i], ROWS), :]
                if CZ[i] != 0:
                    v = pltpu.roll(v, CZ[i] % v.shape[1], 1)
                g.append(v)
                out_ref[i, x, pl.ds(r, ROWS), :] = v
            mask = abuf[NPOP, x + h, pl.ds(r + top, ROWS), :]
            density, mom = moments_chunk(g)
            solid = mask == 2
            for d in range(3):
                flow_s[d, x, pl.ds(r, ROWS), :] = jnp.where(solid, jnp.float32(0.0), mom[d] / density)
        return carry

    lax.fori_loop(0, nx, last_body, 0)

    nz = flow_s.shape[3]
    pz = (
        lax.broadcasted_iota(jnp.int32, (nz // 2, nz), 1) // 2 == lax.broadcasted_iota(jnp.int32, (nz // 2, nz), 0)
    ).astype(jnp.float32)
    py = (
        lax.broadcasted_iota(jnp.int32, (ny, ny // 2), 0) // 2 == lax.broadcasted_iota(jnp.int32, (ny, ny // 2), 1)
    ).astype(jnp.float32)
    for d in range(3):
        for xp in range(nx // 2):
            plane = flow_s[d, 2 * xp] + flow_s[d, 2 * xp + 1]
            zy = lax.dot_general(
                pz,
                plane,
                (((1,), (1,)), ((), ())),
                precision=lax.Precision.HIGHEST,
                preferred_element_type=jnp.float32,
            )
            zc = jnp.dot(zy, py, precision=lax.Precision.HIGHEST, preferred_element_type=jnp.float32)
            coarse_ref[d, xp] = zc * jnp.float32(0.125)


def lb_call(g0, mask, halos, halo):
    _, nx, ny, nz = g0.shape
    f32 = jnp.float32
    vmem = pl.BlockSpec(memory_space=pltpu.VMEM)
    rows = YOFF + ny + 2 * halo
    rows = -(-rows // ROWS) * ROWS
    out_shape = (
        jax.ShapeDtypeStruct(g0.shape, f32),
        jax.ShapeDtypeStruct((3, nx // 2, nz // 2, ny // 2), f32),
    )
    scratch = [
        pltpu.VMEM((NPOP + 1, nx + 2 * halo, rows, nz), f32),
        pltpu.VMEM((NPOP, nx + 2 * halo, rows, nz), f32),
        pltpu.VMEM((3, nx, ny, nz), f32),
    ]
    cells = (nx + halo) * (ny + 2 * halo) * nz * halo
    cost = pl.CostEstimate(flops=320 * cells, transcendentals=0, bytes_accessed=2 * NPOP * 4 * nx * ny * nz * 2)
    return pl.pallas_call(
        functools.partial(lb_kernel, halo, nx, ny),
        out_shape=out_shape,
        in_specs=[vmem] * (2 + len(halos)),
        out_specs=(vmem, vmem),
        scratch_shapes=scratch,
        cost_estimate=cost,
        compiler_params=pltpu.CompilerParams(vmem_limit_bytes=60 * 1024 * 1024),
    )(g0, mask, *halos)


def send(x, dv, db):
    nv = lax.axis_size("vessel")
    nb = lax.axis_size("blk")
    if db == 0:
        return lax.ppermute(x, "vessel", [(i, (i + dv) % nv) for i in range(nv)])
    if dv == 0:
        return lax.ppermute(x, "blk", [(i, (i + db) % nb) for i in range(nb)])
    pairs = []
    for v in range(nv):
        for b in range(nb):
            pairs.append((v * nb + b, ((v + dv) % nv) * nb + (b + db) % nb))
    return lax.ppermute(x, ("vessel", "blk"), pairs)


def lattice_halos(g0, mask, conc, h, w):
    _, nx, ny, nz = g0.shape
    nzc, nxc, nyc = conc.shape
    maskf = mask.astype(jnp.float32)[None]
    lat = {1: slice(nx - h, nx), -1: slice(0, h), 0: slice(0, nx)}
    lat_y = {1: slice(ny - h, ny), -1: slice(0, h), 0: slice(0, ny)}
    trc_x = {1: slice(nxc - w, nxc), -1: slice(0, w), 0: slice(0, nxc)}
    trc_z = {1: slice(nzc - w, nzc), -1: slice(0, w), 0: slice(0, nzc)}
    order = ((1, 0), (-1, 0), (0, 1), (0, -1), (1, 1), (-1, 1), (1, -1), (-1, -1))
    pieces, tracer_pieces = [], []
    for dv, db in order:
        xs, ys = lat[dv], lat_y[db]
        lb = jnp.concatenate([g0[:, xs, ys], maskf[:, xs, ys]], axis=0)
        tp = conc[trc_z[db], trc_x[dv]]
        plane = lb.shape[1] * lb.shape[2] * nz
        flat = jnp.pad(tp.reshape(-1), (0, plane - tp.size))
        msg = jnp.concatenate([lb, flat.reshape(1, lb.shape[1], lb.shape[2], nz)], axis=0)
        got = send(msg, dv, db)
        pieces.append(got)
        tracer_pieces.append(got[NPOP + 1].reshape(-1)[: tp.size].reshape(tp.shape))
    return pieces, tracer_pieces


def tracer_update(c, fx, fy, fz):
    flux_x = fx * c
    flux_y = fy[1:-1, 1:-1] * c[1:-1, 1:-1]
    flux_z = fz * c
    center = c[1:-1, 1:-1]
    div_x = (flux_x[1:-1, 2:] - flux_x[1:-1, :-2]) * 0.5
    div_y = (jnp.roll(flux_y, -1, 2) - jnp.roll(flux_y, 1, 2)) * 0.5
    div_z = (flux_z[2:, 1:-1] - flux_z[:-2, 1:-1]) * 0.5
    divergence = div_x + div_y + div_z
    beside_all = (
        (c[1:-1, 2:] + c[1:-1, :-2])
        + (jnp.roll(center, -1, 2) + jnp.roll(center, 1, 2))
        + (c[2:, 1:-1] + c[:-2, 1:-1])
    )
    laplace = beside_all - 6.0 * center
    return center - advect_gain * divergence + diffusion * laplace


def local(populations, voxel_mask, tracer):
    w = TRACER_STEPS
    halos, tp = lattice_halos(populations, voxel_mask, tracer, STEPS, w)
    state, coarse = lb_call(populations, voxel_mask, halos, STEPS)
    nzt = coarse.shape[2]
    nb = lax.axis_size("blk")
    zb = nzt // nb
    ring = jnp.concatenate([coarse[:, :, nzt - w :], coarse, coarse[:, :, :zb]], axis=2)
    head = ring[:, :, : nb * zb].reshape(3, coarse.shape[1], nb, zb, coarse.shape[3])
    tail = ring[:, :, zb : zb + nb * zb].reshape(3, coarse.shape[1], nb, zb, coarse.shape[3])
    windows = jnp.concatenate([head, tail], axis=3)[:, :, :, : zb + 2 * w]
    moved = lax.all_to_all(windows, "blk", split_axis=2, concat_axis=4, tiled=True)
    flow = moved[:, :, 0]
    nxb = flow.shape[1]
    flow = jnp.concatenate([send(flow[:, nxb - w :], 1, 0), flow, send(flow[:, :w], -1, 0)], axis=1)
    flow = jnp.transpose(flow, (0, 2, 1, 3))
    xlo, xhi, zlo, zhi, c_mm, c_mp, c_pm, c_pp = tp
    conc = jnp.concatenate(
        [
            jnp.concatenate([c_mm, zlo, c_mp], axis=1),
            jnp.concatenate([xlo, tracer, xhi], axis=1),
            jnp.concatenate([c_pm, zhi, c_pp], axis=1),
        ],
        axis=0,
    )
    fx, fy, fz = flow[0], flow[1], flow[2]
    for step in range(TRACER_STEPS):
        conc = tracer_update(conc, fx, fy, fz)
        fx, fy, fz = fx[1:-1, 1:-1], fy[1:-1, 1:-1], fz[1:-1, 1:-1]
    return (state, conc)


def solution(mesh):
    placed = (P(None, "vessel", "blk", None), P("vessel", "blk", None), P("blk", "vessel", None))
    return jax.shard_map(
        local,
        mesh=mesh,
        in_specs=placed,
        out_specs=(P(None, "vessel", "blk", None), P("blk", "vessel", None)),
        check_vma=False,
    )
```

```python
import functools

import jax
import jax.numpy as jnp
import numpy as np
from jax import lax
from jax.experimental import pallas as pl
from jax.experimental.pallas import tpu as pltpu
from jax.sharding import PartitionSpec as P

STEPS = 4
TRACER_STEPS = 2


VELOCITY = np.array(
    [
        [0, 0, 0],
        [1, 0, 0],
        [-1, 0, 0],
        [0, 1, 0],
        [0, -1, 0],
        [0, 0, 1],
        [0, 0, -1],
        [1, 1, 0],
        [-1, -1, 0],
        [1, -1, 0],
        [-1, 1, 0],
        [1, 0, 1],
        [-1, 0, -1],
        [1, 0, -1],
        [-1, 0, 1],
        [0, 1, 1],
        [0, -1, -1],
        [0, 1, -1],
        [0, -1, 1],
    ]
)
WEIGHTS = np.array([1.0 / 3.0] + [1.0 / 18.0] * 6 + [1.0 / 36.0] * 12)
OPPOSITE = [0, 2, 1, 4, 3, 6, 5, 8, 7, 10, 9, 12, 11, 14, 13, 16, 15, 18, 17]
relax_rate = 1.25
pore_damping = 0.5
advect_gain = 8.0
diffusion = 0.1

NPOP = 19
CX = [int(v) for v in VELOCITY[:, 0]]
CY = [int(v) for v in VELOCITY[:, 1]]
CZ = [int(v) for v in VELOCITY[:, 2]]
CXP = [i for i in range(NPOP) if CX[i] == 1]
CXM = [i for i in range(NPOP) if CX[i] == -1]
CYP = [i for i in range(NPOP) if CY[i] == 1]
CYM = [i for i in range(NPOP) if CY[i] == -1]
SHIFTED = [i for i in range(NPOP) if CX[i] != 0 or CY[i] != 0]
ROWS = 8
YOFF = 8


def moments_chunk(g):
    w0 = jnp.float32(WEIGHTS[0])
    w1 = jnp.float32(WEIGHTS[1])
    w2 = jnp.float32(WEIGHTS[7])
    s1 = ((g[1] + g[2]) + (g[3] + g[4])) + (g[5] + g[6])
    s2 = (((g[7] + g[8]) + (g[9] + g[10])) + ((g[11] + g[12]) + (g[13] + g[14]))) + (
        (g[15] + g[16]) + (g[17] + g[18])
    )
    density = w0 * g[0] + w1 * s1 + w2 * s2
    d1, d3, d5 = g[1] - g[2], g[3] - g[4], g[5] - g[6]
    d7, d9, d11, d13 = g[7] - g[8], g[9] - g[10], g[11] - g[12], g[13] - g[14]
    d15, d17 = g[15] - g[16], g[17] - g[18]
    mx = w1 * d1 + w2 * ((d7 + d9) + (d11 + d13))
    my = w1 * d3 + w2 * ((d7 - d9) + (d15 + d17))
    mz = w1 * d5 + w2 * ((d11 - d13) + (d15 - d17))
    return density, (mx, my, mz)


PAIRS = [(1, 2), (3, 4), (5, 6), (7, 8), (9, 10), (11, 12), (13, 14), (15, 16), (17, 18)]


def collide_chunk(g, mask):
    density, (mx, my, mz) = moments_chunk(g)
    scale = jnp.where(mask == 1, jnp.float32(pore_damping), jnp.float32(1.0))
    k = (1.0 / density) * scale
    ux = mx * k
    uy = my * k
    uz = mz * k
    base = 1.0 - 1.5 * (ux * ux + uy * uy + uz * uz)
    dens = relax_rate * density
    keep = 1.0 - relax_rate
    solid = mask == 2
    proj = {
        1: ux,
        3: uy,
        5: uz,
        7: ux + uy,
        9: ux - uy,
        11: ux + uz,
        13: ux - uz,
        15: uy + uz,
        17: uy - uz,
    }
    out = [None] * NPOP
    out[0] = jnp.where(solid, g[0], dens * base + keep * g[0])
    for i, j in PAIRS:
        p = proj[i]
        q = base + 4.5 * (p * p)
        t = 3.0 * p
        relaxed_i = dens * (q + t) + keep * g[i]
        relaxed_j = dens * (q - t) + keep * g[j]
        out[i] = jnp.where(solid, g[j], relaxed_i)
        out[j] = jnp.where(solid, g[i], relaxed_j)
    return out


def lb_kernel(halo, nx, ny, *refs):
    g0, mask_ref, xlo, xhi, ylo, yhi, c_mm, c_mp, c_pm, c_pp = refs[:10]
    out_ref, coarse_ref, abuf, bbuf, flow_s = refs[10:]
    h = halo
    top = YOFF
    abuf[0:NPOP, h : h + nx, top : top + ny, :] = g0[...]
    abuf[NPOP, h : h + nx, top : top + ny, :] = mask_ref[...].astype(jnp.float32)
    planes = NPOP + 1
    abuf[:, 0:h, top : top + ny, :] = xlo[0:planes]
    abuf[:, h + nx : 2 * h + nx, top : top + ny, :] = xhi[0:planes]
    abuf[:, h : h + nx, top - h : top, :] = ylo[0:planes]
    abuf[:, h : h + nx, top + ny : top + ny + h, :] = yhi[0:planes]
    abuf[:, 0:h, top - h : top, :] = c_mm[0:planes]
    abuf[:, h + nx : 2 * h + nx, top - h : top, :] = c_mp[0:planes]
    abuf[:, 0:h, top + ny : top + ny + h, :] = c_pm[0:planes]
    abuf[:, h + nx : 2 * h + nx, top + ny : top + ny + h, :] = c_pp[0:planes]

    bufs = [bbuf, abuf]
    offs = [top] + [h - s for s in range(1, h + 1)]

    def run_step(s):
        src = abuf if s == 0 else bufs[(s - 1) % 2]
        dst = bufs[s % 2]
        if s == 0:
            rows = list(range(0, top + ny + h, ROWS))
        else:
            rows = list(range(0, ny + 2 * (h - s), ROWS))
        shift = offs[s - 1] - offs[s] if s > 0 else 0

        def body(x, carry):
            for r in rows:
                g = []
                for i in range(NPOP):
                    if s == 0:
                        v = src[i, x, pl.ds(r, ROWS), :]
                    else:
                        v = src[i, x - CX[i], pl.ds(r + shift - CY[i], ROWS), :]
                        if CZ[i] != 0:
                            v = pltpu.roll(v, CZ[i] % v.shape[1], 1)
                    g.append(v)
                mask = abuf[NPOP, x, pl.ds(r - offs[s] + top, ROWS), :]
                post = collide_chunk(g, mask)
                for i in range(NPOP):
                    dst[i, x, pl.ds(r, ROWS), :] = post[i]
            return carry

        lax.fori_loop(s, nx + 2 * h - s, body, 0)

    for s in range(h):
        run_step(s)

    src = bufs[(h - 1) % 2]
    shift = offs[h - 1] - 0

    def last_body(x, carry):
        for r in range(0, ny, ROWS):
            g = []
            for i in range(NPOP):
                v = src[i, x + h - CX[i], pl.ds(r + shift - CY[i], ROWS), :]
                if CZ[i] != 0:
                    v = pltpu.roll(v, CZ[i] % v.shape[1], 1)
                g.append(v)
                out_ref[i, x, pl.ds(r, ROWS), :] = v
            mask = abuf[NPOP, x + h, pl.ds(r + top, ROWS), :]
            density, mom = moments_chunk(g)
            inv = 1.0 / density
            solid = mask == 2
            for d in range(3):
                flow_s[d, x, pl.ds(r, ROWS), :] = jnp.where(solid, jnp.float32(0.0), mom[d] * inv)
        return carry

    lax.fori_loop(0, nx, last_body, 0)

    nz = flow_s.shape[3]
    pz = (
        lax.broadcasted_iota(jnp.int32, (nz // 2, nz), 1) // 2 == lax.broadcasted_iota(jnp.int32, (nz // 2, nz), 0)
    ).astype(jnp.float32)
    py = (
        lax.broadcasted_iota(jnp.int32, (ny, ny // 2), 0) // 2 == lax.broadcasted_iota(jnp.int32, (ny, ny // 2), 1)
    ).astype(jnp.float32)
    for d in range(3):
        for xp in range(nx // 2):
            plane = flow_s[d, 2 * xp] + flow_s[d, 2 * xp + 1]
            zy = lax.dot_general(
                pz,
                plane,
                (((1,), (1,)), ((), ())),
                precision=lax.Precision.HIGHEST,
                preferred_element_type=jnp.float32,
            )
            zc = jnp.dot(zy, py, precision=lax.Precision.HIGHEST, preferred_element_type=jnp.float32)
            coarse_ref[d, xp] = zc * jnp.float32(0.125)


def lb_call(g0, mask, halos, halo):
    _, nx, ny, nz = g0.shape
    f32 = jnp.float32
    vmem = pl.BlockSpec(memory_space=pltpu.VMEM)
    rows = YOFF + ny + 2 * halo
    rows = -(-rows // ROWS) * ROWS
    out_shape = (
        jax.ShapeDtypeStruct(g0.shape, f32),
        jax.ShapeDtypeStruct((3, nx // 2, nz // 2, ny // 2), f32),
    )
    scratch = [
        pltpu.VMEM((NPOP + 1, nx + 2 * halo, rows, nz), f32),
        pltpu.VMEM((NPOP, nx + 2 * halo, rows, nz), f32),
        pltpu.VMEM((3, nx, ny, nz), f32),
    ]
    cells = (nx + halo) * (ny + 2 * halo) * nz * halo
    cost = pl.CostEstimate(flops=320 * cells, transcendentals=0, bytes_accessed=2 * NPOP * 4 * nx * ny * nz * 2)
    return pl.pallas_call(
        functools.partial(lb_kernel, halo, nx, ny),
        out_shape=out_shape,
        in_specs=[vmem] * (2 + len(halos)),
        out_specs=(vmem, vmem),
        scratch_shapes=scratch,
        cost_estimate=cost,
        compiler_params=pltpu.CompilerParams(vmem_limit_bytes=60 * 1024 * 1024),
    )(g0, mask, *halos)


def send(x, dv, db):
    nv = lax.axis_size("vessel")
    nb = lax.axis_size("blk")
    if db == 0:
        return lax.ppermute(x, "vessel", [(i, (i + dv) % nv) for i in range(nv)])
    if dv == 0:
        return lax.ppermute(x, "blk", [(i, (i + db) % nb) for i in range(nb)])
    pairs = []
    for v in range(nv):
        for b in range(nb):
            pairs.append((v * nb + b, ((v + dv) % nv) * nb + (b + db) % nb))
    return lax.ppermute(x, ("vessel", "blk"), pairs)


def lattice_halos(g0, mask, conc, h, w):
    _, nx, ny, nz = g0.shape
    nzc, nxc, nyc = conc.shape
    maskf = mask.astype(jnp.float32)[None]
    lat = {1: slice(nx - h, nx), -1: slice(0, h), 0: slice(0, nx)}
    lat_y = {1: slice(ny - h, ny), -1: slice(0, h), 0: slice(0, ny)}
    trc_x = {1: slice(nxc - w, nxc), -1: slice(0, w), 0: slice(0, nxc)}
    trc_z = {1: slice(nzc - w, nzc), -1: slice(0, w), 0: slice(0, nzc)}
    order = ((1, 0), (-1, 0), (0, 1), (0, -1), (1, 1), (-1, 1), (1, -1), (-1, -1))
    pieces, tracer_pieces = [], []
    for dv, db in order:
        xs, ys = lat[dv], lat_y[db]
        lb = jnp.concatenate([g0[:, xs, ys], maskf[:, xs, ys]], axis=0)
        tp = conc[trc_z[db], trc_x[dv]]
        plane = lb.shape[1] * lb.shape[2] * nz
        flat = jnp.pad(tp.reshape(-1), (0, plane - tp.size))
        msg = jnp.concatenate([lb, flat.reshape(1, lb.shape[1], lb.shape[2], nz)], axis=0)
        got = send(msg, dv, db)
        pieces.append(got)
        tracer_pieces.append(got[NPOP + 1].reshape(-1)[: tp.size].reshape(tp.shape))
    return pieces, tracer_pieces


def tracer_update(c, fx, fy, fz):
    flux_x = fx * c
    flux_y = fy[1:-1, 1:-1] * c[1:-1, 1:-1]
    flux_z = fz * c
    center = c[1:-1, 1:-1]
    div_x = (flux_x[1:-1, 2:] - flux_x[1:-1, :-2]) * 0.5
    div_y = (jnp.roll(flux_y, -1, 2) - jnp.roll(flux_y, 1, 2)) * 0.5
    div_z = (flux_z[2:, 1:-1] - flux_z[:-2, 1:-1]) * 0.5
    divergence = div_x + div_y + div_z
    beside_all = (
        (c[1:-1, 2:] + c[1:-1, :-2])
        + (jnp.roll(center, -1, 2) + jnp.roll(center, 1, 2))
        + (c[2:, 1:-1] + c[:-2, 1:-1])
    )
    laplace = beside_all - 6.0 * center
    return center - advect_gain * divergence + diffusion * laplace


def local(populations, voxel_mask, tracer):
    w = TRACER_STEPS
    halos, tp = lattice_halos(populations, voxel_mask, tracer, STEPS, w)
    state, coarse = lb_call(populations, voxel_mask, halos, STEPS)
    nzt = coarse.shape[2]
    nb = lax.axis_size("blk")
    zb = nzt // nb
    ring = jnp.concatenate([coarse[:, :, nzt - w :], coarse, coarse[:, :, :zb]], axis=2)
    head = ring[:, :, : nb * zb].reshape(3, coarse.shape[1], nb, zb, coarse.shape[3])
    tail = ring[:, :, zb : zb + nb * zb].reshape(3, coarse.shape[1], nb, zb, coarse.shape[3])
    windows = jnp.concatenate([head, tail], axis=3)[:, :, :, : zb + 2 * w]
    moved = lax.all_to_all(windows, "blk", split_axis=2, concat_axis=4, tiled=True)
    flow = moved[:, :, 0]
    nxb = flow.shape[1]
    flow = jnp.concatenate([send(flow[:, nxb - w :], 1, 0), flow, send(flow[:, :w], -1, 0)], axis=1)
    flow = jnp.transpose(flow, (0, 2, 1, 3))
    xlo, xhi, zlo, zhi, c_mm, c_mp, c_pm, c_pp = tp
    conc = jnp.concatenate(
        [
            jnp.concatenate([c_mm, zlo, c_mp], axis=1),
            jnp.concatenate([xlo, tracer, xhi], axis=1),
            jnp.concatenate([c_pm, zhi, c_pp], axis=1),
        ],
        axis=0,
    )
    fx, fy, fz = flow[0], flow[1], flow[2]
    for step in range(TRACER_STEPS):
        conc = tracer_update(conc, fx, fy, fz)
        fx, fy, fz = fx[1:-1, 1:-1], fy[1:-1, 1:-1], fz[1:-1, 1:-1]
    return (state, conc)


def solution(mesh):
    placed = (P(None, "vessel", "blk", None), P("vessel", "blk", None), P("blk", "vessel", None))
    return jax.shard_map(
        local,
        mesh=mesh,
        in_specs=placed,
        out_specs=(P(None, "vessel", "blk", None), P("blk", "vessel", None)),
        check_vma=False,
    )
```

```python
import functools

import jax
import jax.numpy as jnp
import numpy as np
from jax import lax
from jax.experimental import pallas as pl
from jax.experimental.pallas import tpu as pltpu
from jax.sharding import PartitionSpec as P

STEPS = 4
TRACER_STEPS = 2


VELOCITY = np.array(
    [
        [0, 0, 0],
        [1, 0, 0],
        [-1, 0, 0],
        [0, 1, 0],
        [0, -1, 0],
        [0, 0, 1],
        [0, 0, -1],
        [1, 1, 0],
        [-1, -1, 0],
        [1, -1, 0],
        [-1, 1, 0],
        [1, 0, 1],
        [-1, 0, -1],
        [1, 0, -1],
        [-1, 0, 1],
        [0, 1, 1],
        [0, -1, -1],
        [0, 1, -1],
        [0, -1, 1],
    ]
)
WEIGHTS = np.array([1.0 / 3.0] + [1.0 / 18.0] * 6 + [1.0 / 36.0] * 12)
OPPOSITE = [0, 2, 1, 4, 3, 6, 5, 8, 7, 10, 9, 12, 11, 14, 13, 16, 15, 18, 17]
relax_rate = 1.25
pore_damping = 0.5
advect_gain = 8.0
diffusion = 0.1

NPOP = 19
CX = [int(v) for v in VELOCITY[:, 0]]
CY = [int(v) for v in VELOCITY[:, 1]]
CZ = [int(v) for v in VELOCITY[:, 2]]
CXP = [i for i in range(NPOP) if CX[i] == 1]
CXM = [i for i in range(NPOP) if CX[i] == -1]
CYP = [i for i in range(NPOP) if CY[i] == 1]
CYM = [i for i in range(NPOP) if CY[i] == -1]
SHIFTED = [i for i in range(NPOP) if CX[i] != 0 or CY[i] != 0]
ROWS = 8
YOFF = 8


def moments_chunk(g):
    w0 = jnp.float32(WEIGHTS[0])
    w1 = jnp.float32(WEIGHTS[1])
    w2 = jnp.float32(WEIGHTS[7])
    s1 = ((g[1] + g[2]) + (g[3] + g[4])) + (g[5] + g[6])
    s2 = (((g[7] + g[8]) + (g[9] + g[10])) + ((g[11] + g[12]) + (g[13] + g[14]))) + (
        (g[15] + g[16]) + (g[17] + g[18])
    )
    density = w0 * g[0] + w1 * s1 + w2 * s2
    d1, d3, d5 = g[1] - g[2], g[3] - g[4], g[5] - g[6]
    d7, d9, d11, d13 = g[7] - g[8], g[9] - g[10], g[11] - g[12], g[13] - g[14]
    d15, d17 = g[15] - g[16], g[17] - g[18]
    mx = w1 * d1 + w2 * ((d7 + d9) + (d11 + d13))
    my = w1 * d3 + w2 * ((d7 - d9) + (d15 + d17))
    mz = w1 * d5 + w2 * ((d11 - d13) + (d15 - d17))
    return density, (mx, my, mz)


PAIRS = [(1, 2), (3, 4), (5, 6), (7, 8), (9, 10), (11, 12), (13, 14), (15, 16), (17, 18)]


def collide_chunk(g, mask):
    density, (mx, my, mz) = moments_chunk(g)
    scale = jnp.where(mask == 1, jnp.float32(pore_damping), jnp.float32(1.0))
    k = (1.0 / density) * scale
    ux = mx * k
    uy = my * k
    uz = mz * k
    base = 1.0 - 1.5 * (ux * ux + uy * uy + uz * uz)
    dens = relax_rate * density
    keep = 1.0 - relax_rate
    solid = mask == 2
    proj = {
        1: ux,
        3: uy,
        5: uz,
        7: ux + uy,
        9: ux - uy,
        11: ux + uz,
        13: ux - uz,
        15: uy + uz,
        17: uy - uz,
    }
    out = [None] * NPOP
    out[0] = jnp.where(solid, g[0], dens * base + keep * g[0])
    for i, j in PAIRS:
        p = proj[i]
        q = base + 4.5 * (p * p)
        t = 3.0 * p
        relaxed_i = dens * (q + t) + keep * g[i]
        relaxed_j = dens * (q - t) + keep * g[j]
        out[i] = jnp.where(solid, g[j], relaxed_i)
        out[j] = jnp.where(solid, g[i], relaxed_j)
    return out


def lb_kernel(halo, nx, ny, *refs):
    g0, mask_ref, pw_ref, py_ref, xlo, xhi, ylo, yhi, c_mm, c_mp, c_pm, c_pp = refs[:12]
    out_ref, coarse_ref, abuf, bbuf, flow_s = refs[12:]
    h = halo
    top = YOFF
    abuf[0:NPOP, h : h + nx, top : top + ny, :] = g0[...]
    abuf[NPOP, h : h + nx, top : top + ny, :] = mask_ref[...].astype(jnp.float32)
    planes = NPOP + 1
    abuf[:, 0:h, top : top + ny, :] = xlo[0:planes]
    abuf[:, h + nx : 2 * h + nx, top : top + ny, :] = xhi[0:planes]
    abuf[:, h : h + nx, top - h : top, :] = ylo[0:planes]
    abuf[:, h : h + nx, top + ny : top + ny + h, :] = yhi[0:planes]
    abuf[:, 0:h, top - h : top, :] = c_mm[0:planes]
    abuf[:, h + nx : 2 * h + nx, top - h : top, :] = c_mp[0:planes]
    abuf[:, 0:h, top + ny : top + ny + h, :] = c_pm[0:planes]
    abuf[:, h + nx : 2 * h + nx, top + ny : top + ny + h, :] = c_pp[0:planes]

    bufs = [bbuf, abuf]
    offs = [top] + [h - s for s in range(1, h + 1)]

    def run_step(s):
        src = abuf if s == 0 else bufs[(s - 1) % 2]
        dst = bufs[s % 2]
        if s == 0:
            rows = list(range(0, top + ny + h, ROWS))
        else:
            rows = list(range(0, ny + 2 * (h - s), ROWS))
        shift = offs[s - 1] - offs[s] if s > 0 else 0

        def body(x, carry):
            for r in rows:
                g = []
                for i in range(NPOP):
                    if s == 0:
                        v = src[i, x, pl.ds(r, ROWS), :]
                    else:
                        v = src[i, x - CX[i], pl.ds(r + shift - CY[i], ROWS), :]
                        if CZ[i] != 0:
                            v = pltpu.roll(v, CZ[i] % v.shape[1], 1)
                    g.append(v)
                mask = abuf[NPOP, x, pl.ds(r - offs[s] + top, ROWS), :]
                post = collide_chunk(g, mask)
                for i in range(NPOP):
                    dst[i, x, pl.ds(r, ROWS), :] = post[i]
            return carry

        lax.fori_loop(s, nx + 2 * h - s, body, 0)

    for s in range(h):
        run_step(s)

    src = bufs[(h - 1) % 2]
    shift = offs[h - 1] - 0

    def last_body(x, carry):
        for r in range(0, ny, ROWS):
            g = []
            for i in range(NPOP):
                v = src[i, x + h - CX[i], pl.ds(r + shift - CY[i], ROWS), :]
                if CZ[i] != 0:
                    v = pltpu.roll(v, CZ[i] % v.shape[1], 1)
                g.append(v)
                out_ref[i, x, pl.ds(r, ROWS), :] = v
            mask = abuf[NPOP, x + h, pl.ds(r + top, ROWS), :]
            density, mom = moments_chunk(g)
            inv = 1.0 / density
            solid = mask == 2
            for d in range(3):
                flow_s[d, x, pl.ds(r, ROWS), :] = jnp.where(solid, jnp.float32(0.0), mom[d] * inv)
        return carry

    lax.fori_loop(0, nx, last_body, 0)

    nwin, win = coarse_ref.shape[0], coarse_ref.shape[3]
    pw = pw_ref[...]
    py = py_ref[...]
    for d in range(3):
        for xp in range(nx // 2):
            plane = flow_s[d, 2 * xp] + flow_s[d, 2 * xp + 1]
            zy = lax.dot_general(
                pw,
                plane,
                (((1,), (1,)), ((), ())),
                precision=lax.Precision.HIGHEST,
                preferred_element_type=jnp.float32,
            )
            zc = jnp.dot(zy, py, precision=lax.Precision.HIGHEST, preferred_element_type=jnp.float32)
            zc = zc * jnp.float32(0.125)
            for j in range(nwin):
                coarse_ref[j, d, xp] = zc[j * win : (j + 1) * win]


def lb_call(g0, mask, halos, halo, nwin, w):
    _, nx, ny, nz = g0.shape
    zb = nz // 2 // nwin
    win = zb + 2 * w
    rows = np.arange(nwin * win)
    coarse_z = (rows // win * zb - w + rows % win) % (nz // 2)
    pw = jnp.asarray((np.arange(nz)[None, :] // 2 == coarse_z[:, None]).astype(np.float32))
    py = jnp.asarray((np.arange(ny)[:, None] // 2 == np.arange(ny // 2)[None, :]).astype(np.float32))
    f32 = jnp.float32
    vmem = pl.BlockSpec(memory_space=pltpu.VMEM)
    rows = YOFF + ny + 2 * halo
    rows = -(-rows // ROWS) * ROWS
    out_shape = (
        jax.ShapeDtypeStruct(g0.shape, f32),
        jax.ShapeDtypeStruct((nwin, 3, nx // 2, win, ny // 2), f32),
    )
    scratch = [
        pltpu.VMEM((NPOP + 1, nx + 2 * halo, rows, nz), f32),
        pltpu.VMEM((NPOP, nx + 2 * halo, rows, nz), f32),
        pltpu.VMEM((3, nx, ny, nz), f32),
    ]
    cells = (nx + halo) * (ny + 2 * halo) * nz * halo
    cost = pl.CostEstimate(flops=320 * cells, transcendentals=0, bytes_accessed=2 * NPOP * 4 * nx * ny * nz * 2)
    return pl.pallas_call(
        functools.partial(lb_kernel, halo, nx, ny),
        out_shape=out_shape,
        in_specs=[vmem] * (4 + len(halos)),
        out_specs=(vmem, vmem),
        scratch_shapes=scratch,
        cost_estimate=cost,
        compiler_params=pltpu.CompilerParams(vmem_limit_bytes=60 * 1024 * 1024),
    )(g0, mask, pw, py, *halos)


def send(x, dv, db):
    nv = lax.axis_size("vessel")
    nb = lax.axis_size("blk")
    if db == 0:
        return lax.ppermute(x, "vessel", [(i, (i + dv) % nv) for i in range(nv)])
    if dv == 0:
        return lax.ppermute(x, "blk", [(i, (i + db) % nb) for i in range(nb)])
    pairs = []
    for v in range(nv):
        for b in range(nb):
            pairs.append((v * nb + b, ((v + dv) % nv) * nb + (b + db) % nb))
    return lax.ppermute(x, ("vessel", "blk"), pairs)


def lattice_halos(g0, mask, conc, h, w):
    _, nx, ny, nz = g0.shape
    nzc, nxc, nyc = conc.shape
    maskf = mask.astype(jnp.float32)[None]
    lat = {1: slice(nx - h, nx), -1: slice(0, h), 0: slice(0, nx)}
    lat_y = {1: slice(ny - h, ny), -1: slice(0, h), 0: slice(0, ny)}
    trc_x = {1: slice(nxc - w, nxc), -1: slice(0, w), 0: slice(0, nxc)}
    trc_z = {1: slice(nzc - w, nzc), -1: slice(0, w), 0: slice(0, nzc)}
    order = ((1, 0), (-1, 0), (0, 1), (0, -1), (1, 1), (-1, 1), (1, -1), (-1, -1))
    pieces, tracer_pieces = [], []
    for dv, db in order:
        xs, ys = lat[dv], lat_y[db]
        lb = jnp.concatenate([g0[:, xs, ys], maskf[:, xs, ys]], axis=0)
        tp = conc[trc_z[db], trc_x[dv]]
        plane = lb.shape[1] * lb.shape[2] * nz
        flat = jnp.pad(tp.reshape(-1), (0, plane - tp.size))
        msg = jnp.concatenate([lb, flat.reshape(1, lb.shape[1], lb.shape[2], nz)], axis=0)
        got = send(msg, dv, db)
        pieces.append(got)
        tracer_pieces.append(got[NPOP + 1].reshape(-1)[: tp.size].reshape(tp.shape))
    return pieces, tracer_pieces


def tracer_update(c, fx, fy, fz):
    flux_x = fx * c
    flux_y = fy[1:-1, 1:-1] * c[1:-1, 1:-1]
    flux_z = fz * c
    center = c[1:-1, 1:-1]
    div_x = (flux_x[1:-1, 2:] - flux_x[1:-1, :-2]) * 0.5
    div_y = (jnp.roll(flux_y, -1, 2) - jnp.roll(flux_y, 1, 2)) * 0.5
    div_z = (flux_z[2:, 1:-1] - flux_z[:-2, 1:-1]) * 0.5
    divergence = div_x + div_y + div_z
    beside_all = (
        (c[1:-1, 2:] + c[1:-1, :-2])
        + (jnp.roll(center, -1, 2) + jnp.roll(center, 1, 2))
        + (c[2:, 1:-1] + c[:-2, 1:-1])
    )
    laplace = beside_all - 6.0 * center
    return center - advect_gain * divergence + diffusion * laplace


def local(populations, voxel_mask, tracer):
    w = TRACER_STEPS
    halos, tp = lattice_halos(populations, voxel_mask, tracer, STEPS, w)
    nb = lax.axis_size("blk")
    state, windows = lb_call(populations, voxel_mask, halos, STEPS, nb, w)
    moved = lax.all_to_all(windows, "blk", split_axis=0, concat_axis=0, tiled=True)
    _, _, nxb, nzw, nys = moved.shape
    flow = jnp.transpose(moved, (1, 3, 2, 0, 4)).reshape(3, nzw, nxb, nb * nys)
    flow = jnp.concatenate([send(flow[:, :, nxb - w :], 1, 0), flow, send(flow[:, :, :w], -1, 0)], axis=2)
    xlo, xhi, zlo, zhi, c_mm, c_mp, c_pm, c_pp = tp
    conc = jnp.concatenate(
        [
            jnp.concatenate([c_mm, zlo, c_mp], axis=1),
            jnp.concatenate([xlo, tracer, xhi], axis=1),
            jnp.concatenate([c_pm, zhi, c_pp], axis=1),
        ],
        axis=0,
    )
    fx, fy, fz = flow[0], flow[1], flow[2]
    for step in range(TRACER_STEPS):
        conc = tracer_update(conc, fx, fy, fz)
        fx, fy, fz = fx[1:-1, 1:-1], fy[1:-1, 1:-1], fz[1:-1, 1:-1]
    return (state, conc)


def solution(mesh):
    placed = (P(None, "vessel", "blk", None), P("vessel", "blk", None), P("blk", "vessel", None))
    return jax.shard_map(
        local,
        mesh=mesh,
        in_specs=placed,
        out_specs=(P(None, "vessel", "blk", None), P("blk", "vessel", None)),
        check_vma=False,
    )
```

```python
import functools

import jax
import jax.numpy as jnp
import numpy as np
from jax import lax
from jax.experimental import pallas as pl
from jax.experimental.pallas import tpu as pltpu
from jax.sharding import PartitionSpec as P

STEPS = 4
TRACER_STEPS = 2


VELOCITY = np.array(
    [
        [0, 0, 0],
        [1, 0, 0],
        [-1, 0, 0],
        [0, 1, 0],
        [0, -1, 0],
        [0, 0, 1],
        [0, 0, -1],
        [1, 1, 0],
        [-1, -1, 0],
        [1, -1, 0],
        [-1, 1, 0],
        [1, 0, 1],
        [-1, 0, -1],
        [1, 0, -1],
        [-1, 0, 1],
        [0, 1, 1],
        [0, -1, -1],
        [0, 1, -1],
        [0, -1, 1],
    ]
)
WEIGHTS = np.array([1.0 / 3.0] + [1.0 / 18.0] * 6 + [1.0 / 36.0] * 12)
OPPOSITE = [0, 2, 1, 4, 3, 6, 5, 8, 7, 10, 9, 12, 11, 14, 13, 16, 15, 18, 17]
relax_rate = 1.25
pore_damping = 0.5
advect_gain = 8.0
diffusion = 0.1

NPOP = 19
CX = [int(v) for v in VELOCITY[:, 0]]
CY = [int(v) for v in VELOCITY[:, 1]]
CZ = [int(v) for v in VELOCITY[:, 2]]
CXP = [i for i in range(NPOP) if CX[i] == 1]
CXM = [i for i in range(NPOP) if CX[i] == -1]
CYP = [i for i in range(NPOP) if CY[i] == 1]
CYM = [i for i in range(NPOP) if CY[i] == -1]
SHIFTED = [i for i in range(NPOP) if CX[i] != 0 or CY[i] != 0]
ROWS = 8
YOFF = 8


def moments_chunk(g):
    w0 = jnp.float32(WEIGHTS[0])
    w1 = jnp.float32(WEIGHTS[1])
    w2 = jnp.float32(WEIGHTS[7])
    s1 = ((g[1] + g[2]) + (g[3] + g[4])) + (g[5] + g[6])
    s2 = (((g[7] + g[8]) + (g[9] + g[10])) + ((g[11] + g[12]) + (g[13] + g[14]))) + (
        (g[15] + g[16]) + (g[17] + g[18])
    )
    density = w0 * g[0] + w1 * s1 + w2 * s2
    d1, d3, d5 = g[1] - g[2], g[3] - g[4], g[5] - g[6]
    d7, d9, d11, d13 = g[7] - g[8], g[9] - g[10], g[11] - g[12], g[13] - g[14]
    d15, d17 = g[15] - g[16], g[17] - g[18]
    mx = w1 * d1 + w2 * ((d7 + d9) + (d11 + d13))
    my = w1 * d3 + w2 * ((d7 - d9) + (d15 + d17))
    mz = w1 * d5 + w2 * ((d11 - d13) + (d15 - d17))
    return density, (mx, my, mz)


PAIRS = [(1, 2), (3, 4), (5, 6), (7, 8), (9, 10), (11, 12), (13, 14), (15, 16), (17, 18)]


def collide_chunk(g, mask):
    density, (mx, my, mz) = moments_chunk(g)
    scale = jnp.where(mask == 1, jnp.float32(pore_damping), jnp.float32(1.0))
    k = (1.0 / density) * scale
    ux = mx * k
    uy = my * k
    uz = mz * k
    base = 1.0 - 1.5 * (ux * ux + uy * uy + uz * uz)
    dens = relax_rate * density
    keep = 1.0 - relax_rate
    solid = mask == 2
    proj = {
        1: ux,
        3: uy,
        5: uz,
        7: ux + uy,
        9: ux - uy,
        11: ux + uz,
        13: ux - uz,
        15: uy + uz,
        17: uy - uz,
    }
    out = [None] * NPOP
    out[0] = jnp.where(solid, g[0], dens * base + keep * g[0])
    for i, j in PAIRS:
        p = proj[i]
        q = base + 4.5 * (p * p)
        t = 3.0 * p
        relaxed_i = dens * (q + t) + keep * g[i]
        relaxed_j = dens * (q - t) + keep * g[j]
        out[i] = jnp.where(solid, g[j], relaxed_i)
        out[j] = jnp.where(solid, g[i], relaxed_j)
    return out


def lb_kernel(halo, nx, ny, *refs):
    g0, mask_ref, xlo, xhi, ylo, yhi, c_mm, c_mp, c_pm, c_pp = refs[:10]
    out_ref, coarse_ref, abuf, bbuf, flow_s = refs[10:]
    h = halo
    top = YOFF
    abuf[0:NPOP, h : h + nx, top : top + ny, :] = g0[...]
    abuf[NPOP, h : h + nx, top : top + ny, :] = mask_ref[...].astype(jnp.float32)
    planes = NPOP + 1
    abuf[:, 0:h, top : top + ny, :] = xlo[0:planes]
    abuf[:, h + nx : 2 * h + nx, top : top + ny, :] = xhi[0:planes]
    abuf[:, h : h + nx, top - h : top, :] = ylo[0:planes]
    abuf[:, h : h + nx, top + ny : top + ny + h, :] = yhi[0:planes]
    abuf[:, 0:h, top - h : top, :] = c_mm[0:planes]
    abuf[:, h + nx : 2 * h + nx, top - h : top, :] = c_mp[0:planes]
    abuf[:, 0:h, top + ny : top + ny + h, :] = c_pm[0:planes]
    abuf[:, h + nx : 2 * h + nx, top + ny : top + ny + h, :] = c_pp[0:planes]

    bufs = [abuf, bbuf]
    offs = [top] + [h - s for s in range(1, h + 1)]

    def run_step(s):
        src = bufs[(s - 1) % 2]
        dst = bufs[s % 2]
        rows = list(range(0, ny + 2 * (h - s), ROWS))
        shift = offs[s - 1] - offs[s]

        def body(x, carry):
            for r in rows:
                g = []
                for i in range(NPOP):
                    v = src[i, x - CX[i], pl.ds(r + shift - CY[i], ROWS), :]
                    if CZ[i] != 0:
                        v = pltpu.roll(v, CZ[i] % v.shape[1], 1)
                    g.append(v)
                mask = abuf[NPOP, x, pl.ds(r - offs[s] + top, ROWS), :]
                post = collide_chunk(g, mask)
                for i in range(NPOP):
                    dst[i, x, pl.ds(r, ROWS), :] = post[i]
            return carry

        lax.fori_loop(s, nx + 2 * h - s, body, 0)

    for s in range(1, h):
        run_step(s)

    src = bufs[(h - 1) % 2]
    shift = offs[h - 1] - 0

    def last_body(x, carry):
        for r in range(0, ny, ROWS):
            g = []
            for i in range(NPOP):
                v = src[i, x + h - CX[i], pl.ds(r + shift - CY[i], ROWS), :]
                if CZ[i] != 0:
                    v = pltpu.roll(v, CZ[i] % v.shape[1], 1)
                g.append(v)
                out_ref[i, x, pl.ds(r, ROWS), :] = v
            mask = abuf[NPOP, x + h, pl.ds(r + top, ROWS), :]
            density, mom = moments_chunk(g)
            inv = 1.0 / density
            solid = mask == 2
            for d in range(3):
                flow_s[d, x, pl.ds(r, ROWS), :] = jnp.where(solid, jnp.float32(0.0), mom[d] * inv)
        return carry

    lax.fori_loop(0, nx, last_body, 0)

    nz = flow_s.shape[3]
    pz = (
        lax.broadcasted_iota(jnp.int32, (nz // 2, nz), 1) // 2 == lax.broadcasted_iota(jnp.int32, (nz // 2, nz), 0)
    ).astype(jnp.float32)
    py = (
        lax.broadcasted_iota(jnp.int32, (ny, ny // 2), 0) // 2 == lax.broadcasted_iota(jnp.int32, (ny, ny // 2), 1)
    ).astype(jnp.float32)
    for d in range(3):
        for xp in range(nx // 2):
            plane = flow_s[d, 2 * xp] + flow_s[d, 2 * xp + 1]
            zy = lax.dot_general(
                pz,
                plane,
                (((1,), (1,)), ((), ())),
                precision=lax.Precision.HIGHEST,
                preferred_element_type=jnp.float32,
            )
            zc = jnp.dot(zy, py, precision=lax.Precision.HIGHEST, preferred_element_type=jnp.float32)
            coarse_ref[d, xp] = zc * jnp.float32(0.125)


def lb_call(g0, mask, halos, halo):
    _, nx, ny, nz = g0.shape
    f32 = jnp.float32
    vmem = pl.BlockSpec(memory_space=pltpu.VMEM)
    rows = YOFF + ny + 2 * halo
    rows = -(-rows // ROWS) * ROWS
    out_shape = (
        jax.ShapeDtypeStruct(g0.shape, f32),
        jax.ShapeDtypeStruct((3, nx // 2, nz // 2, ny // 2), f32),
    )
    scratch = [
        pltpu.VMEM((NPOP + 1, nx + 2 * halo, rows, nz), f32),
        pltpu.VMEM((NPOP, nx + 2 * halo, rows, nz), f32),
        pltpu.VMEM((3, nx, ny, nz), f32),
    ]
    cells = (nx + halo) * (ny + 2 * halo) * nz * halo
    cost = pl.CostEstimate(flops=320 * cells, transcendentals=0, bytes_accessed=2 * NPOP * 4 * nx * ny * nz * 2)
    return pl.pallas_call(
        functools.partial(lb_kernel, halo, nx, ny),
        out_shape=out_shape,
        in_specs=[vmem] * (2 + len(halos)),
        out_specs=(vmem, vmem),
        scratch_shapes=scratch,
        cost_estimate=cost,
        compiler_params=pltpu.CompilerParams(vmem_limit_bytes=60 * 1024 * 1024),
    )(g0, mask, *halos)


def send(x, dv, db):
    nv = lax.axis_size("vessel")
    nb = lax.axis_size("blk")
    if db == 0:
        return lax.ppermute(x, "vessel", [(i, (i + dv) % nv) for i in range(nv)])
    if dv == 0:
        return lax.ppermute(x, "blk", [(i, (i + db) % nb) for i in range(nb)])
    pairs = []
    for v in range(nv):
        for b in range(nb):
            pairs.append((v * nb + b, ((v + dv) % nv) * nb + (b + db) % nb))
    return lax.ppermute(x, ("vessel", "blk"), pairs)


ORDER = ((1, 0), (-1, 0), (0, 1), (0, -1), (1, 1), (-1, 1), (1, -1), (-1, -1))


def edge(n, h, d):
    return {1: slice(n - h, n), -1: slice(0, h), 0: slice(0, n)}[d]


def first_kernel(h, nx, ny, *refs):
    g0, mask_ref = refs[:2]
    tplanes = refs[2:10]
    post_ref = refs[10]
    msgs = refs[11:19]

    def body(x, carry):
        for r in range(0, ny, ROWS):
            g = [g0[i, x, pl.ds(r, ROWS), :] for i in range(NPOP)]
            post = collide_chunk(g, mask_ref[x, pl.ds(r, ROWS), :])
            for i in range(NPOP):
                post_ref[i, x, pl.ds(r, ROWS), :] = post[i]
        return carry

    lax.fori_loop(0, nx, body, 0)
    for k, (dv, db) in enumerate(ORDER):
        xs, ys = edge(nx, h, dv), edge(ny, h, db)
        msgs[k][0:NPOP] = post_ref[:, xs, ys, :]
        msgs[k][NPOP] = mask_ref[xs, ys, :].astype(jnp.float32)
        msgs[k][NPOP + 1] = tplanes[k][...]


def lattice_halos(g0, mask, conc, h, w):
    _, nx, ny, nz = g0.shape
    nzc, nxc, _ = conc.shape
    f32 = jnp.float32
    tplanes, tshapes = [], []
    for dv, db in ORDER:
        a, b = (h if dv else nx), (h if db else ny)
        tp = conc[edge(nzc, w, db), edge(nxc, w, dv)]
        tshapes.append(tp.shape)
        tplanes.append(jnp.pad(tp.reshape(-1), (0, a * b * nz - tp.size)).reshape(a, b, nz))
    vmem = pl.BlockSpec(memory_space=pltpu.VMEM)
    out_shape = (jax.ShapeDtypeStruct(g0.shape, f32),) + tuple(
        jax.ShapeDtypeStruct((NPOP + 2,) + t.shape, f32) for t in tplanes
    )
    cells = nx * ny * nz
    outs = pl.pallas_call(
        functools.partial(first_kernel, h, nx, ny),
        out_shape=out_shape,
        in_specs=[vmem] * 10,
        out_specs=tuple(vmem for _ in out_shape),
        cost_estimate=pl.CostEstimate(flops=200 * cells, transcendentals=0, bytes_accessed=NPOP * 4 * cells * 3),
        compiler_params=pltpu.CompilerParams(vmem_limit_bytes=48 * 1024 * 1024),
    )(g0, mask, *tplanes)
    post0, msgs = outs[0], outs[1:]
    pieces, tracer_pieces = [], []
    for (dv, db), msg, shape in zip(ORDER, msgs, tshapes):
        got = send(msg, dv, db)
        pieces.append(got)
        size = int(np.prod(shape))
        tracer_pieces.append(got[NPOP + 1].reshape(-1)[:size].reshape(shape))
    return post0, pieces, tracer_pieces


def tracer_update(c, fx, fy, fz):
    flux_x = fx * c
    flux_y = fy[1:-1, 1:-1] * c[1:-1, 1:-1]
    flux_z = fz * c
    center = c[1:-1, 1:-1]
    div_x = (flux_x[1:-1, 2:] - flux_x[1:-1, :-2]) * 0.5
    div_y = (jnp.roll(flux_y, -1, 2) - jnp.roll(flux_y, 1, 2)) * 0.5
    div_z = (flux_z[2:, 1:-1] - flux_z[:-2, 1:-1]) * 0.5
    divergence = div_x + div_y + div_z
    beside_all = (
        (c[1:-1, 2:] + c[1:-1, :-2])
        + (jnp.roll(center, -1, 2) + jnp.roll(center, 1, 2))
        + (c[2:, 1:-1] + c[:-2, 1:-1])
    )
    laplace = beside_all - 6.0 * center
    return center - advect_gain * divergence + diffusion * laplace


def local(populations, voxel_mask, tracer):
    w = TRACER_STEPS
    post0, halos, tp = lattice_halos(populations, voxel_mask, tracer, STEPS, w)
    state, coarse = lb_call(post0, voxel_mask, halos, STEPS)
    nzt = coarse.shape[2]
    nb = lax.axis_size("blk")
    zb = nzt // nb
    ring = jnp.concatenate([coarse[:, :, nzt - w :], coarse, coarse[:, :, :zb]], axis=2)
    head = ring[:, :, : nb * zb].reshape(3, coarse.shape[1], nb, zb, coarse.shape[3])
    tail = ring[:, :, zb : zb + nb * zb].reshape(3, coarse.shape[1], nb, zb, coarse.shape[3])
    windows = jnp.concatenate([head, tail], axis=3)[:, :, :, : zb + 2 * w]
    moved = lax.all_to_all(windows, "blk", split_axis=2, concat_axis=4, tiled=True)
    flow = moved[:, :, 0]
    nxb = flow.shape[1]
    flow = jnp.concatenate([send(flow[:, nxb - w :], 1, 0), flow, send(flow[:, :w], -1, 0)], axis=1)
    flow = jnp.transpose(flow, (0, 2, 1, 3))
    xlo, xhi, zlo, zhi, c_mm, c_mp, c_pm, c_pp = tp
    conc = jnp.concatenate(
        [
            jnp.concatenate([c_mm, zlo, c_mp], axis=1),
            jnp.concatenate([xlo, tracer, xhi], axis=1),
            jnp.concatenate([c_pm, zhi, c_pp], axis=1),
        ],
        axis=0,
    )
    fx, fy, fz = flow[0], flow[1], flow[2]
    for step in range(TRACER_STEPS):
        conc = tracer_update(conc, fx, fy, fz)
        fx, fy, fz = fx[1:-1, 1:-1], fy[1:-1, 1:-1], fz[1:-1, 1:-1]
    return (state, conc)


def solution(mesh):
    placed = (P(None, "vessel", "blk", None), P("vessel", "blk", None), P("blk", "vessel", None))
    return jax.shard_map(
        local,
        mesh=mesh,
        in_specs=placed,
        out_specs=(P(None, "vessel", "blk", None), P("blk", "vessel", None)),
        check_vma=False,
    )
```

```python
import functools

import jax
import jax.numpy as jnp
import numpy as np
from jax import lax
from jax.experimental import pallas as pl
from jax.experimental.pallas import tpu as pltpu
from jax.sharding import PartitionSpec as P

STEPS = 4
TRACER_STEPS = 2


VELOCITY = np.array(
    [
        [0, 0, 0],
        [1, 0, 0],
        [-1, 0, 0],
        [0, 1, 0],
        [0, -1, 0],
        [0, 0, 1],
        [0, 0, -1],
        [1, 1, 0],
        [-1, -1, 0],
        [1, -1, 0],
        [-1, 1, 0],
        [1, 0, 1],
        [-1, 0, -1],
        [1, 0, -1],
        [-1, 0, 1],
        [0, 1, 1],
        [0, -1, -1],
        [0, 1, -1],
        [0, -1, 1],
    ]
)
WEIGHTS = np.array([1.0 / 3.0] + [1.0 / 18.0] * 6 + [1.0 / 36.0] * 12)
OPPOSITE = [0, 2, 1, 4, 3, 6, 5, 8, 7, 10, 9, 12, 11, 14, 13, 16, 15, 18, 17]
relax_rate = 1.25
pore_damping = 0.5
advect_gain = 8.0
diffusion = 0.1

NPOP = 19
CX = [int(v) for v in VELOCITY[:, 0]]
CY = [int(v) for v in VELOCITY[:, 1]]
CZ = [int(v) for v in VELOCITY[:, 2]]
CXP = [i for i in range(NPOP) if CX[i] == 1]
CXM = [i for i in range(NPOP) if CX[i] == -1]
CYP = [i for i in range(NPOP) if CY[i] == 1]
CYM = [i for i in range(NPOP) if CY[i] == -1]
SHIFTED = [i for i in range(NPOP) if CX[i] != 0 or CY[i] != 0]
ROWS = 8
YOFF = 8


def moments_chunk(g):
    w0 = jnp.float32(WEIGHTS[0])
    w1 = jnp.float32(WEIGHTS[1])
    w2 = jnp.float32(WEIGHTS[7])
    s1 = ((g[1] + g[2]) + (g[3] + g[4])) + (g[5] + g[6])
    s2 = (((g[7] + g[8]) + (g[9] + g[10])) + ((g[11] + g[12]) + (g[13] + g[14]))) + (
        (g[15] + g[16]) + (g[17] + g[18])
    )
    density = w0 * g[0] + w1 * s1 + w2 * s2
    d1, d3, d5 = g[1] - g[2], g[3] - g[4], g[5] - g[6]
    d7, d9, d11, d13 = g[7] - g[8], g[9] - g[10], g[11] - g[12], g[13] - g[14]
    d15, d17 = g[15] - g[16], g[17] - g[18]
    mx = w1 * d1 + w2 * ((d7 + d9) + (d11 + d13))
    my = w1 * d3 + w2 * ((d7 - d9) + (d15 + d17))
    mz = w1 * d5 + w2 * ((d11 - d13) + (d15 - d17))
    return density, (mx, my, mz)


PAIRS = [(1, 2), (3, 4), (5, 6), (7, 8), (9, 10), (11, 12), (13, 14), (15, 16), (17, 18)]


def collide_chunk(g, mask):
    density, (mx, my, mz) = moments_chunk(g)
    scale = jnp.where(mask == 1, jnp.float32(pore_damping), jnp.float32(1.0))
    k = (1.0 / density) * scale
    ux = mx * k
    uy = my * k
    uz = mz * k
    base = 1.0 - 1.5 * (ux * ux + uy * uy + uz * uz)
    dens = relax_rate * density
    keep = 1.0 - relax_rate
    solid = mask == 2
    proj = {
        1: ux,
        3: uy,
        5: uz,
        7: ux + uy,
        9: ux - uy,
        11: ux + uz,
        13: ux - uz,
        15: uy + uz,
        17: uy - uz,
    }
    out = [None] * NPOP
    out[0] = jnp.where(solid, g[0], dens * base + keep * g[0])
    for i, j in PAIRS:
        p = proj[i]
        q = base + 4.5 * (p * p)
        t = 3.0 * p
        relaxed_i = dens * (q + t) + keep * g[i]
        relaxed_j = dens * (q - t) + keep * g[j]
        out[i] = jnp.where(solid, g[j], relaxed_i)
        out[j] = jnp.where(solid, g[i], relaxed_j)
    return out


def lb_kernel(halo, nx, ny, *refs):
    g0, mask_ref, xlo, xhi, ylo, yhi, c_mm, c_mp, c_pm, c_pp = refs[:10]
    out_ref, coarse_ref, abuf, bbuf, flow_s = refs[10:]
    h = halo
    top = YOFF
    abuf[0:NPOP, h : h + nx, top : top + ny, :] = g0[...]
    abuf[NPOP, h : h + nx, top : top + ny, :] = mask_ref[...].astype(jnp.float32)
    planes = NPOP + 1
    abuf[:, 0:h, top : top + ny, :] = xlo[0:planes]
    abuf[:, h + nx : 2 * h + nx, top : top + ny, :] = xhi[0:planes]
    abuf[:, h : h + nx, top - h : top, :] = ylo[0:planes]
    abuf[:, h : h + nx, top + ny : top + ny + h, :] = yhi[0:planes]
    abuf[:, 0:h, top - h : top, :] = c_mm[0:planes]
    abuf[:, h + nx : 2 * h + nx, top - h : top, :] = c_mp[0:planes]
    abuf[:, 0:h, top + ny : top + ny + h, :] = c_pm[0:planes]
    abuf[:, h + nx : 2 * h + nx, top + ny : top + ny + h, :] = c_pp[0:planes]

    bufs = [abuf, bbuf]
    offs = [top] + [h - s for s in range(1, h + 1)]

    def run_step(s):
        src = bufs[(s - 1) % 2]
        dst = bufs[s % 2]
        rows = list(range(0, ny + 2 * (h - s), ROWS))
        shift = offs[s - 1] - offs[s]

        def body(x, carry):
            for r in rows:
                g = []
                for i in range(NPOP):
                    v = src[i, x - CX[i], pl.ds(r + shift - CY[i], ROWS), :]
                    if CZ[i] != 0:
                        v = pltpu.roll(v, CZ[i] % v.shape[1], 1)
                    g.append(v)
                mask = abuf[NPOP, x, pl.ds(r - offs[s] + top, ROWS), :]
                post = collide_chunk(g, mask)
                for i in range(NPOP):
                    dst[i, x, pl.ds(r, ROWS), :] = post[i]
            return carry

        lax.fori_loop(s, nx + 2 * h - s, body, 0)

    for s in range(1, h):
        run_step(s)

    src = bufs[(h - 1) % 2]
    shift = offs[h - 1] - 0

    def last_body(x, carry):
        for r in range(0, ny, ROWS):
            g = []
            for i in range(NPOP):
                v = src[i, x + h - CX[i], pl.ds(r + shift - CY[i], ROWS), :]
                if CZ[i] != 0:
                    v = pltpu.roll(v, CZ[i] % v.shape[1], 1)
                g.append(v)
                out_ref[i, x, pl.ds(r, ROWS), :] = v
            mask = abuf[NPOP, x + h, pl.ds(r + top, ROWS), :]
            density, mom = moments_chunk(g)
            inv = 1.0 / density
            solid = mask == 2
            for d in range(3):
                flow_s[d, x, pl.ds(r, ROWS), :] = jnp.where(solid, jnp.float32(0.0), mom[d] * inv)
        return carry

    lax.fori_loop(0, nx, last_body, 0)

    nz = flow_s.shape[3]
    pz = (
        lax.broadcasted_iota(jnp.int32, (nz // 2, nz), 1) // 2 == lax.broadcasted_iota(jnp.int32, (nz // 2, nz), 0)
    ).astype(jnp.float32)
    py = (
        lax.broadcasted_iota(jnp.int32, (ny, ny // 2), 0) // 2 == lax.broadcasted_iota(jnp.int32, (ny, ny // 2), 1)
    ).astype(jnp.float32)
    for d in range(3):
        for xp in range(nx // 2):
            plane = flow_s[d, 2 * xp] + flow_s[d, 2 * xp + 1]
            zy = lax.dot_general(
                pz,
                plane,
                (((1,), (1,)), ((), ())),
                precision=lax.Precision.HIGHEST,
                preferred_element_type=jnp.float32,
            )
            zc = jnp.dot(zy, py, precision=lax.Precision.HIGHEST, preferred_element_type=jnp.float32)
            coarse_ref[d, xp] = zc * jnp.float32(0.125)


def lb_call(g0, mask, halos, halo):
    _, nx, ny, nz = g0.shape
    f32 = jnp.float32
    vmem = pl.BlockSpec(memory_space=pltpu.VMEM)
    rows = YOFF + ny + 2 * halo
    rows = -(-rows // ROWS) * ROWS
    out_shape = (
        jax.ShapeDtypeStruct(g0.shape, f32),
        jax.ShapeDtypeStruct((3, nx // 2, nz // 2, ny // 2), f32),
    )
    scratch = [
        pltpu.VMEM((NPOP + 1, nx + 2 * halo, rows, nz), f32),
        pltpu.VMEM((NPOP, nx + 2 * halo, rows, nz), f32),
        pltpu.VMEM((3, nx, ny, nz), f32),
    ]
    cells = (nx + halo) * (ny + 2 * halo) * nz * halo
    cost = pl.CostEstimate(flops=320 * cells, transcendentals=0, bytes_accessed=2 * NPOP * 4 * nx * ny * nz * 2)
    return pl.pallas_call(
        functools.partial(lb_kernel, halo, nx, ny),
        out_shape=out_shape,
        in_specs=[vmem] * (2 + len(halos)),
        out_specs=(vmem, vmem),
        scratch_shapes=scratch,
        cost_estimate=cost,
        compiler_params=pltpu.CompilerParams(vmem_limit_bytes=60 * 1024 * 1024),
    )(g0, mask, *halos)


def send(x, dv, db):
    nv = lax.axis_size("vessel")
    nb = lax.axis_size("blk")
    if db == 0:
        return lax.ppermute(x, "vessel", [(i, (i + dv) % nv) for i in range(nv)])
    if dv == 0:
        return lax.ppermute(x, "blk", [(i, (i + db) % nb) for i in range(nb)])
    pairs = []
    for v in range(nv):
        for b in range(nb):
            pairs.append((v * nb + b, ((v + dv) % nv) * nb + (b + db) % nb))
    return lax.ppermute(x, ("vessel", "blk"), pairs)


ORDER = ((1, 0), (-1, 0), (0, 1), (0, -1), (1, 1), (-1, 1), (1, -1), (-1, -1))


def edge(n, h, d):
    return {1: slice(n - h, n), -1: slice(0, h), 0: slice(0, n)}[d]


def first_kernel(h, nx, ny, *refs):
    g0, mask_ref = refs[:2]
    tplanes = refs[2:10]
    post_ref = refs[10]
    msgs = refs[11:19]

    def body(x, carry):
        for r in range(0, ny, ROWS):
            g = [g0[i, x, pl.ds(r, ROWS), :] for i in range(NPOP)]
            post = collide_chunk(g, mask_ref[x, pl.ds(r, ROWS), :])
            for i in range(NPOP):
                post_ref[i, x, pl.ds(r, ROWS), :] = post[i]
        return carry

    lax.fori_loop(0, nx, body, 0)
    for k, (dv, db) in enumerate(ORDER):
        xs, ys = edge(nx, h, dv), edge(ny, h, db)
        msgs[k][0:NPOP] = post_ref[:, xs, ys, :]
        msgs[k][NPOP] = mask_ref[xs, ys, :].astype(jnp.float32)
        msgs[k][NPOP + 1] = tplanes[k][...]


def lattice_halos(g0, mask, conc, h, w):
    _, nx, ny, nz = g0.shape
    nzc, nxc, _ = conc.shape
    f32 = jnp.float32
    tplanes, tshapes = [], []
    for dv, db in ORDER:
        a, b = (h if dv else nx), (h if db else ny)
        tp = conc[edge(nzc, w, db), edge(nxc, w, dv)]
        tshapes.append(tp.shape)
        tplanes.append(jnp.pad(tp.reshape(-1), (0, a * b * nz - tp.size)).reshape(a, b, nz))
    vmem = pl.BlockSpec(memory_space=pltpu.VMEM)
    out_shape = (jax.ShapeDtypeStruct(g0.shape, f32),) + tuple(
        jax.ShapeDtypeStruct((NPOP + 2,) + t.shape, f32) for t in tplanes
    )
    cells = nx * ny * nz
    outs = pl.pallas_call(
        functools.partial(first_kernel, h, nx, ny),
        out_shape=out_shape,
        in_specs=[vmem] * 10,
        out_specs=tuple(vmem for _ in out_shape),
        cost_estimate=pl.CostEstimate(flops=200 * cells, transcendentals=0, bytes_accessed=NPOP * 4 * cells * 3),
        compiler_params=pltpu.CompilerParams(vmem_limit_bytes=48 * 1024 * 1024),
    )(g0, mask, *tplanes)
    post0, msgs = outs[0], outs[1:]
    pieces, tracer_pieces = [], []
    faces = [send(msg, dv, db) for (dv, db), msg in zip(ORDER[:4], msgs[:4])]
    corner_msgs = lax.optimization_barrier((tuple(msgs[4:]), faces[0], faces[1]))[0]
    corners = [send(msg, dv, db) for (dv, db), msg in zip(ORDER[4:], corner_msgs)]
    for got, shape in zip(faces + corners, tshapes):
        pieces.append(got)
        size = int(np.prod(shape))
        tracer_pieces.append(got[NPOP + 1].reshape(-1)[:size].reshape(shape))
    return post0, pieces, tracer_pieces


def tracer_update(c, fx, fy, fz):
    flux_x = fx * c
    flux_y = fy[1:-1, 1:-1] * c[1:-1, 1:-1]
    flux_z = fz * c
    center = c[1:-1, 1:-1]
    div_x = (flux_x[1:-1, 2:] - flux_x[1:-1, :-2]) * 0.5
    div_y = (jnp.roll(flux_y, -1, 2) - jnp.roll(flux_y, 1, 2)) * 0.5
    div_z = (flux_z[2:, 1:-1] - flux_z[:-2, 1:-1]) * 0.5
    divergence = div_x + div_y + div_z
    beside_all = (
        (c[1:-1, 2:] + c[1:-1, :-2])
        + (jnp.roll(center, -1, 2) + jnp.roll(center, 1, 2))
        + (c[2:, 1:-1] + c[:-2, 1:-1])
    )
    laplace = beside_all - 6.0 * center
    return center - advect_gain * divergence + diffusion * laplace


def local(populations, voxel_mask, tracer):
    w = TRACER_STEPS
    post0, halos, tp = lattice_halos(populations, voxel_mask, tracer, STEPS, w)
    state, coarse = lb_call(post0, voxel_mask, halos, STEPS)
    nzt = coarse.shape[2]
    nb = lax.axis_size("blk")
    zb = nzt // nb
    ring = jnp.concatenate([coarse[:, :, nzt - w :], coarse, coarse[:, :, :zb]], axis=2)
    head = ring[:, :, : nb * zb].reshape(3, coarse.shape[1], nb, zb, coarse.shape[3])
    tail = ring[:, :, zb : zb + nb * zb].reshape(3, coarse.shape[1], nb, zb, coarse.shape[3])
    windows = jnp.concatenate([head, tail], axis=3)[:, :, :, : zb + 2 * w]
    moved = lax.all_to_all(windows, "blk", split_axis=2, concat_axis=4, tiled=True)
    flow = moved[:, :, 0]
    nxb = flow.shape[1]
    flow = jnp.concatenate([send(flow[:, nxb - w :], 1, 0), flow, send(flow[:, :w], -1, 0)], axis=1)
    flow = jnp.transpose(flow, (0, 2, 1, 3))
    xlo, xhi, zlo, zhi, c_mm, c_mp, c_pm, c_pp = tp
    conc = jnp.concatenate(
        [
            jnp.concatenate([c_mm, zlo, c_mp], axis=1),
            jnp.concatenate([xlo, tracer, xhi], axis=1),
            jnp.concatenate([c_pm, zhi, c_pp], axis=1),
        ],
        axis=0,
    )
    fx, fy, fz = flow[0], flow[1], flow[2]
    for step in range(TRACER_STEPS):
        conc = tracer_update(conc, fx, fy, fz)
        fx, fy, fz = fx[1:-1, 1:-1], fy[1:-1, 1:-1], fz[1:-1, 1:-1]
    return (state, conc)


def solution(mesh):
    placed = (P(None, "vessel", "blk", None), P("vessel", "blk", None), P("blk", "vessel", None))
    return jax.shard_map(
        local,
        mesh=mesh,
        in_specs=placed,
        out_specs=(P(None, "vessel", "blk", None), P("blk", "vessel", None)),
        check_vma=False,
    )
```

```python
import functools

import jax
import jax.numpy as jnp
import numpy as np
from jax import lax
from jax.experimental import pallas as pl
from jax.experimental.pallas import tpu as pltpu
from jax.sharding import PartitionSpec as P

STEPS = 4
TRACER_STEPS = 2


VELOCITY = np.array(
    [
        [0, 0, 0],
        [1, 0, 0],
        [-1, 0, 0],
        [0, 1, 0],
        [0, -1, 0],
        [0, 0, 1],
        [0, 0, -1],
        [1, 1, 0],
        [-1, -1, 0],
        [1, -1, 0],
        [-1, 1, 0],
        [1, 0, 1],
        [-1, 0, -1],
        [1, 0, -1],
        [-1, 0, 1],
        [0, 1, 1],
        [0, -1, -1],
        [0, 1, -1],
        [0, -1, 1],
    ]
)
WEIGHTS = np.array([1.0 / 3.0] + [1.0 / 18.0] * 6 + [1.0 / 36.0] * 12)
OPPOSITE = [0, 2, 1, 4, 3, 6, 5, 8, 7, 10, 9, 12, 11, 14, 13, 16, 15, 18, 17]
relax_rate = 1.25
pore_damping = 0.5
advect_gain = 8.0
diffusion = 0.1

NPOP = 19
CX = [int(v) for v in VELOCITY[:, 0]]
CY = [int(v) for v in VELOCITY[:, 1]]
CZ = [int(v) for v in VELOCITY[:, 2]]
CXP = [i for i in range(NPOP) if CX[i] == 1]
CXM = [i for i in range(NPOP) if CX[i] == -1]
CYP = [i for i in range(NPOP) if CY[i] == 1]
CYM = [i for i in range(NPOP) if CY[i] == -1]
SHIFTED = [i for i in range(NPOP) if CX[i] != 0 or CY[i] != 0]
ROWS = 8
YOFF = 8


def moments_chunk(g):
    w0 = jnp.float32(WEIGHTS[0])
    w1 = jnp.float32(WEIGHTS[1])
    w2 = jnp.float32(WEIGHTS[7])
    s1 = ((g[1] + g[2]) + (g[3] + g[4])) + (g[5] + g[6])
    s2 = (((g[7] + g[8]) + (g[9] + g[10])) + ((g[11] + g[12]) + (g[13] + g[14]))) + (
        (g[15] + g[16]) + (g[17] + g[18])
    )
    density = w0 * g[0] + w1 * s1 + w2 * s2
    d1, d3, d5 = g[1] - g[2], g[3] - g[4], g[5] - g[6]
    d7, d9, d11, d13 = g[7] - g[8], g[9] - g[10], g[11] - g[12], g[13] - g[14]
    d15, d17 = g[15] - g[16], g[17] - g[18]
    mx = w1 * d1 + w2 * ((d7 + d9) + (d11 + d13))
    my = w1 * d3 + w2 * ((d7 - d9) + (d15 + d17))
    mz = w1 * d5 + w2 * ((d11 - d13) + (d15 - d17))
    return density, (mx, my, mz)


PAIRS = [(1, 2), (3, 4), (5, 6), (7, 8), (9, 10), (11, 12), (13, 14), (15, 16), (17, 18)]


def collide_chunk(g, mask):
    density, (mx, my, mz) = moments_chunk(g)
    scale = jnp.where(mask == 1, jnp.float32(pore_damping), jnp.float32(1.0))
    k = (1.0 / density) * scale
    ux = mx * k
    uy = my * k
    uz = mz * k
    base = 1.0 - 1.5 * (ux * ux + uy * uy + uz * uz)
    dens = relax_rate * density
    keep = 1.0 - relax_rate
    solid = mask == 2
    proj = {
        1: ux,
        3: uy,
        5: uz,
        7: ux + uy,
        9: ux - uy,
        11: ux + uz,
        13: ux - uz,
        15: uy + uz,
        17: uy - uz,
    }
    out = [None] * NPOP
    out[0] = jnp.where(solid, g[0], dens * base + keep * g[0])
    for i, j in PAIRS:
        p = proj[i]
        q = base + 4.5 * (p * p)
        t = 3.0 * p
        relaxed_i = dens * (q + t) + keep * g[i]
        relaxed_j = dens * (q - t) + keep * g[j]
        out[i] = jnp.where(solid, g[j], relaxed_i)
        out[j] = jnp.where(solid, g[i], relaxed_j)
    return out


def lb_kernel(halo, nx, ny, *refs):
    g0, mask_ref, xlo, xhi, ylo, yhi, c_mm, c_mp, c_pm, c_pp = refs[:10]
    out_ref, coarse_ref = refs[10:12]
    tplanes = refs[12:20]
    abuf, bbuf, flow_s = refs[20:]
    for t_ref, m_ref in zip(tplanes, (xlo, xhi, ylo, yhi, c_mm, c_mp, c_pm, c_pp)):
        t_ref[...] = m_ref[NPOP + 1]
    h = halo
    top = YOFF
    abuf[0:NPOP, h : h + nx, top : top + ny, :] = g0[...]
    abuf[NPOP, h : h + nx, top : top + ny, :] = mask_ref[...].astype(jnp.float32)
    planes = NPOP + 1
    abuf[:, 0:h, top : top + ny, :] = xlo[0:planes]
    abuf[:, h + nx : 2 * h + nx, top : top + ny, :] = xhi[0:planes]
    abuf[:, h : h + nx, top - h : top, :] = ylo[0:planes]
    abuf[:, h : h + nx, top + ny : top + ny + h, :] = yhi[0:planes]
    abuf[:, 0:h, top - h : top, :] = c_mm[0:planes]
    abuf[:, h + nx : 2 * h + nx, top - h : top, :] = c_mp[0:planes]
    abuf[:, 0:h, top + ny : top + ny + h, :] = c_pm[0:planes]
    abuf[:, h + nx : 2 * h + nx, top + ny : top + ny + h, :] = c_pp[0:planes]

    bufs = [bbuf, abuf]
    offs = [top] + [h - s for s in range(1, h + 1)]

    def run_step(s):
        src = abuf if s == 0 else bufs[(s - 1) % 2]
        dst = bufs[s % 2]
        if s == 0:
            rows = list(range(0, top + ny + h, ROWS))
        else:
            rows = list(range(0, ny + 2 * (h - s), ROWS))
        shift = offs[s - 1] - offs[s] if s > 0 else 0

        def body(x, carry):
            for r in rows:
                g = []
                for i in range(NPOP):
                    if s == 0:
                        v = src[i, x, pl.ds(r, ROWS), :]
                    else:
                        v = src[i, x - CX[i], pl.ds(r + shift - CY[i], ROWS), :]
                        if CZ[i] != 0:
                            v = pltpu.roll(v, CZ[i] % v.shape[1], 1)
                    g.append(v)
                mask = abuf[NPOP, x, pl.ds(r - offs[s] + top, ROWS), :]
                post = collide_chunk(g, mask)
                for i in range(NPOP):
                    dst[i, x, pl.ds(r, ROWS), :] = post[i]
            return carry

        lax.fori_loop(s, nx + 2 * h - s, body, 0)

    for s in range(h):
        run_step(s)

    src = bufs[(h - 1) % 2]
    shift = offs[h - 1] - 0

    def last_body(x, carry):
        for r in range(0, ny, ROWS):
            g = []
            for i in range(NPOP):
                v = src[i, x + h - CX[i], pl.ds(r + shift - CY[i], ROWS), :]
                if CZ[i] != 0:
                    v = pltpu.roll(v, CZ[i] % v.shape[1], 1)
                g.append(v)
                out_ref[i, x, pl.ds(r, ROWS), :] = v
            mask = abuf[NPOP, x + h, pl.ds(r + top, ROWS), :]
            density, mom = moments_chunk(g)
            inv = 1.0 / density
            solid = mask == 2
            for d in range(3):
                flow_s[d, x, pl.ds(r, ROWS), :] = jnp.where(solid, jnp.float32(0.0), mom[d] * inv)
        return carry

    lax.fori_loop(0, nx, last_body, 0)

    nz = flow_s.shape[3]
    pz = (
        lax.broadcasted_iota(jnp.int32, (nz // 2, nz), 1) // 2 == lax.broadcasted_iota(jnp.int32, (nz // 2, nz), 0)
    ).astype(jnp.float32)
    py = (
        lax.broadcasted_iota(jnp.int32, (ny, ny // 2), 0) // 2 == lax.broadcasted_iota(jnp.int32, (ny, ny // 2), 1)
    ).astype(jnp.float32)
    for d in range(3):
        for xp in range(nx // 2):
            plane = flow_s[d, 2 * xp] + flow_s[d, 2 * xp + 1]
            zy = lax.dot_general(
                pz,
                plane,
                (((1,), (1,)), ((), ())),
                precision=lax.Precision.HIGHEST,
                preferred_element_type=jnp.float32,
            )
            zc = jnp.dot(zy, py, precision=lax.Precision.HIGHEST, preferred_element_type=jnp.float32)
            coarse_ref[d, xp] = zc * jnp.float32(0.125)


def lb_call(g0, mask, halos, halo):
    _, nx, ny, nz = g0.shape
    f32 = jnp.float32
    vmem = pl.BlockSpec(memory_space=pltpu.VMEM)
    rows = YOFF + ny + 2 * halo
    rows = -(-rows // ROWS) * ROWS
    out_shape = (
        jax.ShapeDtypeStruct(g0.shape, f32),
        jax.ShapeDtypeStruct((3, nx // 2, nz // 2, ny // 2), f32),
    ) + tuple(jax.ShapeDtypeStruct(m.shape[1:], f32) for m in halos)
    scratch = [
        pltpu.VMEM((NPOP + 1, nx + 2 * halo, rows, nz), f32),
        pltpu.VMEM((NPOP, nx + 2 * halo, rows, nz), f32),
        pltpu.VMEM((3, nx, ny, nz), f32),
    ]
    cells = (nx + halo) * (ny + 2 * halo) * nz * halo
    cost = pl.CostEstimate(flops=320 * cells, transcendentals=0, bytes_accessed=2 * NPOP * 4 * nx * ny * nz * 2)
    return pl.pallas_call(
        functools.partial(lb_kernel, halo, nx, ny),
        out_shape=out_shape,
        in_specs=[vmem] * (2 + len(halos)),
        out_specs=tuple(vmem for _ in out_shape),
        scratch_shapes=scratch,
        cost_estimate=cost,
        compiler_params=pltpu.CompilerParams(vmem_limit_bytes=60 * 1024 * 1024),
    )(g0, mask, *halos)


def send(x, dv, db):
    nv = lax.axis_size("vessel")
    nb = lax.axis_size("blk")
    if db == 0:
        return lax.ppermute(x, "vessel", [(i, (i + dv) % nv) for i in range(nv)])
    if dv == 0:
        return lax.ppermute(x, "blk", [(i, (i + db) % nb) for i in range(nb)])
    pairs = []
    for v in range(nv):
        for b in range(nb):
            pairs.append((v * nb + b, ((v + dv) % nv) * nb + (b + db) % nb))
    return lax.ppermute(x, ("vessel", "blk"), pairs)


def lattice_halos(g0, mask, conc, h, w):
    _, nx, ny, nz = g0.shape
    nzc, nxc, nyc = conc.shape
    maskf = mask.astype(jnp.float32)[None]
    lat = {1: slice(nx - h, nx), -1: slice(0, h), 0: slice(0, nx)}
    lat_y = {1: slice(ny - h, ny), -1: slice(0, h), 0: slice(0, ny)}
    trc_x = {1: slice(nxc - w, nxc), -1: slice(0, w), 0: slice(0, nxc)}
    trc_z = {1: slice(nzc - w, nzc), -1: slice(0, w), 0: slice(0, nzc)}
    order = ((1, 0), (-1, 0), (0, 1), (0, -1), (1, 1), (-1, 1), (1, -1), (-1, -1))
    pieces, shapes = [], []
    for dv, db in order:
        xs, ys = lat[dv], lat_y[db]
        lb = jnp.concatenate([g0[:, xs, ys], maskf[:, xs, ys]], axis=0)
        tp = conc[trc_z[db], trc_x[dv]]
        plane = lb.shape[1] * lb.shape[2] * nz
        flat = jnp.pad(tp.reshape(-1), (0, plane - tp.size))
        msg = jnp.concatenate([lb, flat.reshape(1, lb.shape[1], lb.shape[2], nz)], axis=0)
        pieces.append(send(msg, dv, db))
        shapes.append(tp.shape)
    return pieces, shapes


def tracer_update(c, fx, fy, fz):
    flux_x = fx * c
    flux_y = fy[1:-1, 1:-1] * c[1:-1, 1:-1]
    flux_z = fz * c
    center = c[1:-1, 1:-1]
    div_x = (flux_x[1:-1, 2:] - flux_x[1:-1, :-2]) * 0.5
    div_y = (jnp.roll(flux_y, -1, 2) - jnp.roll(flux_y, 1, 2)) * 0.5
    div_z = (flux_z[2:, 1:-1] - flux_z[:-2, 1:-1]) * 0.5
    divergence = div_x + div_y + div_z
    beside_all = (
        (c[1:-1, 2:] + c[1:-1, :-2])
        + (jnp.roll(center, -1, 2) + jnp.roll(center, 1, 2))
        + (c[2:, 1:-1] + c[:-2, 1:-1])
    )
    laplace = beside_all - 6.0 * center
    return center - advect_gain * divergence + diffusion * laplace


def local(populations, voxel_mask, tracer):
    w = TRACER_STEPS
    halos, shapes = lattice_halos(populations, voxel_mask, tracer, STEPS, w)
    state, coarse, *planes = lb_call(populations, voxel_mask, halos, STEPS)
    tp = [p.reshape(-1)[: int(np.prod(s))].reshape(s) for p, s in zip(planes, shapes)]
    nzt = coarse.shape[2]
    nb = lax.axis_size("blk")
    zb = nzt // nb
    ring = jnp.concatenate([coarse[:, :, nzt - w :], coarse, coarse[:, :, :zb]], axis=2)
    head = ring[:, :, : nb * zb].reshape(3, coarse.shape[1], nb, zb, coarse.shape[3])
    tail = ring[:, :, zb : zb + nb * zb].reshape(3, coarse.shape[1], nb, zb, coarse.shape[3])
    windows = jnp.concatenate([head, tail], axis=3)[:, :, :, : zb + 2 * w]
    moved = lax.all_to_all(windows, "blk", split_axis=2, concat_axis=4, tiled=True)
    flow = moved[:, :, 0]
    nxb = flow.shape[1]
    flow = jnp.concatenate([send(flow[:, nxb - w :], 1, 0), flow, send(flow[:, :w], -1, 0)], axis=1)
    flow = jnp.transpose(flow, (0, 2, 1, 3))
    xlo, xhi, zlo, zhi, c_mm, c_mp, c_pm, c_pp = tp
    conc = jnp.concatenate(
        [
            jnp.concatenate([c_mm, zlo, c_mp], axis=1),
            jnp.concatenate([xlo, tracer, xhi], axis=1),
            jnp.concatenate([c_pm, zhi, c_pp], axis=1),
        ],
        axis=0,
    )
    fx, fy, fz = flow[0], flow[1], flow[2]
    for step in range(TRACER_STEPS):
        conc = tracer_update(conc, fx, fy, fz)
        fx, fy, fz = fx[1:-1, 1:-1], fy[1:-1, 1:-1], fz[1:-1, 1:-1]
    return (state, conc)


def solution(mesh):
    placed = (P(None, "vessel", "blk", None), P("vessel", "blk", None), P("blk", "vessel", None))
    return jax.shard_map(
        local,
        mesh=mesh,
        in_specs=placed,
        out_specs=(P(None, "vessel", "blk", None), P("blk", "vessel", None)),
        check_vma=False,
    )
```

```python
import functools

import jax
import jax.numpy as jnp
import numpy as np
from jax import lax
from jax.experimental import pallas as pl
from jax.experimental.pallas import tpu as pltpu
from jax.sharding import PartitionSpec as P

STEPS = 4
TRACER_STEPS = 2


VELOCITY = np.array(
    [
        [0, 0, 0],
        [1, 0, 0],
        [-1, 0, 0],
        [0, 1, 0],
        [0, -1, 0],
        [0, 0, 1],
        [0, 0, -1],
        [1, 1, 0],
        [-1, -1, 0],
        [1, -1, 0],
        [-1, 1, 0],
        [1, 0, 1],
        [-1, 0, -1],
        [1, 0, -1],
        [-1, 0, 1],
        [0, 1, 1],
        [0, -1, -1],
        [0, 1, -1],
        [0, -1, 1],
    ]
)
WEIGHTS = np.array([1.0 / 3.0] + [1.0 / 18.0] * 6 + [1.0 / 36.0] * 12)
OPPOSITE = [0, 2, 1, 4, 3, 6, 5, 8, 7, 10, 9, 12, 11, 14, 13, 16, 15, 18, 17]
relax_rate = 1.25
pore_damping = 0.5
advect_gain = 8.0
diffusion = 0.1

NPOP = 19
CX = [int(v) for v in VELOCITY[:, 0]]
CY = [int(v) for v in VELOCITY[:, 1]]
CZ = [int(v) for v in VELOCITY[:, 2]]
CXP = [i for i in range(NPOP) if CX[i] == 1]
CXM = [i for i in range(NPOP) if CX[i] == -1]
CYP = [i for i in range(NPOP) if CY[i] == 1]
CYM = [i for i in range(NPOP) if CY[i] == -1]
SHIFTED = [i for i in range(NPOP) if CX[i] != 0 or CY[i] != 0]
ROWS = 8
YOFF = 8


def moments_chunk(g):
    w0 = jnp.float32(WEIGHTS[0])
    w1 = jnp.float32(WEIGHTS[1])
    w2 = jnp.float32(WEIGHTS[7])
    s1 = ((g[1] + g[2]) + (g[3] + g[4])) + (g[5] + g[6])
    s2 = (((g[7] + g[8]) + (g[9] + g[10])) + ((g[11] + g[12]) + (g[13] + g[14]))) + (
        (g[15] + g[16]) + (g[17] + g[18])
    )
    density = w0 * g[0] + w1 * s1 + w2 * s2
    d1, d3, d5 = g[1] - g[2], g[3] - g[4], g[5] - g[6]
    d7, d9, d11, d13 = g[7] - g[8], g[9] - g[10], g[11] - g[12], g[13] - g[14]
    d15, d17 = g[15] - g[16], g[17] - g[18]
    mx = w1 * d1 + w2 * ((d7 + d9) + (d11 + d13))
    my = w1 * d3 + w2 * ((d7 - d9) + (d15 + d17))
    mz = w1 * d5 + w2 * ((d11 - d13) + (d15 - d17))
    return density, (mx, my, mz)


PAIRS = [(1, 2), (3, 4), (5, 6), (7, 8), (9, 10), (11, 12), (13, 14), (15, 16), (17, 18)]


def collide_chunk(g, mask):
    density, (mx, my, mz) = moments_chunk(g)
    scale = jnp.where(mask == 1, jnp.float32(pore_damping), jnp.float32(1.0))
    k = (1.0 / density) * scale
    ux = mx * k
    uy = my * k
    uz = mz * k
    base = 1.0 - 1.5 * (ux * ux + uy * uy + uz * uz)
    dens = relax_rate * density
    keep = 1.0 - relax_rate
    solid = mask == 2
    proj = {
        1: ux,
        3: uy,
        5: uz,
        7: ux + uy,
        9: ux - uy,
        11: ux + uz,
        13: ux - uz,
        15: uy + uz,
        17: uy - uz,
    }
    out = [None] * NPOP
    out[0] = jnp.where(solid, g[0], dens * base + keep * g[0])
    for i, j in PAIRS:
        p = proj[i]
        q = base + 4.5 * (p * p)
        t = 3.0 * p
        relaxed_i = dens * (q + t) + keep * g[i]
        relaxed_j = dens * (q - t) + keep * g[j]
        out[i] = jnp.where(solid, g[j], relaxed_i)
        out[j] = jnp.where(solid, g[i], relaxed_j)
    return out


def lb_kernel(halo, nx, ny, *refs):
    g0, mask_ref, xlo, xhi, ylo, yhi, c_mm, c_mp, c_pm, c_pp = refs[:10]
    out_ref, coarse_ref, abuf, bbuf, flow_s = refs[10:]
    h = halo
    top = YOFF
    abuf[0:NPOP, h : h + nx, top : top + ny, :] = g0[...]
    abuf[NPOP, h : h + nx, top : top + ny, :] = mask_ref[...].astype(jnp.float32)
    planes = NPOP + 1
    abuf[:, 0:h, top : top + ny, :] = xlo[0:planes]
    abuf[:, h + nx : 2 * h + nx, top : top + ny, :] = xhi[0:planes]
    abuf[:, h : h + nx, top - h : top, :] = ylo[0:planes]
    abuf[:, h : h + nx, top + ny : top + ny + h, :] = yhi[0:planes]
    abuf[:, 0:h, top - h : top, :] = c_mm[0:planes]
    abuf[:, h + nx : 2 * h + nx, top - h : top, :] = c_mp[0:planes]
    abuf[:, 0:h, top + ny : top + ny + h, :] = c_pm[0:planes]
    abuf[:, h + nx : 2 * h + nx, top + ny : top + ny + h, :] = c_pp[0:planes]

    bufs = [bbuf, abuf]
    offs = [top] + [h - s for s in range(1, h + 1)]

    def run_step(s):
        src = abuf if s == 0 else bufs[(s - 1) % 2]
        dst = bufs[s % 2]
        if s == 0:
            rows = list(range(0, top + ny + h, ROWS))
        else:
            rows = list(range(0, ny + 2 * (h - s), ROWS))
        shift = offs[s - 1] - offs[s] if s > 0 else 0

        def body(x, carry):
            for r in rows:
                g = []
                for i in range(NPOP):
                    if s == 0:
                        v = src[i, x, pl.ds(r, ROWS), :]
                    else:
                        v = src[i, x - CX[i], pl.ds(r + shift - CY[i], ROWS), :]
                        if CZ[i] != 0:
                            v = pltpu.roll(v, CZ[i] % v.shape[1], 1)
                    g.append(v)
                mask = abuf[NPOP, x, pl.ds(r - offs[s] + top, ROWS), :]
                post = collide_chunk(g, mask)
                for i in range(NPOP):
                    dst[i, x, pl.ds(r, ROWS), :] = post[i]
            return carry

        lax.fori_loop(s, nx + 2 * h - s, body, 0)

    for s in range(h):
        run_step(s)

    src = bufs[(h - 1) % 2]
    shift = offs[h - 1] - 0

    def last_body(x, carry):
        for r in range(0, ny, ROWS):
            g = []
            for i in range(NPOP):
                v = src[i, x + h - CX[i], pl.ds(r + shift - CY[i], ROWS), :]
                if CZ[i] != 0:
                    v = pltpu.roll(v, CZ[i] % v.shape[1], 1)
                g.append(v)
                out_ref[i, x, pl.ds(r, ROWS), :] = v
            mask = abuf[NPOP, x + h, pl.ds(r + top, ROWS), :]
            density, mom = moments_chunk(g)
            inv = 1.0 / density
            solid = mask == 2
            for d in range(3):
                flow_s[d, x, pl.ds(r, ROWS), :] = jnp.where(solid, jnp.float32(0.0), mom[d] * inv)
        return carry

    lax.fori_loop(0, nx, last_body, 0)

    nz = flow_s.shape[3]
    pz = (
        lax.broadcasted_iota(jnp.int32, (nz // 2, nz), 1) // 2 == lax.broadcasted_iota(jnp.int32, (nz // 2, nz), 0)
    ).astype(jnp.float32)
    py = (
        lax.broadcasted_iota(jnp.int32, (ny, ny // 2), 0) // 2 == lax.broadcasted_iota(jnp.int32, (ny, ny // 2), 1)
    ).astype(jnp.float32)
    for d in range(3):
        for xp in range(nx // 2):
            plane = flow_s[d, 2 * xp] + flow_s[d, 2 * xp + 1]
            zy = lax.dot_general(
                pz,
                plane,
                (((1,), (1,)), ((), ())),
                precision=lax.Precision.HIGHEST,
                preferred_element_type=jnp.float32,
            )
            zc = jnp.dot(zy, py, precision=lax.Precision.HIGHEST, preferred_element_type=jnp.float32)
            coarse_ref[d, xp] = zc * jnp.float32(0.125)


def lb_call(g0, mask, halos, halo):
    _, nx, ny, nz = g0.shape
    f32 = jnp.float32
    vmem = pl.BlockSpec(memory_space=pltpu.VMEM)
    rows = YOFF + ny + 2 * halo
    rows = -(-rows // ROWS) * ROWS
    out_shape = (
        jax.ShapeDtypeStruct(g0.shape, f32),
        jax.ShapeDtypeStruct((3, nx // 2, nz // 2, ny // 2), f32),
    )
    scratch = [
        pltpu.VMEM((NPOP + 1, nx + 2 * halo, rows, nz), f32),
        pltpu.VMEM((NPOP, nx + 2 * halo, rows, nz), f32),
        pltpu.VMEM((3, nx, ny, nz), f32),
    ]
    cells = (nx + halo) * (ny + 2 * halo) * nz * halo
    cost = pl.CostEstimate(flops=320 * cells, transcendentals=0, bytes_accessed=2 * NPOP * 4 * nx * ny * nz * 2)
    return pl.pallas_call(
        functools.partial(lb_kernel, halo, nx, ny),
        out_shape=out_shape,
        in_specs=[vmem] * (2 + len(halos)),
        out_specs=(vmem, vmem),
        scratch_shapes=scratch,
        cost_estimate=cost,
        compiler_params=pltpu.CompilerParams(vmem_limit_bytes=60 * 1024 * 1024),
    )(g0, mask, *halos)


def send(x, dv, db):
    nv = lax.axis_size("vessel")
    nb = lax.axis_size("blk")
    if db == 0:
        return lax.ppermute(x, "vessel", [(i, (i + dv) % nv) for i in range(nv)])
    if dv == 0:
        return lax.ppermute(x, "blk", [(i, (i + db) % nb) for i in range(nb)])
    pairs = []
    for v in range(nv):
        for b in range(nb):
            pairs.append((v * nb + b, ((v + dv) % nv) * nb + (b + db) % nb))
    return lax.ppermute(x, ("vessel", "blk"), pairs)


def lattice_halos(g0, mask, conc, h, w):
    _, nx, ny, nz = g0.shape
    nzc, nxc, nyc = conc.shape
    lat = {1: slice(nx - h, nx), -1: slice(0, h), 0: slice(0, nx)}
    lat_y = {1: slice(ny - h, ny), -1: slice(0, h), 0: slice(0, ny)}
    trc_x = {1: slice(nxc - w, nxc), -1: slice(0, w), 0: slice(0, nxc)}
    trc_z = {1: slice(nzc - w, nzc), -1: slice(0, w), 0: slice(0, nzc)}
    order = ((1, 0), (-1, 0), (0, 1), (0, -1), (1, 1), (-1, 1), (1, -1), (-1, -1))
    pieces, tracer_pieces = [], []
    for dv, db in order:
        xs, ys = lat[dv], lat_y[db]
        lb = jnp.concatenate([g0[:, xs, ys], mask[None, xs, ys].astype(jnp.float32)], axis=0)
        tp = conc[trc_z[db], trc_x[dv]]
        plane = lb.shape[1] * lb.shape[2] * nz
        flat = jnp.pad(tp.reshape(-1), (0, plane - tp.size))
        msg = jnp.concatenate([lb, flat.reshape(1, lb.shape[1], lb.shape[2], nz)], axis=0)
        got = send(msg, dv, db)
        pieces.append(got)
        tracer_pieces.append(got[NPOP + 1].reshape(-1)[: tp.size].reshape(tp.shape))
    return pieces, tracer_pieces


def tracer_update(c, fx, fy, fz):
    flux_x = fx * c
    flux_y = fy[1:-1, 1:-1] * c[1:-1, 1:-1]
    flux_z = fz * c
    center = c[1:-1, 1:-1]
    div_x = (flux_x[1:-1, 2:] - flux_x[1:-1, :-2]) * 0.5
    div_y = (jnp.roll(flux_y, -1, 2) - jnp.roll(flux_y, 1, 2)) * 0.5
    div_z = (flux_z[2:, 1:-1] - flux_z[:-2, 1:-1]) * 0.5
    divergence = div_x + div_y + div_z
    beside_all = (
        (c[1:-1, 2:] + c[1:-1, :-2])
        + (jnp.roll(center, -1, 2) + jnp.roll(center, 1, 2))
        + (c[2:, 1:-1] + c[:-2, 1:-1])
    )
    laplace = beside_all - 6.0 * center
    return center - advect_gain * divergence + diffusion * laplace


def local(populations, voxel_mask, tracer):
    w = TRACER_STEPS
    halos, tp = lattice_halos(populations, voxel_mask, tracer, STEPS, w)
    state, coarse = lb_call(populations, voxel_mask, halos, STEPS)
    nzt = coarse.shape[2]
    nb = lax.axis_size("blk")
    zb = nzt // nb
    ring = jnp.concatenate([coarse[:, :, nzt - w :], coarse, coarse[:, :, :zb]], axis=2)
    head = ring[:, :, : nb * zb].reshape(3, coarse.shape[1], nb, zb, coarse.shape[3])
    tail = ring[:, :, zb : zb + nb * zb].reshape(3, coarse.shape[1], nb, zb, coarse.shape[3])
    windows = jnp.concatenate([head, tail], axis=3)[:, :, :, : zb + 2 * w]
    moved = lax.all_to_all(windows, "blk", split_axis=2, concat_axis=4, tiled=True)
    flow = moved[:, :, 0]
    nxb = flow.shape[1]
    flow = jnp.concatenate([send(flow[:, nxb - w :], 1, 0), flow, send(flow[:, :w], -1, 0)], axis=1)
    flow = jnp.transpose(flow, (0, 2, 1, 3))
    xlo, xhi, zlo, zhi, c_mm, c_mp, c_pm, c_pp = tp
    conc = jnp.concatenate(
        [
            jnp.concatenate([c_mm, zlo, c_mp], axis=1),
            jnp.concatenate([xlo, tracer, xhi], axis=1),
            jnp.concatenate([c_pm, zhi, c_pp], axis=1),
        ],
        axis=0,
    )
    fx, fy, fz = flow[0], flow[1], flow[2]
    for step in range(TRACER_STEPS):
        conc = tracer_update(conc, fx, fy, fz)
        fx, fy, fz = fx[1:-1, 1:-1], fy[1:-1, 1:-1], fz[1:-1, 1:-1]
    return (state, conc)


def solution(mesh):
    placed = (P(None, "vessel", "blk", None), P("vessel", "blk", None), P("blk", "vessel", None))
    return jax.shard_map(
        local,
        mesh=mesh,
        in_specs=placed,
        out_specs=(P(None, "vessel", "blk", None), P("blk", "vessel", None)),
        check_vma=False,
    )
```

```python
import functools

import jax
import jax.numpy as jnp
import numpy as np
from jax import lax
from jax.experimental import pallas as pl
from jax.experimental.pallas import tpu as pltpu
from jax.sharding import PartitionSpec as P

STEPS = 4
TRACER_STEPS = 2


VELOCITY = np.array(
    [
        [0, 0, 0],
        [1, 0, 0],
        [-1, 0, 0],
        [0, 1, 0],
        [0, -1, 0],
        [0, 0, 1],
        [0, 0, -1],
        [1, 1, 0],
        [-1, -1, 0],
        [1, -1, 0],
        [-1, 1, 0],
        [1, 0, 1],
        [-1, 0, -1],
        [1, 0, -1],
        [-1, 0, 1],
        [0, 1, 1],
        [0, -1, -1],
        [0, 1, -1],
        [0, -1, 1],
    ]
)
WEIGHTS = np.array([1.0 / 3.0] + [1.0 / 18.0] * 6 + [1.0 / 36.0] * 12)
OPPOSITE = [0, 2, 1, 4, 3, 6, 5, 8, 7, 10, 9, 12, 11, 14, 13, 16, 15, 18, 17]
relax_rate = 1.25
pore_damping = 0.5
advect_gain = 8.0
diffusion = 0.1

NPOP = 19
CX = [int(v) for v in VELOCITY[:, 0]]
CY = [int(v) for v in VELOCITY[:, 1]]
CZ = [int(v) for v in VELOCITY[:, 2]]
CXP = [i for i in range(NPOP) if CX[i] == 1]
CXM = [i for i in range(NPOP) if CX[i] == -1]
CYP = [i for i in range(NPOP) if CY[i] == 1]
CYM = [i for i in range(NPOP) if CY[i] == -1]
SHIFTED = [i for i in range(NPOP) if CX[i] != 0 or CY[i] != 0]
ROWS = 8
YOFF = 8


def moments_chunk(g):
    w0 = jnp.float32(WEIGHTS[0])
    w1 = jnp.float32(WEIGHTS[1])
    w2 = jnp.float32(WEIGHTS[7])
    s1 = ((g[1] + g[2]) + (g[3] + g[4])) + (g[5] + g[6])
    s2 = (((g[7] + g[8]) + (g[9] + g[10])) + ((g[11] + g[12]) + (g[13] + g[14]))) + (
        (g[15] + g[16]) + (g[17] + g[18])
    )
    density = w0 * g[0] + w1 * s1 + w2 * s2
    d1, d3, d5 = g[1] - g[2], g[3] - g[4], g[5] - g[6]
    d7, d9, d11, d13 = g[7] - g[8], g[9] - g[10], g[11] - g[12], g[13] - g[14]
    d15, d17 = g[15] - g[16], g[17] - g[18]
    mx = w1 * d1 + w2 * ((d7 + d9) + (d11 + d13))
    my = w1 * d3 + w2 * ((d7 - d9) + (d15 + d17))
    mz = w1 * d5 + w2 * ((d11 - d13) + (d15 - d17))
    return density, (mx, my, mz)


PAIRS = [(1, 2), (3, 4), (5, 6), (7, 8), (9, 10), (11, 12), (13, 14), (15, 16), (17, 18)]


def collide_chunk(g, mask):
    density, (mx, my, mz) = moments_chunk(g)
    scale = jnp.where(mask == 1, jnp.float32(pore_damping), jnp.float32(1.0))
    k = (1.0 / density) * scale
    ux = mx * k
    uy = my * k
    uz = mz * k
    base = 1.0 - 1.5 * (ux * ux + uy * uy + uz * uz)
    dens = relax_rate * density
    keep = 1.0 - relax_rate
    solid = mask == 2
    proj = {
        1: ux,
        3: uy,
        5: uz,
        7: ux + uy,
        9: ux - uy,
        11: ux + uz,
        13: ux - uz,
        15: uy + uz,
        17: uy - uz,
    }
    out = [None] * NPOP
    out[0] = jnp.where(solid, g[0], dens * base + keep * g[0])
    for i, j in PAIRS:
        p = proj[i]
        q = base + 4.5 * (p * p)
        t = 3.0 * p
        relaxed_i = dens * (q + t) + keep * g[i]
        relaxed_j = dens * (q - t) + keep * g[j]
        out[i] = jnp.where(solid, g[j], relaxed_i)
        out[j] = jnp.where(solid, g[i], relaxed_j)
    return out


def lb_kernel(halo, nx, ny, *refs):
    g0, mask_ref, pw_ref, py_ref, xlo, xhi, ylo, yhi, c_mm, c_mp, c_pm, c_pp = refs[:12]
    out_ref, coarse_ref, abuf, bbuf, flow_s = refs[12:]
    h = halo
    top = YOFF
    abuf[0:NPOP, h : h + nx, top : top + ny, :] = g0[...]
    abuf[NPOP, h : h + nx, top : top + ny, :] = mask_ref[...].astype(jnp.float32)
    planes = NPOP + 1
    abuf[:, 0:h, top : top + ny, :] = xlo[0:planes]
    abuf[:, h + nx : 2 * h + nx, top : top + ny, :] = xhi[0:planes]
    abuf[:, h : h + nx, top - h : top, :] = ylo[0:planes]
    abuf[:, h : h + nx, top + ny : top + ny + h, :] = yhi[0:planes]
    abuf[:, 0:h, top - h : top, :] = c_mm[0:planes]
    abuf[:, h + nx : 2 * h + nx, top - h : top, :] = c_mp[0:planes]
    abuf[:, 0:h, top + ny : top + ny + h, :] = c_pm[0:planes]
    abuf[:, h + nx : 2 * h + nx, top + ny : top + ny + h, :] = c_pp[0:planes]

    bufs = [bbuf, abuf]
    offs = [top] + [h - s for s in range(1, h + 1)]

    def run_step(s):
        src = abuf if s == 0 else bufs[(s - 1) % 2]
        dst = bufs[s % 2]
        if s == 0:
            rows = list(range(0, top + ny + h, ROWS))
        else:
            rows = list(range(0, ny + 2 * (h - s), ROWS))
        shift = offs[s - 1] - offs[s] if s > 0 else 0

        def body(x, carry):
            for r in rows:
                g = []
                for i in range(NPOP):
                    if s == 0:
                        v = src[i, x, pl.ds(r, ROWS), :]
                    else:
                        v = src[i, x - CX[i], pl.ds(r + shift - CY[i], ROWS), :]
                        if CZ[i] != 0:
                            v = pltpu.roll(v, CZ[i] % v.shape[1], 1)
                    g.append(v)
                mask = abuf[NPOP, x, pl.ds(r - offs[s] + top, ROWS), :]
                post = collide_chunk(g, mask)
                for i in range(NPOP):
                    dst[i, x, pl.ds(r, ROWS), :] = post[i]
            return carry

        lax.fori_loop(s, nx + 2 * h - s, body, 0)

    for s in range(h):
        run_step(s)

    src = bufs[(h - 1) % 2]
    shift = offs[h - 1] - 0

    def last_body(x, carry):
        for r in range(0, ny, ROWS):
            g = []
            for i in range(NPOP):
                v = src[i, x + h - CX[i], pl.ds(r + shift - CY[i], ROWS), :]
                if CZ[i] != 0:
                    v = pltpu.roll(v, CZ[i] % v.shape[1], 1)
                g.append(v)
                out_ref[i, x, pl.ds(r, ROWS), :] = v
            mask = abuf[NPOP, x + h, pl.ds(r + top, ROWS), :]
            density, mom = moments_chunk(g)
            inv = 1.0 / density
            solid = mask == 2
            for d in range(3):
                flow_s[d, x, pl.ds(r, ROWS), :] = jnp.where(solid, jnp.float32(0.0), mom[d] * inv)
        return carry

    lax.fori_loop(0, nx, last_body, 0)

    pw = pw_ref[...]
    py = py_ref[...]
    for d in range(3):
        for xp in range(nx // 2):
            plane = flow_s[d, 2 * xp] + flow_s[d, 2 * xp + 1]
            zy = lax.dot_general(
                pw,
                plane,
                (((1,), (1,)), ((), ())),
                precision=lax.Precision.HIGHEST,
                preferred_element_type=jnp.float32,
            )
            zc = jnp.dot(zy, py, precision=lax.Precision.HIGHEST, preferred_element_type=jnp.float32)
            coarse_ref[d, xp] = zc * jnp.float32(0.125)


def lb_call(g0, mask, halos, halo, nwin, w):
    _, nx, ny, nz = g0.shape
    zb = nz // 2 // nwin
    win = zb + 2 * w
    rows = np.arange(nwin * win)
    coarse_z = (rows // win * zb - w + rows % win) % (nz // 2)
    pw = jnp.asarray((np.arange(nz)[None, :] // 2 == coarse_z[:, None]).astype(np.float32))
    py = jnp.asarray((np.arange(ny)[:, None] // 2 == np.arange(ny // 2)[None, :]).astype(np.float32))
    f32 = jnp.float32
    vmem = pl.BlockSpec(memory_space=pltpu.VMEM)
    rows = YOFF + ny + 2 * halo
    rows = -(-rows // ROWS) * ROWS
    out_shape = (
        jax.ShapeDtypeStruct(g0.shape, f32),
        jax.ShapeDtypeStruct((3, nx // 2, nwin * win, ny // 2), f32),
    )
    scratch = [
        pltpu.VMEM((NPOP + 1, nx + 2 * halo, rows, nz), f32),
        pltpu.VMEM((NPOP, nx + 2 * halo, rows, nz), f32),
        pltpu.VMEM((3, nx, ny, nz), f32),
    ]
    cells = (nx + halo) * (ny + 2 * halo) * nz * halo
    cost = pl.CostEstimate(flops=320 * cells, transcendentals=0, bytes_accessed=2 * NPOP * 4 * nx * ny * nz * 2)
    return pl.pallas_call(
        functools.partial(lb_kernel, halo, nx, ny),
        out_shape=out_shape,
        in_specs=[vmem] * (4 + len(halos)),
        out_specs=(vmem, vmem),
        scratch_shapes=scratch,
        cost_estimate=cost,
        compiler_params=pltpu.CompilerParams(vmem_limit_bytes=60 * 1024 * 1024),
    )(g0, mask, pw, py, *halos)


def send(x, dv, db):
    nv = lax.axis_size("vessel")
    nb = lax.axis_size("blk")
    if db == 0:
        return lax.ppermute(x, "vessel", [(i, (i + dv) % nv) for i in range(nv)])
    if dv == 0:
        return lax.ppermute(x, "blk", [(i, (i + db) % nb) for i in range(nb)])
    pairs = []
    for v in range(nv):
        for b in range(nb):
            pairs.append((v * nb + b, ((v + dv) % nv) * nb + (b + db) % nb))
    return lax.ppermute(x, ("vessel", "blk"), pairs)


def lattice_halos(g0, mask, conc, h, w):
    _, nx, ny, nz = g0.shape
    nzc, nxc, nyc = conc.shape
    maskf = mask.astype(jnp.float32)[None]
    lat = {1: slice(nx - h, nx), -1: slice(0, h), 0: slice(0, nx)}
    lat_y = {1: slice(ny - h, ny), -1: slice(0, h), 0: slice(0, ny)}
    trc_x = {1: slice(nxc - w, nxc), -1: slice(0, w), 0: slice(0, nxc)}
    trc_z = {1: slice(nzc - w, nzc), -1: slice(0, w), 0: slice(0, nzc)}
    order = ((1, 0), (-1, 0), (0, 1), (0, -1), (1, 1), (-1, 1), (1, -1), (-1, -1))
    pieces, tracer_pieces = [], []
    for dv, db in order:
        xs, ys = lat[dv], lat_y[db]
        lb = jnp.concatenate([g0[:, xs, ys], maskf[:, xs, ys]], axis=0)
        tp = conc[trc_z[db], trc_x[dv]]
        plane = lb.shape[1] * lb.shape[2] * nz
        flat = jnp.pad(tp.reshape(-1), (0, plane - tp.size))
        msg = jnp.concatenate([lb, flat.reshape(1, lb.shape[1], lb.shape[2], nz)], axis=0)
        got = send(msg, dv, db)
        pieces.append(got)
        tracer_pieces.append(got[NPOP + 1].reshape(-1)[: tp.size].reshape(tp.shape))
    return pieces, tracer_pieces


def tracer_update(c, fx, fy, fz):
    flux_x = fx * c
    flux_y = fy[1:-1, 1:-1] * c[1:-1, 1:-1]
    flux_z = fz * c
    center = c[1:-1, 1:-1]
    div_x = (flux_x[1:-1, 2:] - flux_x[1:-1, :-2]) * 0.5
    div_y = (jnp.roll(flux_y, -1, 2) - jnp.roll(flux_y, 1, 2)) * 0.5
    div_z = (flux_z[2:, 1:-1] - flux_z[:-2, 1:-1]) * 0.5
    divergence = div_x + div_y + div_z
    beside_all = (
        (c[1:-1, 2:] + c[1:-1, :-2])
        + (jnp.roll(center, -1, 2) + jnp.roll(center, 1, 2))
        + (c[2:, 1:-1] + c[:-2, 1:-1])
    )
    laplace = beside_all - 6.0 * center
    return center - advect_gain * divergence + diffusion * laplace


def local(populations, voxel_mask, tracer):
    w = TRACER_STEPS
    halos, tp = lattice_halos(populations, voxel_mask, tracer, STEPS, w)
    nb = lax.axis_size("blk")
    state, coarse = lb_call(populations, voxel_mask, halos, STEPS, nb, w)
    windows = coarse.reshape(3, coarse.shape[1], nb, coarse.shape[2] // nb, coarse.shape[3])
    moved = lax.all_to_all(windows, "blk", split_axis=2, concat_axis=4, tiled=True)
    flow = moved[:, :, 0]
    nxb = flow.shape[1]
    flow = jnp.concatenate([send(flow[:, nxb - w :], 1, 0), flow, send(flow[:, :w], -1, 0)], axis=1)
    flow = jnp.transpose(flow, (0, 2, 1, 3))
    xlo, xhi, zlo, zhi, c_mm, c_mp, c_pm, c_pp = tp
    conc = jnp.concatenate(
        [
            jnp.concatenate([c_mm, zlo, c_mp], axis=1),
            jnp.concatenate([xlo, tracer, xhi], axis=1),
            jnp.concatenate([c_pm, zhi, c_pp], axis=1),
        ],
        axis=0,
    )
    fx, fy, fz = flow[0], flow[1], flow[2]
    for step in range(TRACER_STEPS):
        conc = tracer_update(conc, fx, fy, fz)
        fx, fy, fz = fx[1:-1, 1:-1], fy[1:-1, 1:-1], fz[1:-1, 1:-1]
    return (state, conc)


def solution(mesh):
    placed = (P(None, "vessel", "blk", None), P("vessel", "blk", None), P("blk", "vessel", None))
    return jax.shard_map(
        local,
        mesh=mesh,
        in_specs=placed,
        out_specs=(P(None, "vessel", "blk", None), P("blk", "vessel", None)),
        check_vma=False,
    )
```

```python
import functools

import jax
import jax.numpy as jnp
import numpy as np
from jax import lax
from jax.experimental import pallas as pl
from jax.experimental.pallas import tpu as pltpu
from jax.sharding import PartitionSpec as P

STEPS = 4
TRACER_STEPS = 2


VELOCITY = np.array(
    [
        [0, 0, 0],
        [1, 0, 0],
        [-1, 0, 0],
        [0, 1, 0],
        [0, -1, 0],
        [0, 0, 1],
        [0, 0, -1],
        [1, 1, 0],
        [-1, -1, 0],
        [1, -1, 0],
        [-1, 1, 0],
        [1, 0, 1],
        [-1, 0, -1],
        [1, 0, -1],
        [-1, 0, 1],
        [0, 1, 1],
        [0, -1, -1],
        [0, 1, -1],
        [0, -1, 1],
    ]
)
WEIGHTS = np.array([1.0 / 3.0] + [1.0 / 18.0] * 6 + [1.0 / 36.0] * 12)
OPPOSITE = [0, 2, 1, 4, 3, 6, 5, 8, 7, 10, 9, 12, 11, 14, 13, 16, 15, 18, 17]
relax_rate = 1.25
pore_damping = 0.5
advect_gain = 8.0
diffusion = 0.1

NPOP = 19
CX = [int(v) for v in VELOCITY[:, 0]]
CY = [int(v) for v in VELOCITY[:, 1]]
CZ = [int(v) for v in VELOCITY[:, 2]]
CXP = [i for i in range(NPOP) if CX[i] == 1]
CXM = [i for i in range(NPOP) if CX[i] == -1]
CYP = [i for i in range(NPOP) if CY[i] == 1]
CYM = [i for i in range(NPOP) if CY[i] == -1]
SHIFTED = [i for i in range(NPOP) if CX[i] != 0 or CY[i] != 0]
ROWS = 8
YOFF = 8


def moments_chunk(g):
    w0 = jnp.float32(WEIGHTS[0])
    w1 = jnp.float32(WEIGHTS[1])
    w2 = jnp.float32(WEIGHTS[7])
    s1 = ((g[1] + g[2]) + (g[3] + g[4])) + (g[5] + g[6])
    s2 = (((g[7] + g[8]) + (g[9] + g[10])) + ((g[11] + g[12]) + (g[13] + g[14]))) + (
        (g[15] + g[16]) + (g[17] + g[18])
    )
    density = w0 * g[0] + w1 * s1 + w2 * s2
    d1, d3, d5 = g[1] - g[2], g[3] - g[4], g[5] - g[6]
    d7, d9, d11, d13 = g[7] - g[8], g[9] - g[10], g[11] - g[12], g[13] - g[14]
    d15, d17 = g[15] - g[16], g[17] - g[18]
    mx = w1 * d1 + w2 * ((d7 + d9) + (d11 + d13))
    my = w1 * d3 + w2 * ((d7 - d9) + (d15 + d17))
    mz = w1 * d5 + w2 * ((d11 - d13) + (d15 - d17))
    return density, (mx, my, mz)


PAIRS = [(1, 2), (3, 4), (5, 6), (7, 8), (9, 10), (11, 12), (13, 14), (15, 16), (17, 18)]


def collide_chunk(g, mask):
    density, (mx, my, mz) = moments_chunk(g)
    scale = jnp.where(mask == 1, jnp.float32(pore_damping), jnp.float32(1.0))
    k = (1.0 / density) * scale
    ux = mx * k
    uy = my * k
    uz = mz * k
    base = 1.0 - 1.5 * (ux * ux + uy * uy + uz * uz)
    dens = relax_rate * density
    keep = 1.0 - relax_rate
    solid = mask == 2
    proj = {
        1: ux,
        3: uy,
        5: uz,
        7: ux + uy,
        9: ux - uy,
        11: ux + uz,
        13: ux - uz,
        15: uy + uz,
        17: uy - uz,
    }
    out = [None] * NPOP
    out[0] = jnp.where(solid, g[0], dens * base + keep * g[0])
    for i, j in PAIRS:
        p = proj[i]
        q = base + 4.5 * (p * p)
        t = 3.0 * p
        relaxed_i = dens * (q + t) + keep * g[i]
        relaxed_j = dens * (q - t) + keep * g[j]
        out[i] = jnp.where(solid, g[j], relaxed_i)
        out[j] = jnp.where(solid, g[i], relaxed_j)
    return out


def lb_kernel(halo, nx, ny, *refs):
    g0, mask_ref, xlo, xhi, ylo, yhi, c_mm, c_mp, c_pm, c_pp = refs[:10]
    out_ref, coarse_ref, abuf, bbuf, flow_s = refs[10:]
    h = halo
    top = YOFF
    abuf[0:NPOP, h : h + nx, top : top + ny, :] = g0[...]
    abuf[NPOP, h : h + nx, top : top + ny, :] = mask_ref[...].astype(jnp.float32)
    planes = NPOP + 1
    abuf[:, 0:h, top : top + ny, :] = xlo[0:planes]
    abuf[:, h + nx : 2 * h + nx, top : top + ny, :] = xhi[0:planes]
    abuf[:, h : h + nx, top - h : top, :] = ylo[0:planes]
    abuf[:, h : h + nx, top + ny : top + ny + h, :] = yhi[0:planes]
    abuf[:, 0:h, top - h : top, :] = c_mm[0:planes]
    abuf[:, h + nx : 2 * h + nx, top - h : top, :] = c_mp[0:planes]
    abuf[:, 0:h, top + ny : top + ny + h, :] = c_pm[0:planes]
    abuf[:, h + nx : 2 * h + nx, top + ny : top + ny + h, :] = c_pp[0:planes]

    bufs = [bbuf, abuf]
    offs = [top] + [h - s for s in range(1, h + 1)]

    def run_step(s):
        src = abuf if s == 0 else bufs[(s - 1) % 2]
        dst = bufs[s % 2]
        if s == 0:
            rows = list(range(0, top + ny + h, ROWS))
        else:
            rows = list(range(0, ny + 2 * (h - s), ROWS))
        shift = offs[s - 1] - offs[s] if s > 0 else 0

        def body(x, carry):
            for r in rows:
                g = []
                for i in range(NPOP):
                    if s == 0:
                        v = src[i, x, pl.ds(r, ROWS), :]
                    else:
                        v = src[i, x - CX[i], pl.ds(r + shift - CY[i], ROWS), :]
                        if CZ[i] != 0:
                            v = pltpu.roll(v, CZ[i] % v.shape[1], 1)
                    g.append(v)
                mask = abuf[NPOP, x, pl.ds(r - offs[s] + top, ROWS), :]
                post = collide_chunk(g, mask)
                for i in range(NPOP):
                    dst[i, x, pl.ds(r, ROWS), :] = post[i]
            return carry

        lax.fori_loop(s, nx + 2 * h - s, body, 0, unroll=2)

    for s in range(h):
        run_step(s)

    src = bufs[(h - 1) % 2]
    shift = offs[h - 1] - 0

    def last_body(x, carry):
        for r in range(0, ny, ROWS):
            g = []
            for i in range(NPOP):
                v = src[i, x + h - CX[i], pl.ds(r + shift - CY[i], ROWS), :]
                if CZ[i] != 0:
                    v = pltpu.roll(v, CZ[i] % v.shape[1], 1)
                g.append(v)
                out_ref[i, x, pl.ds(r, ROWS), :] = v
            mask = abuf[NPOP, x + h, pl.ds(r + top, ROWS), :]
            density, mom = moments_chunk(g)
            inv = 1.0 / density
            solid = mask == 2
            for d in range(3):
                flow_s[d, x, pl.ds(r, ROWS), :] = jnp.where(solid, jnp.float32(0.0), mom[d] * inv)
        return carry

    lax.fori_loop(0, nx, last_body, 0, unroll=2)

    nz = flow_s.shape[3]
    pz = (
        lax.broadcasted_iota(jnp.int32, (nz // 2, nz), 1) // 2 == lax.broadcasted_iota(jnp.int32, (nz // 2, nz), 0)
    ).astype(jnp.float32)
    py = (
        lax.broadcasted_iota(jnp.int32, (ny, ny // 2), 0) // 2 == lax.broadcasted_iota(jnp.int32, (ny, ny // 2), 1)
    ).astype(jnp.float32)
    for d in range(3):
        for xp in range(nx // 2):
            plane = flow_s[d, 2 * xp] + flow_s[d, 2 * xp + 1]
            zy = lax.dot_general(
                pz,
                plane,
                (((1,), (1,)), ((), ())),
                precision=lax.Precision.HIGHEST,
                preferred_element_type=jnp.float32,
            )
            zc = jnp.dot(zy, py, precision=lax.Precision.HIGHEST, preferred_element_type=jnp.float32)
            coarse_ref[d, xp] = zc * jnp.float32(0.125)


def lb_call(g0, mask, halos, halo):
    _, nx, ny, nz = g0.shape
    f32 = jnp.float32
    vmem = pl.BlockSpec(memory_space=pltpu.VMEM)
    rows = YOFF + ny + 2 * halo
    rows = -(-rows // ROWS) * ROWS
    out_shape = (
        jax.ShapeDtypeStruct(g0.shape, f32),
        jax.ShapeDtypeStruct((3, nx // 2, nz // 2, ny // 2), f32),
    )
    scratch = [
        pltpu.VMEM((NPOP + 1, nx + 2 * halo, rows, nz), f32),
        pltpu.VMEM((NPOP, nx + 2 * halo, rows, nz), f32),
        pltpu.VMEM((3, nx, ny, nz), f32),
    ]
    cells = (nx + halo) * (ny + 2 * halo) * nz * halo
    cost = pl.CostEstimate(flops=320 * cells, transcendentals=0, bytes_accessed=2 * NPOP * 4 * nx * ny * nz * 2)
    return pl.pallas_call(
        functools.partial(lb_kernel, halo, nx, ny),
        out_shape=out_shape,
        in_specs=[vmem] * (2 + len(halos)),
        out_specs=(vmem, vmem),
        scratch_shapes=scratch,
        cost_estimate=cost,
        compiler_params=pltpu.CompilerParams(vmem_limit_bytes=60 * 1024 * 1024),
    )(g0, mask, *halos)


def send(x, dv, db):
    nv = lax.axis_size("vessel")
    nb = lax.axis_size("blk")
    if db == 0:
        return lax.ppermute(x, "vessel", [(i, (i + dv) % nv) for i in range(nv)])
    if dv == 0:
        return lax.ppermute(x, "blk", [(i, (i + db) % nb) for i in range(nb)])
    pairs = []
    for v in range(nv):
        for b in range(nb):
            pairs.append((v * nb + b, ((v + dv) % nv) * nb + (b + db) % nb))
    return lax.ppermute(x, ("vessel", "blk"), pairs)


def lattice_halos(g0, mask, conc, h, w):
    _, nx, ny, nz = g0.shape
    nzc, nxc, nyc = conc.shape
    maskf = mask.astype(jnp.float32)[None]
    lat = {1: slice(nx - h, nx), -1: slice(0, h), 0: slice(0, nx)}
    lat_y = {1: slice(ny - h, ny), -1: slice(0, h), 0: slice(0, ny)}
    trc_x = {1: slice(nxc - w, nxc), -1: slice(0, w), 0: slice(0, nxc)}
    trc_z = {1: slice(nzc - w, nzc), -1: slice(0, w), 0: slice(0, nzc)}
    order = ((1, 0), (-1, 0), (0, 1), (0, -1), (1, 1), (-1, 1), (1, -1), (-1, -1))
    pieces, tracer_pieces = [], []
    for dv, db in order:
        xs, ys = lat[dv], lat_y[db]
        lb = jnp.concatenate([g0[:, xs, ys], maskf[:, xs, ys]], axis=0)
        tp = conc[trc_z[db], trc_x[dv]]
        plane = lb.shape[1] * lb.shape[2] * nz
        flat = jnp.pad(tp.reshape(-1), (0, plane - tp.size))
        msg = jnp.concatenate([lb, flat.reshape(1, lb.shape[1], lb.shape[2], nz)], axis=0)
        got = send(msg, dv, db)
        pieces.append(got)
        tracer_pieces.append(got[NPOP + 1].reshape(-1)[: tp.size].reshape(tp.shape))
    return pieces, tracer_pieces


def tracer_update(c, fx, fy, fz):
    flux_x = fx * c
    flux_y = fy[1:-1, 1:-1] * c[1:-1, 1:-1]
    flux_z = fz * c
    center = c[1:-1, 1:-1]
    div_x = (flux_x[1:-1, 2:] - flux_x[1:-1, :-2]) * 0.5
    div_y = (jnp.roll(flux_y, -1, 2) - jnp.roll(flux_y, 1, 2)) * 0.5
    div_z = (flux_z[2:, 1:-1] - flux_z[:-2, 1:-1]) * 0.5
    divergence = div_x + div_y + div_z
    beside_all = (
        (c[1:-1, 2:] + c[1:-1, :-2])
        + (jnp.roll(center, -1, 2) + jnp.roll(center, 1, 2))
        + (c[2:, 1:-1] + c[:-2, 1:-1])
    )
    laplace = beside_all - 6.0 * center
    return center - advect_gain * divergence + diffusion * laplace


def local(populations, voxel_mask, tracer):
    w = TRACER_STEPS
    halos, tp = lattice_halos(populations, voxel_mask, tracer, STEPS, w)
    state, coarse = lb_call(populations, voxel_mask, halos, STEPS)
    nzt = coarse.shape[2]
    nb = lax.axis_size("blk")
    zb = nzt // nb
    ring = jnp.concatenate([coarse[:, :, nzt - w :], coarse, coarse[:, :, :zb]], axis=2)
    head = ring[:, :, : nb * zb].reshape(3, coarse.shape[1], nb, zb, coarse.shape[3])
    tail = ring[:, :, zb : zb + nb * zb].reshape(3, coarse.shape[1], nb, zb, coarse.shape[3])
    windows = jnp.concatenate([head, tail], axis=3)[:, :, :, : zb + 2 * w]
    moved = lax.all_to_all(windows, "blk", split_axis=2, concat_axis=4, tiled=True)
    flow = moved[:, :, 0]
    nxb = flow.shape[1]
    flow = jnp.concatenate([send(flow[:, nxb - w :], 1, 0), flow, send(flow[:, :w], -1, 0)], axis=1)
    flow = jnp.transpose(flow, (0, 2, 1, 3))
    xlo, xhi, zlo, zhi, c_mm, c_mp, c_pm, c_pp = tp
    conc = jnp.concatenate(
        [
            jnp.concatenate([c_mm, zlo, c_mp], axis=1),
            jnp.concatenate([xlo, tracer, xhi], axis=1),
            jnp.concatenate([c_pm, zhi, c_pp], axis=1),
        ],
        axis=0,
    )
    fx, fy, fz = flow[0], flow[1], flow[2]
    for step in range(TRACER_STEPS):
        conc = tracer_update(conc, fx, fy, fz)
        fx, fy, fz = fx[1:-1, 1:-1], fy[1:-1, 1:-1], fz[1:-1, 1:-1]
    return (state, conc)


def solution(mesh):
    placed = (P(None, "vessel", "blk", None), P("vessel", "blk", None), P("blk", "vessel", None))
    return jax.shard_map(
        local,
        mesh=mesh,
        in_specs=placed,
        out_specs=(P(None, "vessel", "blk", None), P("blk", "vessel", None)),
        check_vma=False,
    )
```

```python
import functools

import jax
import jax.numpy as jnp
import numpy as np
from jax import lax
from jax.experimental import pallas as pl
from jax.experimental.pallas import tpu as pltpu
from jax.sharding import PartitionSpec as P

STEPS = 4
TRACER_STEPS = 2


VELOCITY = np.array(
    [
        [0, 0, 0],
        [1, 0, 0],
        [-1, 0, 0],
        [0, 1, 0],
        [0, -1, 0],
        [0, 0, 1],
        [0, 0, -1],
        [1, 1, 0],
        [-1, -1, 0],
        [1, -1, 0],
        [-1, 1, 0],
        [1, 0, 1],
        [-1, 0, -1],
        [1, 0, -1],
        [-1, 0, 1],
        [0, 1, 1],
        [0, -1, -1],
        [0, 1, -1],
        [0, -1, 1],
    ]
)
WEIGHTS = np.array([1.0 / 3.0] + [1.0 / 18.0] * 6 + [1.0 / 36.0] * 12)
OPPOSITE = [0, 2, 1, 4, 3, 6, 5, 8, 7, 10, 9, 12, 11, 14, 13, 16, 15, 18, 17]
relax_rate = 1.25
pore_damping = 0.5
advect_gain = 8.0
diffusion = 0.1

NPOP = 19
CX = [int(v) for v in VELOCITY[:, 0]]
CY = [int(v) for v in VELOCITY[:, 1]]
CZ = [int(v) for v in VELOCITY[:, 2]]
CXP = [i for i in range(NPOP) if CX[i] == 1]
CXM = [i for i in range(NPOP) if CX[i] == -1]
CYP = [i for i in range(NPOP) if CY[i] == 1]
CYM = [i for i in range(NPOP) if CY[i] == -1]
SHIFTED = [i for i in range(NPOP) if CX[i] != 0 or CY[i] != 0]
ROWS = 8
YOFF = 8


def moments_chunk(g):
    w0 = jnp.float32(WEIGHTS[0])
    w1 = jnp.float32(WEIGHTS[1])
    w2 = jnp.float32(WEIGHTS[7])
    s1 = ((g[1] + g[2]) + (g[3] + g[4])) + (g[5] + g[6])
    s2 = (((g[7] + g[8]) + (g[9] + g[10])) + ((g[11] + g[12]) + (g[13] + g[14]))) + (
        (g[15] + g[16]) + (g[17] + g[18])
    )
    density = w0 * g[0] + w1 * s1 + w2 * s2
    d1, d3, d5 = g[1] - g[2], g[3] - g[4], g[5] - g[6]
    d7, d9, d11, d13 = g[7] - g[8], g[9] - g[10], g[11] - g[12], g[13] - g[14]
    d15, d17 = g[15] - g[16], g[17] - g[18]
    mx = w1 * d1 + w2 * ((d7 + d9) + (d11 + d13))
    my = w1 * d3 + w2 * ((d7 - d9) + (d15 + d17))
    mz = w1 * d5 + w2 * ((d11 - d13) + (d15 - d17))
    return density, (mx, my, mz)


PAIRS = [(1, 2), (3, 4), (5, 6), (7, 8), (9, 10), (11, 12), (13, 14), (15, 16), (17, 18)]


def collide_chunk(g, mask):
    density, (mx, my, mz) = moments_chunk(g)
    scale = jnp.where(mask == 1, jnp.float32(pore_damping), jnp.float32(1.0))
    k = (1.0 / density) * scale
    ux = mx * k
    uy = my * k
    uz = mz * k
    base = 1.0 - 1.5 * (ux * ux + uy * uy + uz * uz)
    dens = relax_rate * density
    keep = 1.0 - relax_rate
    solid = mask == 2
    proj = {
        1: ux,
        3: uy,
        5: uz,
        7: ux + uy,
        9: ux - uy,
        11: ux + uz,
        13: ux - uz,
        15: uy + uz,
        17: uy - uz,
    }
    out = [None] * NPOP
    out[0] = jnp.where(solid, g[0], dens * base + keep * g[0])
    for i, j in PAIRS:
        p = proj[i]
        q = base + 4.5 * (p * p)
        t = 3.0 * p
        relaxed_i = dens * (q + t) + keep * g[i]
        relaxed_j = dens * (q - t) + keep * g[j]
        out[i] = jnp.where(solid, g[j], relaxed_i)
        out[j] = jnp.where(solid, g[i], relaxed_j)
    return out


def lb_kernel(halo, nx, ny, *refs):
    g0, mask_ref, xlo, xhi, ylo, yhi, c_mm, c_mp, c_pm, c_pp = refs[:10]
    out_ref, coarse_ref, abuf, bbuf, flow_s = refs[10:]
    h = halo
    top = YOFF
    abuf[0:NPOP, h : h + nx, top : top + ny, :] = g0[...]
    abuf[NPOP, h : h + nx, top : top + ny, :] = mask_ref[...].astype(jnp.float32)
    planes = NPOP + 1
    abuf[:, 0:h, top : top + ny, :] = xlo[0:planes]
    abuf[:, h + nx : 2 * h + nx, top : top + ny, :] = xhi[0:planes]
    abuf[:, h : h + nx, top - h : top, :] = ylo[0:planes]
    abuf[:, h : h + nx, top + ny : top + ny + h, :] = yhi[0:planes]
    abuf[:, 0:h, top - h : top, :] = c_mm[0:planes]
    abuf[:, h + nx : 2 * h + nx, top - h : top, :] = c_mp[0:planes]
    abuf[:, 0:h, top + ny : top + ny + h, :] = c_pm[0:planes]
    abuf[:, h + nx : 2 * h + nx, top + ny : top + ny + h, :] = c_pp[0:planes]

    bufs = [bbuf, abuf]
    offs = [top] + [h - s for s in range(1, h + 1)]

    def run_step(s):
        src = abuf if s == 0 else bufs[(s - 1) % 2]
        dst = bufs[s % 2]
        if s == 0:
            rows = list(range(0, top + ny + h, ROWS))
        else:
            rows = list(range(0, ny + 2 * (h - s), ROWS))
        shift = offs[s - 1] - offs[s] if s > 0 else 0

        def body(x, carry):
            for r in rows:
                g = []
                for i in range(NPOP):
                    if s == 0:
                        v = src[i, x, pl.ds(r, ROWS), :]
                    else:
                        v = src[i, x - CX[i], pl.ds(r + shift - CY[i], ROWS), :]
                        if CZ[i] != 0:
                            v = pltpu.roll(v, CZ[i] % v.shape[1], 1)
                    g.append(v)
                mask = abuf[NPOP, x, pl.ds(r - offs[s] + top, ROWS), :]
                post = collide_chunk(g, mask)
                for i in range(NPOP):
                    dst[i, x, pl.ds(r, ROWS), :] = post[i]
            return carry

        lax.fori_loop(s, nx + 2 * h - s, body, 0, unroll=4)

    for s in range(h):
        run_step(s)

    src = bufs[(h - 1) % 2]
    shift = offs[h - 1] - 0

    def last_body(x, carry):
        for r in range(0, ny, ROWS):
            g = []
            for i in range(NPOP):
                v = src[i, x + h - CX[i], pl.ds(r + shift - CY[i], ROWS), :]
                if CZ[i] != 0:
                    v = pltpu.roll(v, CZ[i] % v.shape[1], 1)
                g.append(v)
                out_ref[i, x, pl.ds(r, ROWS), :] = v
            mask = abuf[NPOP, x + h, pl.ds(r + top, ROWS), :]
            density, mom = moments_chunk(g)
            inv = 1.0 / density
            solid = mask == 2
            for d in range(3):
                flow_s[d, x, pl.ds(r, ROWS), :] = jnp.where(solid, jnp.float32(0.0), mom[d] * inv)
        return carry

    lax.fori_loop(0, nx, last_body, 0, unroll=4)

    nz = flow_s.shape[3]
    pz = (
        lax.broadcasted_iota(jnp.int32, (nz // 2, nz), 1) // 2 == lax.broadcasted_iota(jnp.int32, (nz // 2, nz), 0)
    ).astype(jnp.float32)
    py = (
        lax.broadcasted_iota(jnp.int32, (ny, ny // 2), 0) // 2 == lax.broadcasted_iota(jnp.int32, (ny, ny // 2), 1)
    ).astype(jnp.float32)
    for d in range(3):
        for xp in range(nx // 2):
            plane = flow_s[d, 2 * xp] + flow_s[d, 2 * xp + 1]
            zy = lax.dot_general(
                pz,
                plane,
                (((1,), (1,)), ((), ())),
                precision=lax.Precision.HIGHEST,
                preferred_element_type=jnp.float32,
            )
            zc = jnp.dot(zy, py, precision=lax.Precision.HIGHEST, preferred_element_type=jnp.float32)
            coarse_ref[d, xp] = zc * jnp.float32(0.125)


def lb_call(g0, mask, halos, halo):
    _, nx, ny, nz = g0.shape
    f32 = jnp.float32
    vmem = pl.BlockSpec(memory_space=pltpu.VMEM)
    rows = YOFF + ny + 2 * halo
    rows = -(-rows // ROWS) * ROWS
    out_shape = (
        jax.ShapeDtypeStruct(g0.shape, f32),
        jax.ShapeDtypeStruct((3, nx // 2, nz // 2, ny // 2), f32),
    )
    scratch = [
        pltpu.VMEM((NPOP + 1, nx + 2 * halo, rows, nz), f32),
        pltpu.VMEM((NPOP, nx + 2 * halo, rows, nz), f32),
        pltpu.VMEM((3, nx, ny, nz), f32),
    ]
    cells = (nx + halo) * (ny + 2 * halo) * nz * halo
    cost = pl.CostEstimate(flops=320 * cells, transcendentals=0, bytes_accessed=2 * NPOP * 4 * nx * ny * nz * 2)
    return pl.pallas_call(
        functools.partial(lb_kernel, halo, nx, ny),
        out_shape=out_shape,
        in_specs=[vmem] * (2 + len(halos)),
        out_specs=(vmem, vmem),
        scratch_shapes=scratch,
        cost_estimate=cost,
        compiler_params=pltpu.CompilerParams(vmem_limit_bytes=60 * 1024 * 1024),
    )(g0, mask, *halos)


def send(x, dv, db):
    nv = lax.axis_size("vessel")
    nb = lax.axis_size("blk")
    if db == 0:
        return lax.ppermute(x, "vessel", [(i, (i + dv) % nv) for i in range(nv)])
    if dv == 0:
        return lax.ppermute(x, "blk", [(i, (i + db) % nb) for i in range(nb)])
    pairs = []
    for v in range(nv):
        for b in range(nb):
            pairs.append((v * nb + b, ((v + dv) % nv) * nb + (b + db) % nb))
    return lax.ppermute(x, ("vessel", "blk"), pairs)


def lattice_halos(g0, mask, conc, h, w):
    _, nx, ny, nz = g0.shape
    nzc, nxc, nyc = conc.shape
    maskf = mask.astype(jnp.float32)[None]
    lat = {1: slice(nx - h, nx), -1: slice(0, h), 0: slice(0, nx)}
    lat_y = {1: slice(ny - h, ny), -1: slice(0, h), 0: slice(0, ny)}
    trc_x = {1: slice(nxc - w, nxc), -1: slice(0, w), 0: slice(0, nxc)}
    trc_z = {1: slice(nzc - w, nzc), -1: slice(0, w), 0: slice(0, nzc)}
    order = ((1, 0), (-1, 0), (0, 1), (0, -1), (1, 1), (-1, 1), (1, -1), (-1, -1))
    pieces, tracer_pieces = [], []
    for dv, db in order:
        xs, ys = lat[dv], lat_y[db]
        lb = jnp.concatenate([g0[:, xs, ys], maskf[:, xs, ys]], axis=0)
        tp = conc[trc_z[db], trc_x[dv]]
        plane = lb.shape[1] * lb.shape[2] * nz
        flat = jnp.pad(tp.reshape(-1), (0, plane - tp.size))
        msg = jnp.concatenate([lb, flat.reshape(1, lb.shape[1], lb.shape[2], nz)], axis=0)
        got = send(msg, dv, db)
        pieces.append(got)
        tracer_pieces.append(got[NPOP + 1].reshape(-1)[: tp.size].reshape(tp.shape))
    return pieces, tracer_pieces


def tracer_update(c, fx, fy, fz):
    flux_x = fx * c
    flux_y = fy[1:-1, 1:-1] * c[1:-1, 1:-1]
    flux_z = fz * c
    center = c[1:-1, 1:-1]
    div_x = (flux_x[1:-1, 2:] - flux_x[1:-1, :-2]) * 0.5
    div_y = (jnp.roll(flux_y, -1, 2) - jnp.roll(flux_y, 1, 2)) * 0.5
    div_z = (flux_z[2:, 1:-1] - flux_z[:-2, 1:-1]) * 0.5
    divergence = div_x + div_y + div_z
    beside_all = (
        (c[1:-1, 2:] + c[1:-1, :-2])
        + (jnp.roll(center, -1, 2) + jnp.roll(center, 1, 2))
        + (c[2:, 1:-1] + c[:-2, 1:-1])
    )
    laplace = beside_all - 6.0 * center
    return center - advect_gain * divergence + diffusion * laplace


def local(populations, voxel_mask, tracer):
    w = TRACER_STEPS
    halos, tp = lattice_halos(populations, voxel_mask, tracer, STEPS, w)
    state, coarse = lb_call(populations, voxel_mask, halos, STEPS)
    nzt = coarse.shape[2]
    nb = lax.axis_size("blk")
    zb = nzt // nb
    ring = jnp.concatenate([coarse[:, :, nzt - w :], coarse, coarse[:, :, :zb]], axis=2)
    head = ring[:, :, : nb * zb].reshape(3, coarse.shape[1], nb, zb, coarse.shape[3])
    tail = ring[:, :, zb : zb + nb * zb].reshape(3, coarse.shape[1], nb, zb, coarse.shape[3])
    windows = jnp.concatenate([head, tail], axis=3)[:, :, :, : zb + 2 * w]
    moved = lax.all_to_all(windows, "blk", split_axis=2, concat_axis=4, tiled=True)
    flow = moved[:, :, 0]
    nxb = flow.shape[1]
    flow = jnp.concatenate([send(flow[:, nxb - w :], 1, 0), flow, send(flow[:, :w], -1, 0)], axis=1)
    flow = jnp.transpose(flow, (0, 2, 1, 3))
    xlo, xhi, zlo, zhi, c_mm, c_mp, c_pm, c_pp = tp
    conc = jnp.concatenate(
        [
            jnp.concatenate([c_mm, zlo, c_mp], axis=1),
            jnp.concatenate([xlo, tracer, xhi], axis=1),
            jnp.concatenate([c_pm, zhi, c_pp], axis=1),
        ],
        axis=0,
    )
    fx, fy, fz = flow[0], flow[1], flow[2]
    for step in range(TRACER_STEPS):
        conc = tracer_update(conc, fx, fy, fz)
        fx, fy, fz = fx[1:-1, 1:-1], fy[1:-1, 1:-1], fz[1:-1, 1:-1]
    return (state, conc)


def solution(mesh):
    placed = (P(None, "vessel", "blk", None), P("vessel", "blk", None), P("blk", "vessel", None))
    return jax.shard_map(
        local,
        mesh=mesh,
        in_specs=placed,
        out_specs=(P(None, "vessel", "blk", None), P("blk", "vessel", None)),
        check_vma=False,
    )
```

```python
import functools

import jax
import jax.numpy as jnp
import numpy as np
from jax import lax
from jax.experimental import pallas as pl
from jax.experimental.pallas import tpu as pltpu
from jax.sharding import PartitionSpec as P

STEPS = 4
TRACER_STEPS = 2


VELOCITY = np.array(
    [
        [0, 0, 0],
        [1, 0, 0],
        [-1, 0, 0],
        [0, 1, 0],
        [0, -1, 0],
        [0, 0, 1],
        [0, 0, -1],
        [1, 1, 0],
        [-1, -1, 0],
        [1, -1, 0],
        [-1, 1, 0],
        [1, 0, 1],
        [-1, 0, -1],
        [1, 0, -1],
        [-1, 0, 1],
        [0, 1, 1],
        [0, -1, -1],
        [0, 1, -1],
        [0, -1, 1],
    ]
)
WEIGHTS = np.array([1.0 / 3.0] + [1.0 / 18.0] * 6 + [1.0 / 36.0] * 12)
OPPOSITE = [0, 2, 1, 4, 3, 6, 5, 8, 7, 10, 9, 12, 11, 14, 13, 16, 15, 18, 17]
relax_rate = 1.25
pore_damping = 0.5
advect_gain = 8.0
diffusion = 0.1

NPOP = 19
CX = [int(v) for v in VELOCITY[:, 0]]
CY = [int(v) for v in VELOCITY[:, 1]]
CZ = [int(v) for v in VELOCITY[:, 2]]
CXP = [i for i in range(NPOP) if CX[i] == 1]
CXM = [i for i in range(NPOP) if CX[i] == -1]
CYP = [i for i in range(NPOP) if CY[i] == 1]
CYM = [i for i in range(NPOP) if CY[i] == -1]
SHIFTED = [i for i in range(NPOP) if CX[i] != 0 or CY[i] != 0]
ROWS = 8
YOFF = 8


def moments_chunk(g):
    w0 = jnp.float32(WEIGHTS[0])
    w1 = jnp.float32(WEIGHTS[1])
    w2 = jnp.float32(WEIGHTS[7])
    s1 = ((g[1] + g[2]) + (g[3] + g[4])) + (g[5] + g[6])
    s2 = (((g[7] + g[8]) + (g[9] + g[10])) + ((g[11] + g[12]) + (g[13] + g[14]))) + (
        (g[15] + g[16]) + (g[17] + g[18])
    )
    density = w0 * g[0] + w1 * s1 + w2 * s2
    d1, d3, d5 = g[1] - g[2], g[3] - g[4], g[5] - g[6]
    d7, d9, d11, d13 = g[7] - g[8], g[9] - g[10], g[11] - g[12], g[13] - g[14]
    d15, d17 = g[15] - g[16], g[17] - g[18]
    mx = w1 * d1 + w2 * ((d7 + d9) + (d11 + d13))
    my = w1 * d3 + w2 * ((d7 - d9) + (d15 + d17))
    mz = w1 * d5 + w2 * ((d11 - d13) + (d15 - d17))
    return density, (mx, my, mz)


PAIRS = [(1, 2), (3, 4), (5, 6), (7, 8), (9, 10), (11, 12), (13, 14), (15, 16), (17, 18)]


def collide_chunk(g, mask):
    density, (mx, my, mz) = moments_chunk(g)
    scale = jnp.where(mask == 1, jnp.float32(pore_damping), jnp.float32(1.0))
    k = (1.0 / density) * scale
    ux = mx * k
    uy = my * k
    uz = mz * k
    base = 1.0 - 1.5 * (ux * ux + uy * uy + uz * uz)
    dens = relax_rate * density
    keep = 1.0 - relax_rate
    solid = mask == 2
    proj = {
        1: ux,
        3: uy,
        5: uz,
        7: ux + uy,
        9: ux - uy,
        11: ux + uz,
        13: ux - uz,
        15: uy + uz,
        17: uy - uz,
    }
    out = [None] * NPOP
    out[0] = jnp.where(solid, g[0], dens * base + keep * g[0])
    for i, j in PAIRS:
        p = proj[i]
        q = base + 4.5 * (p * p)
        t = 3.0 * p
        relaxed_i = dens * (q + t) + keep * g[i]
        relaxed_j = dens * (q - t) + keep * g[j]
        out[i] = jnp.where(solid, g[j], relaxed_i)
        out[j] = jnp.where(solid, g[i], relaxed_j)
    return out


def lb_kernel(halo, nx, ny, *refs):
    g0, mask_ref, xlo, xhi, ylo, yhi, c_mm, c_mp, c_pm, c_pp = refs[:10]
    out_ref, coarse_ref, abuf, bbuf, flow_s = refs[10:]
    h = halo
    top = YOFF
    abuf[0:NPOP, h : h + nx, top : top + ny, :] = g0[...]
    abuf[NPOP, h : h + nx, top : top + ny, :] = mask_ref[...].astype(jnp.float32)
    planes = NPOP + 1
    abuf[:, 0:h, top : top + ny, :] = xlo[0:planes]
    abuf[:, h + nx : 2 * h + nx, top : top + ny, :] = xhi[0:planes]
    abuf[:, h : h + nx, top - h : top, :] = ylo[0:planes]
    abuf[:, h : h + nx, top + ny : top + ny + h, :] = yhi[0:planes]
    abuf[:, 0:h, top - h : top, :] = c_mm[0:planes]
    abuf[:, h + nx : 2 * h + nx, top - h : top, :] = c_mp[0:planes]
    abuf[:, 0:h, top + ny : top + ny + h, :] = c_pm[0:planes]
    abuf[:, h + nx : 2 * h + nx, top + ny : top + ny + h, :] = c_pp[0:planes]

    bufs = [bbuf, abuf]
    offs = [top] + [h - s for s in range(1, h + 1)]

    def run_step(s):
        src = abuf if s == 0 else bufs[(s - 1) % 2]
        dst = bufs[s % 2]
        if s == 0:
            rows = list(range(0, top + ny + h, ROWS))
        else:
            rows = list(range(0, ny + 2 * (h - s), ROWS))
        shift = offs[s - 1] - offs[s] if s > 0 else 0

        def body(x, carry):
            for r in rows:
                g = []
                for i in range(NPOP):
                    if s == 0:
                        v = src[i, x, pl.ds(r, ROWS), :]
                    else:
                        v = src[i, x - CX[i], pl.ds(r + shift - CY[i], ROWS), :]
                        if CZ[i] != 0:
                            v = pltpu.roll(v, CZ[i] % v.shape[1], 1)
                    g.append(v)
                mask = abuf[NPOP, x, pl.ds(r - offs[s] + top, ROWS), :]
                post = collide_chunk(g, mask)
                for i in range(NPOP):
                    dst[i, x, pl.ds(r, ROWS), :] = post[i]
            return carry

        lax.fori_loop(s, nx + 2 * h - s, body, 0, unroll=8)

    for s in range(h):
        run_step(s)

    src = bufs[(h - 1) % 2]
    shift = offs[h - 1] - 0

    def last_body(x, carry):
        for r in range(0, ny, ROWS):
            g = []
            for i in range(NPOP):
                v = src[i, x + h - CX[i], pl.ds(r + shift - CY[i], ROWS), :]
                if CZ[i] != 0:
                    v = pltpu.roll(v, CZ[i] % v.shape[1], 1)
                g.append(v)
                out_ref[i, x, pl.ds(r, ROWS), :] = v
            mask = abuf[NPOP, x + h, pl.ds(r + top, ROWS), :]
            density, mom = moments_chunk(g)
            inv = 1.0 / density
            solid = mask == 2
            for d in range(3):
                flow_s[d, x, pl.ds(r, ROWS), :] = jnp.where(solid, jnp.float32(0.0), mom[d] * inv)
        return carry

    lax.fori_loop(0, nx, last_body, 0, unroll=8)

    nz = flow_s.shape[3]
    pz = (
        lax.broadcasted_iota(jnp.int32, (nz // 2, nz), 1) // 2 == lax.broadcasted_iota(jnp.int32, (nz // 2, nz), 0)
    ).astype(jnp.float32)
    py = (
        lax.broadcasted_iota(jnp.int32, (ny, ny // 2), 0) // 2 == lax.broadcasted_iota(jnp.int32, (ny, ny // 2), 1)
    ).astype(jnp.float32)
    for d in range(3):
        for xp in range(nx // 2):
            plane = flow_s[d, 2 * xp] + flow_s[d, 2 * xp + 1]
            zy = lax.dot_general(
                pz,
                plane,
                (((1,), (1,)), ((), ())),
                precision=lax.Precision.HIGHEST,
                preferred_element_type=jnp.float32,
            )
            zc = jnp.dot(zy, py, precision=lax.Precision.HIGHEST, preferred_element_type=jnp.float32)
            coarse_ref[d, xp] = zc * jnp.float32(0.125)


def lb_call(g0, mask, halos, halo):
    _, nx, ny, nz = g0.shape
    f32 = jnp.float32
    vmem = pl.BlockSpec(memory_space=pltpu.VMEM)
    rows = YOFF + ny + 2 * halo
    rows = -(-rows // ROWS) * ROWS
    out_shape = (
        jax.ShapeDtypeStruct(g0.shape, f32),
        jax.ShapeDtypeStruct((3, nx // 2, nz // 2, ny // 2), f32),
    )
    scratch = [
        pltpu.VMEM((NPOP + 1, nx + 2 * halo, rows, nz), f32),
        pltpu.VMEM((NPOP, nx + 2 * halo, rows, nz), f32),
        pltpu.VMEM((3, nx, ny, nz), f32),
    ]
    cells = (nx + halo) * (ny + 2 * halo) * nz * halo
    cost = pl.CostEstimate(flops=320 * cells, transcendentals=0, bytes_accessed=2 * NPOP * 4 * nx * ny * nz * 2)
    return pl.pallas_call(
        functools.partial(lb_kernel, halo, nx, ny),
        out_shape=out_shape,
        in_specs=[vmem] * (2 + len(halos)),
        out_specs=(vmem, vmem),
        scratch_shapes=scratch,
        cost_estimate=cost,
        compiler_params=pltpu.CompilerParams(vmem_limit_bytes=60 * 1024 * 1024),
    )(g0, mask, *halos)


def send(x, dv, db):
    nv = lax.axis_size("vessel")
    nb = lax.axis_size("blk")
    if db == 0:
        return lax.ppermute(x, "vessel", [(i, (i + dv) % nv) for i in range(nv)])
    if dv == 0:
        return lax.ppermute(x, "blk", [(i, (i + db) % nb) for i in range(nb)])
    pairs = []
    for v in range(nv):
        for b in range(nb):
            pairs.append((v * nb + b, ((v + dv) % nv) * nb + (b + db) % nb))
    return lax.ppermute(x, ("vessel", "blk"), pairs)


def lattice_halos(g0, mask, conc, h, w):
    _, nx, ny, nz = g0.shape
    nzc, nxc, nyc = conc.shape
    maskf = mask.astype(jnp.float32)[None]
    lat = {1: slice(nx - h, nx), -1: slice(0, h), 0: slice(0, nx)}
    lat_y = {1: slice(ny - h, ny), -1: slice(0, h), 0: slice(0, ny)}
    trc_x = {1: slice(nxc - w, nxc), -1: slice(0, w), 0: slice(0, nxc)}
    trc_z = {1: slice(nzc - w, nzc), -1: slice(0, w), 0: slice(0, nzc)}
    order = ((1, 0), (-1, 0), (0, 1), (0, -1), (1, 1), (-1, 1), (1, -1), (-1, -1))
    pieces, tracer_pieces = [], []
    for dv, db in order:
        xs, ys = lat[dv], lat_y[db]
        lb = jnp.concatenate([g0[:, xs, ys], maskf[:, xs, ys]], axis=0)
        tp = conc[trc_z[db], trc_x[dv]]
        plane = lb.shape[1] * lb.shape[2] * nz
        flat = jnp.pad(tp.reshape(-1), (0, plane - tp.size))
        msg = jnp.concatenate([lb, flat.reshape(1, lb.shape[1], lb.shape[2], nz)], axis=0)
        got = send(msg, dv, db)
        pieces.append(got)
        tracer_pieces.append(got[NPOP + 1].reshape(-1)[: tp.size].reshape(tp.shape))
    return pieces, tracer_pieces


def tracer_update(c, fx, fy, fz):
    flux_x = fx * c
    flux_y = fy[1:-1, 1:-1] * c[1:-1, 1:-1]
    flux_z = fz * c
    center = c[1:-1, 1:-1]
    div_x = (flux_x[1:-1, 2:] - flux_x[1:-1, :-2]) * 0.5
    div_y = (jnp.roll(flux_y, -1, 2) - jnp.roll(flux_y, 1, 2)) * 0.5
    div_z = (flux_z[2:, 1:-1] - flux_z[:-2, 1:-1]) * 0.5
    divergence = div_x + div_y + div_z
    beside_all = (
        (c[1:-1, 2:] + c[1:-1, :-2])
        + (jnp.roll(center, -1, 2) + jnp.roll(center, 1, 2))
        + (c[2:, 1:-1] + c[:-2, 1:-1])
    )
    laplace = beside_all - 6.0 * center
    return center - advect_gain * divergence + diffusion * laplace


def local(populations, voxel_mask, tracer):
    w = TRACER_STEPS
    halos, tp = lattice_halos(populations, voxel_mask, tracer, STEPS, w)
    state, coarse = lb_call(populations, voxel_mask, halos, STEPS)
    nzt = coarse.shape[2]
    nb = lax.axis_size("blk")
    zb = nzt // nb
    ring = jnp.concatenate([coarse[:, :, nzt - w :], coarse, coarse[:, :, :zb]], axis=2)
    head = ring[:, :, : nb * zb].reshape(3, coarse.shape[1], nb, zb, coarse.shape[3])
    tail = ring[:, :, zb : zb + nb * zb].reshape(3, coarse.shape[1], nb, zb, coarse.shape[3])
    windows = jnp.concatenate([head, tail], axis=3)[:, :, :, : zb + 2 * w]
    moved = lax.all_to_all(windows, "blk", split_axis=2, concat_axis=4, tiled=True)
    flow = moved[:, :, 0]
    nxb = flow.shape[1]
    flow = jnp.concatenate([send(flow[:, nxb - w :], 1, 0), flow, send(flow[:, :w], -1, 0)], axis=1)
    flow = jnp.transpose(flow, (0, 2, 1, 3))
    xlo, xhi, zlo, zhi, c_mm, c_mp, c_pm, c_pp = tp
    conc = jnp.concatenate(
        [
            jnp.concatenate([c_mm, zlo, c_mp], axis=1),
            jnp.concatenate([xlo, tracer, xhi], axis=1),
            jnp.concatenate([c_pm, zhi, c_pp], axis=1),
        ],
        axis=0,
    )
    fx, fy, fz = flow[0], flow[1], flow[2]
    for step in range(TRACER_STEPS):
        conc = tracer_update(conc, fx, fy, fz)
        fx, fy, fz = fx[1:-1, 1:-1], fy[1:-1, 1:-1], fz[1:-1, 1:-1]
    return (state, conc)


def solution(mesh):
    placed = (P(None, "vessel", "blk", None), P("vessel", "blk", None), P("blk", "vessel", None))
    return jax.shard_map(
        local,
        mesh=mesh,
        in_specs=placed,
        out_specs=(P(None, "vessel", "blk", None), P("blk", "vessel", None)),
        check_vma=False,
    )
```
